32 devices in a mesh: inl: 4 (over y, core), xl: 2 (over x), gz: 4 (over z).
Axes of the slice: x: 2, y: 2, z: 4, core: 2. Of those that a mesh axis runs over, the one named last changes fastest.
Arguments:
- wave_p: float32 [32, 32, 256], P('gz', 'inl', 'xl'), may hold values from -6 to 6
- wave_p_old: float32 [32, 32, 256], P('gz', 'inl', 'xl'), may hold values from -6 to 6
- wave_q: float32 [32, 32, 256], P('gz', 'inl', 'xl'), may hold values from -6 to 6
- wave_q_old: float32 [32, 32, 256], P('gz', 'inl', 'xl'), may hold values from -6 to 6
- courant_square: float32 [32, 32, 256], P('gz', 'inl', 'xl'), may hold values from 0.05 to 0.11
- thomsen_epsilon: float32 [32, 32, 256], P('gz', 'inl', 'xl'), may hold values from 0.1 to 0.35
- thomsen_delta: float32 [32, 32, 256], P('gz', 'inl', 'xl'), may hold values from 0.02 to 0.2
- tilt_angle: float32 [32, 32, 256], P('gz', 'inl', 'xl'), may hold values from -3.140625 to 3.140625
- azimuth: float32 [32, 32, 256], P('gz', 'inl', 'xl'), may hold values from -3.140625 to 3.140625
- shear_ratio: float32 [32, 32, 256], P('gz', 'inl', 'xl'), may hold values from 0.1 to 0.6
- damping: float32 [32, 32, 256], P('gz', 'inl', 'xl'), may hold values from 0 to 0.3
- trace_samples: float32 [8192, 256], P(('inl', 'xl', 'gz')), may hold values from -6 to 6
- resample_filter: float32 [2, 256], replicated, may hold values from -0.375 to 0.375
- line_gain: float32 [64], replicated, may hold values from 0.5 to 4
- receiver_inline: int32 [8192], P(('inl', 'xl', 'gz')), may hold values from 0 to 31, as said below
- receiver_crossline: int32 [8192], P(('inl', 'xl', 'gz')), may hold values from 0 to 255, as said below
- shot_line: int32 [8192], P(('inl', 'xl', 'gz')), may hold values from 0 to 63
Outputs:
- next_p: float32 [32, 32, 256], P('gz', 'inl', 'xl')
- next_q: float32 [32, 32, 256], P('gz', 'inl', 'xl')
- prior_p: float32 [32, 32, 256], P('gz', 'inl', 'xl')
- prior_q: float32 [32, 32, 256], P('gz', 'inl', 'xl')
The draws below stay inside these ranges and needn't reach their ends.
Inputs may be any that keep to these rules, and one draw needn't show every extreme that they name: In each aligned block of 256 traces (the traces of one device), at most 64 traces lie in one device column (equal receiver_inline // 8 and receiver_crossline // 128); in every block some column holds exactly 64. `receiver_crossline`: see receiver_inline.
All inputs are finite; a program needn't handle non-finite values.
Results may differ from the reference program's by a relative error of at most 0.000075.
Values sent between devices are 32-bit elements; how exact they have to be, the bound alone decides.
No kernel may reach another device: no remote copies, remote signals or barrier semaphores. Data moves between devices by JAX's collectives and lax.ppermute only.
A program may use at most 64 MiB of HBM per device.

```python
import math
import jax
import jax.numpy as jnp
import numpy as np
from jax import lax

CX = 8
CY = 128
REC_DEV = 256
SAMPLES = 256
STEPS = 2
LINES = 64
NZ = 32
NX = 32
NY = 256
COLUMNS = 8
CAP = 64
RECS = 8192


def receiver_cells(key):
    blocks = RECS // REC_DEV
    base = jax.random.fold_in(key, 11)
    keys = jax.random.split(base, 5)
    sizes = jax.random.randint(keys[0], (blocks, REC_DEV), (CAP + 1) // 2, CAP + 1)
    sizes = sizes.at[:, 0].set(CAP)
    ends = jnp.cumsum(sizes, axis=1)
    positions = jnp.arange(REC_DEV, dtype=jnp.int32)
    group = jax.vmap(lambda edge: jnp.searchsorted(edge, positions, side='right'))(ends).astype(jnp.int32)
    orders = jax.vmap(lambda sub: jax.random.permutation(sub, COLUMNS))(jax.random.split(keys[1], blocks)).astype(jnp.int32)
    column = jnp.take_along_axis(orders, group, axis=1)
    shuffles = jax.vmap(lambda sub: jax.random.permutation(sub, REC_DEV))(jax.random.split(keys[2], blocks)).astype(jnp.int32)
    column = jnp.take_along_axis(column, shuffles, axis=1)
    per_row = NY // CY
    inline_cell = column // per_row * CX + jax.random.randint(keys[3], (blocks, REC_DEV), 0, CX)
    cross_cell = column % per_row * CY + jax.random.randint(keys[4], (blocks, REC_DEV), 0, CY)
    return (inline_cell.reshape(-1).astype(jnp.int32), cross_cell.reshape(-1).astype(jnp.int32))


def draw_receiver_inline(key, part):
    return receiver_cells(key)[0]


def draw_receiver_crossline(key, part):
    return receiver_cells(key)[1]


def with_ends(result, stream_key, low, high):
    spot = [jax.random.randint(jax.random.fold_in(stream_key, axis), (), 0, length) for axis, length in enumerate(result.shape)]
    main_axis = result.shape.index(max(result.shape))
    beside = spot[:main_axis] + [(spot[main_axis] + 1) % result.shape[main_axis]] + spot[main_axis + 1:]
    return result.at[tuple(spot)].set(low).at[tuple(beside)].set(high)


def level_of(stream_key, dims, pieces, low, largest):
    factor_of = 1.0
    for dim, shards_of in pieces:
        steps = jax.random.uniform(jax.random.fold_in(jax.random.fold_in(stream_key, 6), dim), (shards_of,), jnp.float32, low / len(pieces), largest / len(pieces))
        factor_of = factor_of * jnp.repeat(jnp.exp(steps), dims[dim] // shards_of).reshape((-1,) + (1,) * (len(dims) - 1 - dim))
    return factor_of


def rank_bounds(count, lean):
    portions = [(1 << 20) // math.isqrt(standing ** lean) + 1 for standing in range(1, count + 1)]
    scale = 1 + sum(portions) // (1 << 30)
    return np.cumsum(np.array([max(1, weight // scale) for weight in portions]))


def ranked(key, shape, amount, skew):
    grid = rank_bounds(amount, skew)
    lot = jax.random.randint(jax.random.fold_in(key, 1), shape, 0, int(grid[amount - 1]))
    rank = jnp.searchsorted(jnp.asarray(grid, jnp.int32), lot, side="right")
    return jax.random.permutation(jax.random.fold_in(key, 2), amount)[rank].astype(jnp.int32)


def gaussian(key, extent, scale, bound, cuts=(), kind=jnp.bfloat16):
    entries = jax.random.normal(key, extent, jnp.float32) * scale
    if len(cuts) > 0:
        entries = level_of(key, extent, cuts, -0.22, 0.18) * entries
    return jnp.clip(entries, min=-bound, max=bound).astype(kind)


def setup_inputs(seed: int = 0) -> dict:
    key_list = jax.random.split(jax.random.key(seed), 18)
    wave_p = gaussian(key_list[0], (NZ, NX, NY), 1.0, 6.0, ((0, 4), (1, 4), (2, 2)), jnp.float32)
    wave_p_old = gaussian(key_list[1], (NZ, NX, NY), 1.0, 6.0, ((0, 4), (1, 4), (2, 2)), jnp.float32)
    wave_q = gaussian(key_list[2], (NZ, NX, NY), 1.0, 6.0, ((0, 4), (1, 4), (2, 2)), jnp.float32)
    wave_q_old = gaussian(key_list[3], (NZ, NX, NY), 1.0, 6.0, ((0, 4), (1, 4), (2, 2)), jnp.float32)
    courant_square = jnp.clip(0.05 + 0.06 * jax.random.uniform(key_list[4], (NZ, NX, NY), jnp.float32) ** level_of(key_list[4], (NZ, NX, NY), ((0, 4), (1, 4), (2, 2)), -0.2, 0.2), 0.05, 0.11)
    thomsen_epsilon = jnp.clip(0.1 + 0.25 * jax.random.uniform(key_list[5], (NZ, NX, NY), jnp.float32) ** level_of(key_list[5], (NZ, NX, NY), ((0, 4), (1, 4), (2, 2)), -0.2, 0.2), 0.1, 0.35)
    thomsen_delta = jnp.clip(0.02 + 0.18 * jax.random.uniform(key_list[6], (NZ, NX, NY), jnp.float32) ** level_of(key_list[6], (NZ, NX, NY), ((0, 4), (1, 4), (2, 2)), -0.2, 0.2), 0.02, 0.2)
    tilt_angle = jnp.clip(jax.random.uniform(key_list[7], (NZ, NX, NY), jnp.float32, -3.140625, 3.140625), -3.140625, 3.140625)
    azimuth = jnp.clip(jax.random.uniform(key_list[8], (NZ, NX, NY), jnp.float32, -3.140625, 3.140625), -3.140625, 3.140625)
    shear_ratio = jnp.clip(0.1 + 0.5 * jax.random.uniform(key_list[9], (NZ, NX, NY), jnp.float32) ** level_of(key_list[9], (NZ, NX, NY), ((0, 4), (1, 4), (2, 2)), -0.2, 0.2), 0.1, 0.6)
    damping = jnp.clip(0.3 * jax.random.uniform(key_list[10], (NZ, NX, NY), jnp.float32) ** level_of(key_list[10], (NZ, NX, NY), ((0, 4), (1, 4), (2, 2)), -0.2, 0.2), 0.0, 0.3)
    trace_samples = gaussian(key_list[11], (RECS, SAMPLES), 1.0, 6.0, ((0, 32),), jnp.float32)
    resample_filter = gaussian(key_list[12], (STEPS, SAMPLES), SAMPLES ** -0.5, 0.375, (), jnp.float32)
    line_gain = jnp.clip(jnp.exp(jax.random.uniform(key_list[13], (LINES,), jnp.float32, math.log(0.5), math.log(4.0))), 0.5, 4.0)
    receiver_inline = draw_receiver_inline(jax.random.fold_in(key_list[17], 71), 0)
    receiver_crossline = draw_receiver_crossline(jax.random.fold_in(key_list[17], 71), 0)
    shot_line = with_ends(ranked(key_list[16], (RECS,), LINES, 2), jax.random.fold_in(key_list[16], 3), 0, LINES - 1).astype(jnp.int32)
    return {"wave_p": wave_p, "wave_p_old": wave_p_old, "wave_q": wave_q, "wave_q_old": wave_q_old, "courant_square": courant_square, "thomsen_epsilon": thomsen_epsilon, "thomsen_delta": thomsen_delta, "tilt_angle": tilt_angle, "azimuth": azimuth, "shear_ratio": shear_ratio, "damping": damping, "trace_samples": trace_samples, "resample_filter": resample_filter, "line_gain": line_gain, "receiver_inline": receiver_inline, "receiver_crossline": receiver_crossline, "shot_line": shot_line}


second_coef = (-205.0 / 72.0, 8.0 / 5.0, -1.0 / 5.0, 8.0 / 315.0, -1.0 / 560.0)
first_coef = (0.0, 4.0 / 5.0, -1.0 / 5.0, 4.0 / 105.0, -1.0 / 280.0)


def derivatives(padded):
    depth = padded.shape[-3] - 8
    across = padded.shape[-2] - 8
    along = padded.shape[-1] - 8

    def piece(dz, dx, dy):
        return padded[..., 4 + dz:4 + dz + depth, 4 + dx:4 + dx + across, 4 + dy:4 + dy + along]

    center = piece(0, 0, 0)
    u_zz = second_coef[0] * center
    u_xx = second_coef[0] * center
    u_yy = second_coef[0] * center
    for k in range(1, 5):
        u_zz = u_zz + second_coef[k] * (piece(k, 0, 0) + piece(-k, 0, 0))
        u_xx = u_xx + second_coef[k] * (piece(0, k, 0) + piece(0, -k, 0))
        u_yy = u_yy + second_coef[k] * (piece(0, 0, k) + piece(0, 0, -k))
    grad_x = first_coef[1] * (padded[..., :, 5:5 + across, :] - padded[..., :, 3:3 + across, :])
    grad_y = first_coef[1] * (padded[..., :, 4:4 + across, 5:5 + along] - padded[..., :, 4:4 + across, 3:3 + along])
    for k in range(2, 5):
        grad_x = grad_x + first_coef[k] * (padded[..., :, 4 + k:4 + k + across, :] - padded[..., :, 4 - k:4 - k + across, :])
        grad_y = grad_y + first_coef[k] * (padded[..., :, 4:4 + across, 4 + k:4 + k + along] - padded[..., :, 4:4 + across, 4 - k:4 - k + along])
    u_xy = first_coef[1] * (grad_x[..., 4:4 + depth, :, 5:5 + along] - grad_x[..., 4:4 + depth, :, 3:3 + along])
    u_xz = first_coef[1] * (grad_x[..., 5:5 + depth, :, 4:4 + along] - grad_x[..., 3:3 + depth, :, 4:4 + along])
    u_yz = first_coef[1] * (grad_y[..., 5:5 + depth, :, :] - grad_y[..., 3:3 + depth, :, :])
    for k in range(2, 5):
        u_xy = u_xy + first_coef[k] * (grad_x[..., 4:4 + depth, :, 4 + k:4 + k + along] - grad_x[..., 4:4 + depth, :, 4 - k:4 - k + along])
        u_xz = u_xz + first_coef[k] * (grad_x[..., 4 + k:4 + k + depth, :, 4:4 + along] - grad_x[..., 4 - k:4 - k + depth, :, 4:4 + along])
        u_yz = u_yz + first_coef[k] * (grad_y[..., 4 + k:4 + k + depth, :, :] - grad_y[..., 4 - k:4 - k + depth, :, :])
    return u_zz, u_xx, u_yy, u_xy, u_xz, u_yz


def anisotropy(tilt_angle, azimuth):
    sin_t = jnp.sin(tilt_angle)
    cos_t = jnp.cos(tilt_angle)
    sin_f = jnp.sin(azimuth)
    cos_f = jnp.cos(azimuth)
    a_xx = sin_t * sin_t * cos_f * cos_f
    a_yy = sin_t * sin_t * sin_f * sin_f
    a_zz = cos_t * cos_t
    a_xy = 2.0 * sin_t * sin_t * sin_f * cos_f
    a_xz = 2.0 * sin_t * cos_t * cos_f
    a_yz = 2.0 * sin_t * cos_t * sin_f
    return a_xx, a_yy, a_zz, a_xy, a_xz, a_yz


def advance(padded, current, previous, fields, coefs, plane):
    courant, eps_field, delta_field, shear, damp = fields
    a_xx, a_yy, a_zz, a_xy, a_xz, a_yz = coefs
    u_zz, u_xx, u_yy, u_xy, u_xz, u_yz = derivatives(padded)
    h_one = a_xx * u_xx + a_yy * u_yy + a_zz * u_zz + a_xy * u_xy + a_xz * u_xz + a_yz * u_yz
    h_two = u_xx + u_yy + u_zz - h_one
    wave_a = current[0]
    wave_b = current[1]
    old_a = previous[0]
    old_b = previous[1]
    new_a = 2.0 * wave_a - old_a + courant * ((1.0 + 2.0 * eps_field) * h_two[0] + h_one[1] + shear * (h_one[0] - h_one[1])) - damp * (wave_a - old_a)
    new_b = 2.0 * wave_b - old_b + courant * ((1.0 + 2.0 * delta_field) * h_two[0] + h_one[1] + shear * (h_two[1] - h_two[0])) - damp * (wave_b - old_b)
    new_a = new_a.at[0].add(plane)
    new_b = new_b.at[0].add(plane)
    return jnp.stack([new_a, new_b])


def reference(wave_p, wave_p_old, wave_q, wave_q_old, courant_square, thomsen_epsilon, thomsen_delta, tilt_angle, azimuth, shear_ratio, damping, trace_samples, resample_filter, line_gain, receiver_inline, receiver_crossline, shot_line):
    gains = line_gain[shot_line.astype(jnp.int32)]
    amplitude = jnp.dot(trace_samples, resample_filter.T, precision=lax.Precision.HIGHEST) * gains[:, None]
    target = (receiver_inline * NY + receiver_crossline).astype(jnp.int32)
    planes = jnp.zeros((STEPS, NX * NY), jnp.float32).at[:, target].add(amplitude.T)
    planes = planes.reshape(STEPS, NX, NY)
    coefs = anisotropy(tilt_angle, azimuth)
    fields = (courant_square, thomsen_epsilon, thomsen_delta, shear_ratio, damping)
    current = jnp.stack([wave_p, wave_q])
    previous = jnp.stack([wave_p_old, wave_q_old])
    for step in range(STEPS):
        padded = jnp.pad(current, ((0, 0), (4, 4), (4, 4), (4, 4)))
        newer = advance(padded, current, previous, fields, coefs, planes[step])
        previous = current
        current = newer
    return current[0], current[1], previous[0], previous[1]
```

```python
import jax
import jax.numpy as jnp
from jax import lax
from jax.sharding import PartitionSpec as P

second_coef = (-205.0 / 72.0, 8.0 / 5.0, -1.0 / 5.0, 8.0 / 315.0, -1.0 / 560.0)
first_coef = (0.0, 4.0 / 5.0, -1.0 / 5.0, 4.0 / 105.0, -1.0 / 280.0)


def with_halo(block, sides, width):
    for axis, dim in sides:
        count = lax.axis_size(axis)
        forward = [(i, i + 1) for i in range(count - 1)]
        backward = [(target, source) for source, target in forward]
        low = lax.ppermute(
            lax.slice_in_dim(block, block.shape[dim] - width, None, axis=dim), axis, forward
        )
        high = lax.ppermute(lax.slice_in_dim(block, 0, width, axis=dim), axis, backward)
        block = jnp.concatenate([low, block, high], axis=dim)
    return block


def derivatives(padded):
    depth = padded.shape[-3] - 8
    across = padded.shape[-2] - 8
    along = padded.shape[-1] - 8

    def piece(dz, dx, dy):
        return padded[
            ..., 4 + dz : 4 + dz + depth, 4 + dx : 4 + dx + across, 4 + dy : 4 + dy + along
        ]

    center = piece(0, 0, 0)
    u_zz = second_coef[0] * center
    u_xx = second_coef[0] * center
    u_yy = second_coef[0] * center
    for k in range(1, 5):
        u_zz = u_zz + second_coef[k] * (piece(k, 0, 0) + piece(-k, 0, 0))
        u_xx = u_xx + second_coef[k] * (piece(0, k, 0) + piece(0, -k, 0))
        u_yy = u_yy + second_coef[k] * (piece(0, 0, k) + piece(0, 0, -k))
    grad_x = first_coef[1] * (padded[..., :, 5 : 5 + across, :] - padded[..., :, 3 : 3 + across, :])
    grad_y = first_coef[1] * (
        padded[..., :, 4 : 4 + across, 5 : 5 + along]
        - padded[..., :, 4 : 4 + across, 3 : 3 + along]
    )
    for k in range(2, 5):
        grad_x = grad_x + first_coef[k] * (
            padded[..., :, 4 + k : 4 + k + across, :] - padded[..., :, 4 - k : 4 - k + across, :]
        )
        grad_y = grad_y + first_coef[k] * (
            padded[..., :, 4 : 4 + across, 4 + k : 4 + k + along]
            - padded[..., :, 4 : 4 + across, 4 - k : 4 - k + along]
        )
    u_xy = first_coef[1] * (
        grad_x[..., 4 : 4 + depth, :, 5 : 5 + along] - grad_x[..., 4 : 4 + depth, :, 3 : 3 + along]
    )
    u_xz = first_coef[1] * (
        grad_x[..., 5 : 5 + depth, :, 4 : 4 + along] - grad_x[..., 3 : 3 + depth, :, 4 : 4 + along]
    )
    u_yz = first_coef[1] * (grad_y[..., 5 : 5 + depth, :, :] - grad_y[..., 3 : 3 + depth, :, :])
    for k in range(2, 5):
        u_xy = u_xy + first_coef[k] * (
            grad_x[..., 4 : 4 + depth, :, 4 + k : 4 + k + along]
            - grad_x[..., 4 : 4 + depth, :, 4 - k : 4 - k + along]
        )
        u_xz = u_xz + first_coef[k] * (
            grad_x[..., 4 + k : 4 + k + depth, :, 4 : 4 + along]
            - grad_x[..., 4 - k : 4 - k + depth, :, 4 : 4 + along]
        )
        u_yz = u_yz + first_coef[k] * (
            grad_y[..., 4 + k : 4 + k + depth, :, :] - grad_y[..., 4 - k : 4 - k + depth, :, :]
        )
    return (u_zz, u_xx, u_yy, u_xy, u_xz, u_yz)


def anisotropy(tilt_angle, azimuth):
    sin_t = jnp.sin(tilt_angle)
    cos_t = jnp.cos(tilt_angle)
    sin_f = jnp.sin(azimuth)
    cos_f = jnp.cos(azimuth)
    a_xx = sin_t * sin_t * cos_f * cos_f
    a_yy = sin_t * sin_t * sin_f * sin_f
    a_zz = cos_t * cos_t
    a_xy = 2.0 * sin_t * sin_t * sin_f * cos_f
    a_xz = 2.0 * sin_t * cos_t * cos_f
    a_yz = 2.0 * sin_t * cos_t * sin_f
    return (a_xx, a_yy, a_zz, a_xy, a_xz, a_yz)


def advance(padded, current, previous, fields, coefs, plane, top):
    courant, eps_field, delta_field, shear, damp = fields
    a_xx, a_yy, a_zz, a_xy, a_xz, a_yz = coefs
    u_zz, u_xx, u_yy, u_xy, u_xz, u_yz = derivatives(padded)
    h_one = a_xx * u_xx + a_yy * u_yy + a_zz * u_zz + a_xy * u_xy + a_xz * u_xz + a_yz * u_yz
    h_two = u_xx + u_yy + u_zz - h_one
    wave_a = current[0]
    wave_b = current[1]
    old_a = previous[0]
    old_b = previous[1]
    new_a = (
        2.0 * wave_a
        - old_a
        + courant * ((1.0 + 2.0 * eps_field) * h_two[0] + h_one[1] + shear * (h_one[0] - h_one[1]))
        - damp * (wave_a - old_a)
    )
    new_b = (
        2.0 * wave_b
        - old_b
        + courant
        * ((1.0 + 2.0 * delta_field) * h_two[0] + h_one[1] + shear * (h_two[1] - h_two[0]))
        - damp * (wave_b - old_b)
    )
    new_a = new_a.at[top].add(plane)
    new_b = new_b.at[top].add(plane)
    return jnp.stack([new_a, new_b])


def step_amplitudes(samples, resample_filter, line_gain, lines):
    table = jnp.arange(line_gain.shape[0], dtype=jnp.int32)
    gains = jnp.sum(jnp.where(lines[:, None] == table[None, :], line_gain[None, :], 0.0), axis=1)
    return jnp.dot(samples, resample_filter.T, precision=lax.Precision.HIGHEST) * gains[:, None]


def local(
    wave_p,
    wave_p_old,
    wave_q,
    wave_q_old,
    courant_square,
    thomsen_epsilon,
    thomsen_delta,
    tilt_angle,
    azimuth,
    shear_ratio,
    damping,
    trace_samples,
    resample_filter,
    line_gain,
    receiver_inline,
    receiver_crossline,
    shot_line,
):
    depth, inline_cells, cross_cells = wave_p.shape
    cells = inline_cells * cross_cells
    steps = resample_filter.shape[0]
    xl_count = lax.axis_size("xl")
    gz_count = lax.axis_size("gz")
    columns = lax.axis_size("inl") * xl_count
    capacity = 2 * trace_samples.shape[0] // columns
    owner = receiver_inline // inline_cells * xl_count + receiver_crossline // cross_cells
    local_cell = receiver_inline % inline_cells * cross_cells + receiver_crossline % cross_cells
    payload = step_amplitudes(trace_samples, resample_filter, line_gain, shot_line)
    onehot = (owner[:, None] == jnp.arange(columns, dtype=jnp.int32)[None, :]).astype(jnp.int32)
    rank = jnp.sum(jnp.cumsum(onehot, axis=0) * onehot, axis=1) - 1
    slot = owner * (gz_count * capacity) + rank
    packed = jnp.concatenate([payload, local_cell.astype(jnp.float32)[:, None]], axis=1)
    width = packed.shape[1]
    send = jnp.zeros((columns * gz_count * capacity, width), jnp.float32).at[slot].set(packed)
    arrived = lax.all_to_all(send, ("inl", "xl", "gz"), split_axis=0, concat_axis=0, tiled=True)
    target = arrived[:, steps].astype(jnp.int32)
    planes = jnp.zeros((steps, cells), jnp.float32).at[:, target].add(arrived[:, :steps].T, mode="drop")
    planes = planes.reshape(steps, inline_cells, cross_cells)
    fields = (courant_square, thomsen_epsilon, thomsen_delta, shear_ratio, damping)
    current = jnp.stack([wave_p, wave_q])
    previous = jnp.stack([wave_p_old, wave_q_old])
    coefs = anisotropy(tilt_angle, azimuth)
    for step in range(steps):
        padded = with_halo(current, (("inl", 2), ("xl", 3), ("gz", 1)), 4)
        newer = advance(padded, current, previous, fields, coefs, planes[step], 0)
        previous = current
        current = newer
    return (current[0], current[1], previous[0], previous[1])


def solution(mesh):
    return jax.shard_map(
        local,
        mesh=mesh,
        in_specs=(
            P("gz", "inl", "xl"),
            P("gz", "inl", "xl"),
            P("gz", "inl", "xl"),
            P("gz", "inl", "xl"),
            P("gz", "inl", "xl"),
            P("gz", "inl", "xl"),
            P("gz", "inl", "xl"),
            P("gz", "inl", "xl"),
            P("gz", "inl", "xl"),
            P("gz", "inl", "xl"),
            P("gz", "inl", "xl"),
            P(("inl", "xl", "gz"), None),
            P(),
            P(),
            P(("inl", "xl", "gz")),
            P(("inl", "xl", "gz")),
            P(("inl", "xl", "gz")),
        ),
        out_specs=(
            P("gz", "inl", "xl"),
            P("gz", "inl", "xl"),
            P("gz", "inl", "xl"),
            P("gz", "inl", "xl"),
        ),
        check_vma=False,
    )
```

```python
import jax
import jax.numpy as jnp
from jax import lax
from jax.sharding import PartitionSpec as P

second_coef = (-205.0 / 72.0, 8.0 / 5.0, -1.0 / 5.0, 8.0 / 315.0, -1.0 / 560.0)
first_coef = (0.0, 4.0 / 5.0, -1.0 / 5.0, 4.0 / 105.0, -1.0 / 280.0)


def with_halo(block, sides, width):
    for axis, dim in sides:
        count = lax.axis_size(axis)
        forward = [(i, i + 1) for i in range(count - 1)]
        backward = [(target, source) for source, target in forward]
        low = lax.ppermute(
            lax.slice_in_dim(block, block.shape[dim] - width, None, axis=dim), axis, forward
        )
        high = lax.ppermute(lax.slice_in_dim(block, 0, width, axis=dim), axis, backward)
        block = jnp.concatenate([low, block, high], axis=dim)
    return block


def derivatives(padded):
    depth = padded.shape[-3] - 8
    across = padded.shape[-2] - 8
    along = padded.shape[-1] - 8

    def piece(dz, dx, dy):
        return padded[
            ..., 4 + dz : 4 + dz + depth, 4 + dx : 4 + dx + across, 4 + dy : 4 + dy + along
        ]

    center = piece(0, 0, 0)
    u_zz = second_coef[0] * center
    u_xx = second_coef[0] * center
    u_yy = second_coef[0] * center
    for k in range(1, 5):
        u_zz = u_zz + second_coef[k] * (piece(k, 0, 0) + piece(-k, 0, 0))
        u_xx = u_xx + second_coef[k] * (piece(0, k, 0) + piece(0, -k, 0))
        u_yy = u_yy + second_coef[k] * (piece(0, 0, k) + piece(0, 0, -k))
    grad_x = first_coef[1] * (padded[..., :, 5 : 5 + across, :] - padded[..., :, 3 : 3 + across, :])
    grad_y = first_coef[1] * (
        padded[..., :, 4 : 4 + across, 5 : 5 + along]
        - padded[..., :, 4 : 4 + across, 3 : 3 + along]
    )
    for k in range(2, 5):
        grad_x = grad_x + first_coef[k] * (
            padded[..., :, 4 + k : 4 + k + across, :] - padded[..., :, 4 - k : 4 - k + across, :]
        )
        grad_y = grad_y + first_coef[k] * (
            padded[..., :, 4 : 4 + across, 4 + k : 4 + k + along]
            - padded[..., :, 4 : 4 + across, 4 - k : 4 - k + along]
        )
    u_xy = first_coef[1] * (
        grad_x[..., 4 : 4 + depth, :, 5 : 5 + along] - grad_x[..., 4 : 4 + depth, :, 3 : 3 + along]
    )
    u_xz = first_coef[1] * (
        grad_x[..., 5 : 5 + depth, :, 4 : 4 + along] - grad_x[..., 3 : 3 + depth, :, 4 : 4 + along]
    )
    u_yz = first_coef[1] * (grad_y[..., 5 : 5 + depth, :, :] - grad_y[..., 3 : 3 + depth, :, :])
    for k in range(2, 5):
        u_xy = u_xy + first_coef[k] * (
            grad_x[..., 4 : 4 + depth, :, 4 + k : 4 + k + along]
            - grad_x[..., 4 : 4 + depth, :, 4 - k : 4 - k + along]
        )
        u_xz = u_xz + first_coef[k] * (
            grad_x[..., 4 + k : 4 + k + depth, :, 4 : 4 + along]
            - grad_x[..., 4 - k : 4 - k + depth, :, 4 : 4 + along]
        )
        u_yz = u_yz + first_coef[k] * (
            grad_y[..., 4 + k : 4 + k + depth, :, :] - grad_y[..., 4 - k : 4 - k + depth, :, :]
        )
    return (u_zz, u_xx, u_yy, u_xy, u_xz, u_yz)


def anisotropy(tilt_angle, azimuth):
    sin_t = jnp.sin(tilt_angle)
    cos_t = jnp.cos(tilt_angle)
    sin_f = jnp.sin(azimuth)
    cos_f = jnp.cos(azimuth)
    a_xx = sin_t * sin_t * cos_f * cos_f
    a_yy = sin_t * sin_t * sin_f * sin_f
    a_zz = cos_t * cos_t
    a_xy = 2.0 * sin_t * sin_t * sin_f * cos_f
    a_xz = 2.0 * sin_t * cos_t * cos_f
    a_yz = 2.0 * sin_t * cos_t * sin_f
    return (a_xx, a_yy, a_zz, a_xy, a_xz, a_yz)


def advance(padded, current, previous, fields, coefs, plane, top):
    courant, eps_field, delta_field, shear, damp = fields
    a_xx, a_yy, a_zz, a_xy, a_xz, a_yz = coefs
    u_zz, u_xx, u_yy, u_xy, u_xz, u_yz = derivatives(padded)
    h_one = a_xx * u_xx + a_yy * u_yy + a_zz * u_zz + a_xy * u_xy + a_xz * u_xz + a_yz * u_yz
    h_two = u_xx + u_yy + u_zz - h_one
    wave_a = current[0]
    wave_b = current[1]
    old_a = previous[0]
    old_b = previous[1]
    new_a = (
        2.0 * wave_a
        - old_a
        + courant * ((1.0 + 2.0 * eps_field) * h_two[0] + h_one[1] + shear * (h_one[0] - h_one[1]))
        - damp * (wave_a - old_a)
    )
    new_b = (
        2.0 * wave_b
        - old_b
        + courant
        * ((1.0 + 2.0 * delta_field) * h_two[0] + h_one[1] + shear * (h_two[1] - h_two[0]))
        - damp * (wave_b - old_b)
    )
    new_a = new_a.at[top].add(plane)
    new_b = new_b.at[top].add(plane)
    return jnp.stack([new_a, new_b])


def step_amplitudes(samples, resample_filter, line_gain, lines):
    table = jnp.arange(line_gain.shape[0], dtype=jnp.int32)
    gains = jnp.sum(jnp.where(lines[:, None] == table[None, :], line_gain[None, :], 0.0), axis=1)
    return jnp.dot(samples, resample_filter.T, precision=lax.Precision.HIGHEST) * gains[:, None]


def local(
    wave_p,
    wave_p_old,
    wave_q,
    wave_q_old,
    courant_square,
    thomsen_epsilon,
    thomsen_delta,
    tilt_angle,
    azimuth,
    shear_ratio,
    damping,
    trace_samples,
    resample_filter,
    line_gain,
    receiver_inline,
    receiver_crossline,
    shot_line,
):
    depth, inline_cells, cross_cells = wave_p.shape
    cells = inline_cells * cross_cells
    steps = resample_filter.shape[0]
    xl_count = lax.axis_size("xl")
    gz_count = lax.axis_size("gz")
    columns = lax.axis_size("inl") * xl_count
    capacity = 2 * trace_samples.shape[0] // columns
    owner = receiver_inline // inline_cells * xl_count + receiver_crossline // cross_cells
    local_cell = receiver_inline % inline_cells * cross_cells + receiver_crossline % cross_cells
    payload = step_amplitudes(trace_samples, resample_filter, line_gain, shot_line)
    onehot = (owner[:, None] == jnp.arange(columns, dtype=jnp.int32)[None, :]).astype(jnp.int32)
    rank = jnp.sum(jnp.cumsum(onehot, axis=0) * onehot, axis=1) - 1
    slot = owner * (gz_count * capacity) + rank
    packed = jnp.concatenate([payload, local_cell.astype(jnp.float32)[:, None]], axis=1)
    width = packed.shape[1]
    send = jnp.zeros((columns * gz_count * capacity, width), jnp.float32).at[slot].set(packed)
    arrived = lax.all_to_all(send, ("inl", "xl", "gz"), split_axis=0, concat_axis=0, tiled=True)
    target = arrived[:, steps].astype(jnp.int32)
    row_hit = (
        target[:, None] // cross_cells == jnp.arange(inline_cells, dtype=jnp.int32)[None, :]
    ).astype(jnp.float32)
    col_hit = (
        target[:, None] % cross_cells == jnp.arange(cross_cells, dtype=jnp.int32)[None, :]
    ).astype(jnp.float32)
    weighted = arrived[:, :steps, None] * row_hit[:, None, :]
    planes = jnp.einsum("nkx,ny->kxy", weighted, col_hit, precision=lax.Precision.HIGHEST)
    fields = (courant_square, thomsen_epsilon, thomsen_delta, shear_ratio, damping)
    current = jnp.stack([wave_p, wave_q])
    previous = jnp.stack([wave_p_old, wave_q_old])
    coefs = anisotropy(tilt_angle, azimuth)
    for step in range(steps):
        padded = with_halo(current, (("inl", 2), ("xl", 3), ("gz", 1)), 4)
        newer = advance(padded, current, previous, fields, coefs, planes[step], 0)
        previous = current
        current = newer
    return (current[0], current[1], previous[0], previous[1])


def solution(mesh):
    return jax.shard_map(
        local,
        mesh=mesh,
        in_specs=(
            P("gz", "inl", "xl"),
            P("gz", "inl", "xl"),
            P("gz", "inl", "xl"),
            P("gz", "inl", "xl"),
            P("gz", "inl", "xl"),
            P("gz", "inl", "xl"),
            P("gz", "inl", "xl"),
            P("gz", "inl", "xl"),
            P("gz", "inl", "xl"),
            P("gz", "inl", "xl"),
            P("gz", "inl", "xl"),
            P(("inl", "xl", "gz"), None),
            P(),
            P(),
            P(("inl", "xl", "gz")),
            P(("inl", "xl", "gz")),
            P(("inl", "xl", "gz")),
        ),
        out_specs=(
            P("gz", "inl", "xl"),
            P("gz", "inl", "xl"),
            P("gz", "inl", "xl"),
            P("gz", "inl", "xl"),
        ),
        check_vma=False,
    )
```

```python
import jax
import jax.numpy as jnp
from jax import lax
from jax.sharding import PartitionSpec as P

second_coef = (-205.0 / 72.0, 8.0 / 5.0, -1.0 / 5.0, 8.0 / 315.0, -1.0 / 560.0)
first_coef = (0.0, 4.0 / 5.0, -1.0 / 5.0, 4.0 / 105.0, -1.0 / 280.0)


def derivatives(padded):
    depth = padded.shape[-3] - 8
    across = padded.shape[-2] - 8
    along = padded.shape[-1] - 8

    def piece(dz, dx, dy):
        return padded[
            ..., 4 + dz : 4 + dz + depth, 4 + dx : 4 + dx + across, 4 + dy : 4 + dy + along
        ]

    center = piece(0, 0, 0)
    u_zz = second_coef[0] * center
    u_xx = second_coef[0] * center
    u_yy = second_coef[0] * center
    for k in range(1, 5):
        u_zz = u_zz + second_coef[k] * (piece(k, 0, 0) + piece(-k, 0, 0))
        u_xx = u_xx + second_coef[k] * (piece(0, k, 0) + piece(0, -k, 0))
        u_yy = u_yy + second_coef[k] * (piece(0, 0, k) + piece(0, 0, -k))
    grad_x = first_coef[1] * (padded[..., :, 5 : 5 + across, :] - padded[..., :, 3 : 3 + across, :])
    grad_y = first_coef[1] * (
        padded[..., :, 4 : 4 + across, 5 : 5 + along]
        - padded[..., :, 4 : 4 + across, 3 : 3 + along]
    )
    for k in range(2, 5):
        grad_x = grad_x + first_coef[k] * (
            padded[..., :, 4 + k : 4 + k + across, :] - padded[..., :, 4 - k : 4 - k + across, :]
        )
        grad_y = grad_y + first_coef[k] * (
            padded[..., :, 4 : 4 + across, 4 + k : 4 + k + along]
            - padded[..., :, 4 : 4 + across, 4 - k : 4 - k + along]
        )
    u_xy = first_coef[1] * (
        grad_x[..., 4 : 4 + depth, :, 5 : 5 + along] - grad_x[..., 4 : 4 + depth, :, 3 : 3 + along]
    )
    u_xz = first_coef[1] * (
        grad_x[..., 5 : 5 + depth, :, 4 : 4 + along] - grad_x[..., 3 : 3 + depth, :, 4 : 4 + along]
    )
    u_yz = first_coef[1] * (grad_y[..., 5 : 5 + depth, :, :] - grad_y[..., 3 : 3 + depth, :, :])
    for k in range(2, 5):
        u_xy = u_xy + first_coef[k] * (
            grad_x[..., 4 : 4 + depth, :, 4 + k : 4 + k + along]
            - grad_x[..., 4 : 4 + depth, :, 4 - k : 4 - k + along]
        )
        u_xz = u_xz + first_coef[k] * (
            grad_x[..., 4 + k : 4 + k + depth, :, 4 : 4 + along]
            - grad_x[..., 4 - k : 4 - k + depth, :, 4 : 4 + along]
        )
        u_yz = u_yz + first_coef[k] * (
            grad_y[..., 4 + k : 4 + k + depth, :, :] - grad_y[..., 4 - k : 4 - k + depth, :, :]
        )
    return (u_zz, u_xx, u_yy, u_xy, u_xz, u_yz)


def anisotropy(tilt_angle, azimuth):
    sin_t = jnp.sin(tilt_angle)
    cos_t = jnp.cos(tilt_angle)
    sin_f = jnp.sin(azimuth)
    cos_f = jnp.cos(azimuth)
    a_xx = sin_t * sin_t * cos_f * cos_f
    a_yy = sin_t * sin_t * sin_f * sin_f
    a_zz = cos_t * cos_t
    a_xy = 2.0 * sin_t * sin_t * sin_f * cos_f
    a_xz = 2.0 * sin_t * cos_t * cos_f
    a_yz = 2.0 * sin_t * cos_t * sin_f
    return (a_xx, a_yy, a_zz, a_xy, a_xz, a_yz)


def advance_raw(padded, current, previous, fields, coefs):
    courant, eps_field, delta_field, shear, damp = fields
    a_xx, a_yy, a_zz, a_xy, a_xz, a_yz = coefs
    u_zz, u_xx, u_yy, u_xy, u_xz, u_yz = derivatives(padded)
    h_one = a_xx * u_xx + a_yy * u_yy + a_zz * u_zz + a_xy * u_xy + a_xz * u_xz + a_yz * u_yz
    h_two = u_xx + u_yy + u_zz - h_one
    wave_a = current[0]
    wave_b = current[1]
    old_a = previous[0]
    old_b = previous[1]
    new_a = (
        2.0 * wave_a
        - old_a
        + courant * ((1.0 + 2.0 * eps_field) * h_two[0] + h_one[1] + shear * (h_one[0] - h_one[1]))
        - damp * (wave_a - old_a)
    )
    new_b = (
        2.0 * wave_b
        - old_b
        + courant
        * ((1.0 + 2.0 * delta_field) * h_two[0] + h_one[1] + shear * (h_two[1] - h_two[0]))
        - damp * (wave_b - old_b)
    )
    return jnp.stack([new_a, new_b])


def step_amplitudes(samples, resample_filter, line_gain, lines):
    table = jnp.arange(line_gain.shape[0], dtype=jnp.int32)
    gains = jnp.sum(jnp.where(lines[:, None] == table[None, :], line_gain[None, :], 0.0), axis=1)
    return jnp.dot(samples, resample_filter.T, precision=lax.Precision.HIGHEST) * gains[:, None]


def exchange(groups, axis, dim):
    count = lax.axis_size(axis)
    forward = [(i, i + 1) for i in range(count - 1)]
    backward = [(target, source) for source, target in forward]
    lows = [lax.slice_in_dim(a, a.shape[dim] - w, None, axis=dim) for a, w in groups]
    highs = [lax.slice_in_dim(a, 0, w, axis=dim) for a, w in groups]
    got_low = lax.ppermute(jnp.concatenate([x.reshape(-1) for x in lows]), axis, forward)
    got_high = lax.ppermute(jnp.concatenate([x.reshape(-1) for x in highs]), axis, backward)
    out = []
    offset = 0
    for (a, w), piece in zip(groups, lows):
        n = piece.size
        low = got_low[offset : offset + n].reshape(piece.shape)
        high = got_high[offset : offset + n].reshape(piece.shape)
        offset += n
        out.append((jnp.concatenate([low, a, high], axis=dim), w))
    return out


def plane_entries(receiver_inline, receiver_crossline, payload, inline_cells, cross_cells, halo):
    inl_count = lax.axis_size("inl")
    xl_count = lax.axis_size("xl")
    col_x = receiver_inline // inline_cells
    col_y = receiver_crossline // cross_cells
    off_x = receiver_inline % inline_cells
    off_y = receiver_crossline % cross_cells
    near_x = jnp.where(off_x < halo, col_x - 1, jnp.where(off_x >= inline_cells - halo, col_x + 1, -1))
    near_y = jnp.where(off_y < halo, col_y - 1, jnp.where(off_y >= cross_cells - halo, col_y + 1, -1))
    ok_x = (near_x >= 0) & (near_x < inl_count)
    ok_y = (near_y >= 0) & (near_y < xl_count)
    dest_x = jnp.concatenate([col_x, near_x, col_x, near_x])
    dest_y = jnp.concatenate([col_y, col_y, near_y, near_y])
    valid = jnp.concatenate([jnp.ones_like(ok_x), ok_x, ok_y, ok_x & ok_y])
    gx = jnp.concatenate([receiver_inline] * 4)
    gy = jnp.concatenate([receiver_crossline] * 4)
    local_x = gx - dest_x * inline_cells + halo
    local_y = gy - dest_y * cross_cells + halo
    dest = jnp.where(valid, dest_x * xl_count + dest_y, inl_count * xl_count)
    amps = jnp.concatenate([payload] * 4, axis=0)
    entries = jnp.concatenate(
        [amps, local_x.astype(jnp.float32)[:, None], local_y.astype(jnp.float32)[:, None]], axis=1
    )
    return dest, entries


def local(
    wave_p,
    wave_p_old,
    wave_q,
    wave_q_old,
    courant_square,
    thomsen_epsilon,
    thomsen_delta,
    tilt_angle,
    azimuth,
    shear_ratio,
    damping,
    trace_samples,
    resample_filter,
    line_gain,
    receiver_inline,
    receiver_crossline,
    shot_line,
):
    halo = 4
    depth, inline_cells, cross_cells = wave_p.shape
    steps = resample_filter.shape[0]
    xl_count = lax.axis_size("xl")
    gz_count = lax.axis_size("gz")
    columns = lax.axis_size("inl") * xl_count
    traces = trace_samples.shape[0]
    capacity = min(9 * (2 * traces // columns), traces)

    wide = [
        (jnp.stack([wave_p, wave_q]), 2 * halo),
        (
            jnp.stack(
                [
                    wave_p_old,
                    wave_q_old,
                    courant_square,
                    thomsen_epsilon,
                    thomsen_delta,
                    tilt_angle,
                    azimuth,
                    shear_ratio,
                    damping,
                ]
            ),
            halo,
        ),
    ]
    for axis, dim in (("inl", 2), ("gz", 1), ("xl", 3)):
        wide = exchange(wide, axis, dim)
    current_wide = wide[0][0]
    rest = wide[1][0]

    payload = step_amplitudes(trace_samples, resample_filter, line_gain, shot_line)
    dest, entries = plane_entries(
        receiver_inline, receiver_crossline, payload, inline_cells, cross_cells, halo
    )
    onehot = (dest[:, None] == jnp.arange(columns, dtype=jnp.int32)[None, :]).astype(jnp.int32)
    rank = jnp.sum(jnp.cumsum(onehot, axis=0) * onehot, axis=1) - 1
    slot = jnp.where(dest < columns, dest * (gz_count * capacity) + rank, columns * gz_count * capacity)
    width = entries.shape[1]
    send = (
        jnp.zeros((columns * gz_count * capacity, width), jnp.float32)
        .at[slot]
        .set(entries, mode="drop")
    )
    arrived = lax.all_to_all(send, ("inl", "xl", "gz"), split_axis=0, concat_axis=0, tiled=True)
    row_at = arrived[:, steps].astype(jnp.int32)
    col_at = arrived[:, steps + 1].astype(jnp.int32)
    row_hit = (
        row_at[:, None] == jnp.arange(inline_cells + 2 * halo, dtype=jnp.int32)[None, :]
    ).astype(jnp.float32)
    col_hit = (
        col_at[:, None] == jnp.arange(cross_cells + 2 * halo, dtype=jnp.int32)[None, :]
    ).astype(jnp.float32)
    weighted = arrived[:, :steps, None] * row_hit[:, None, :]
    planes = jnp.einsum("nkx,ny->kxy", weighted, col_hit, precision=lax.Precision.HIGHEST)

    inner = (slice(None), slice(halo, -halo), slice(halo, -halo), slice(halo, -halo))
    courant, eps_field, delta_field, tilt_wide, azimuth_wide, shear, damp = [rest[i] for i in range(2, 9)]
    fields_wide = (courant, eps_field, delta_field, shear, damp)
    coefs_wide = anisotropy(tilt_wide, azimuth_wide)
    first = advance_raw(current_wide, current_wide[inner], rest[0:2], fields_wide, coefs_wide)
    first = lax.optimization_barrier(first)
    first = first.at[:, halo].add(planes[0][None])

    block = inner[1:]
    fields = tuple(f[block] for f in fields_wide)
    coefs = tuple(c[block] for c in coefs_wide)
    previous = jnp.stack([wave_p, wave_q])
    second = advance_raw(first, first[inner], previous, fields, coefs)
    second = second.at[:, 0].add(planes[1][halo:-halo, halo:-halo][None])
    middle = first[inner]
    return (second[0], second[1], middle[0], middle[1])


def solution(mesh):
    return jax.shard_map(
        local,
        mesh=mesh,
        in_specs=(
            P("gz", "inl", "xl"),
            P("gz", "inl", "xl"),
            P("gz", "inl", "xl"),
            P("gz", "inl", "xl"),
            P("gz", "inl", "xl"),
            P("gz", "inl", "xl"),
            P("gz", "inl", "xl"),
            P("gz", "inl", "xl"),
            P("gz", "inl", "xl"),
            P("gz", "inl", "xl"),
            P("gz", "inl", "xl"),
            P(("inl", "xl", "gz"), None),
            P(),
            P(),
            P(("inl", "xl", "gz")),
            P(("inl", "xl", "gz")),
            P(("inl", "xl", "gz")),
        ),
        out_specs=(
            P("gz", "inl", "xl"),
            P("gz", "inl", "xl"),
            P("gz", "inl", "xl"),
            P("gz", "inl", "xl"),
        ),
        check_vma=False,
    )
```

```python
import jax
import jax.numpy as jnp
from jax import lax
from jax.sharding import PartitionSpec as P

second_coef = (-205.0 / 72.0, 8.0 / 5.0, -1.0 / 5.0, 8.0 / 315.0, -1.0 / 560.0)
first_coef = (0.0, 4.0 / 5.0, -1.0 / 5.0, 4.0 / 105.0, -1.0 / 280.0)


def with_halo(block, sides, width, tie=None):
    for index, (axis, dim) in enumerate(sides):
        if index == 1 and tie is not None:
            block, tie = lax.optimization_barrier((block, tie))
        count = lax.axis_size(axis)
        forward = [(i, i + 1) for i in range(count - 1)]
        backward = [(target, source) for source, target in forward]
        low = lax.ppermute(
            lax.slice_in_dim(block, block.shape[dim] - width, None, axis=dim), axis, forward
        )
        high = lax.ppermute(lax.slice_in_dim(block, 0, width, axis=dim), axis, backward)
        block = jnp.concatenate([low, block, high], axis=dim)
    if tie is not None:
        return block, tie
    return block


def derivatives(padded):
    depth = padded.shape[-3] - 8
    across = padded.shape[-2] - 8
    along = padded.shape[-1] - 8

    def piece(dz, dx, dy):
        return padded[
            ..., 4 + dz : 4 + dz + depth, 4 + dx : 4 + dx + across, 4 + dy : 4 + dy + along
        ]

    center = piece(0, 0, 0)
    u_zz = second_coef[0] * center
    u_xx = second_coef[0] * center
    u_yy = second_coef[0] * center
    for k in range(1, 5):
        u_zz = u_zz + second_coef[k] * (piece(k, 0, 0) + piece(-k, 0, 0))
        u_xx = u_xx + second_coef[k] * (piece(0, k, 0) + piece(0, -k, 0))
        u_yy = u_yy + second_coef[k] * (piece(0, 0, k) + piece(0, 0, -k))
    grad_x = first_coef[1] * (padded[..., :, 5 : 5 + across, :] - padded[..., :, 3 : 3 + across, :])
    grad_y = first_coef[1] * (
        padded[..., :, 4 : 4 + across, 5 : 5 + along]
        - padded[..., :, 4 : 4 + across, 3 : 3 + along]
    )
    for k in range(2, 5):
        grad_x = grad_x + first_coef[k] * (
            padded[..., :, 4 + k : 4 + k + across, :] - padded[..., :, 4 - k : 4 - k + across, :]
        )
        grad_y = grad_y + first_coef[k] * (
            padded[..., :, 4 : 4 + across, 4 + k : 4 + k + along]
            - padded[..., :, 4 : 4 + across, 4 - k : 4 - k + along]
        )
    u_xy = first_coef[1] * (
        grad_x[..., 4 : 4 + depth, :, 5 : 5 + along] - grad_x[..., 4 : 4 + depth, :, 3 : 3 + along]
    )
    u_xz = first_coef[1] * (
        grad_x[..., 5 : 5 + depth, :, 4 : 4 + along] - grad_x[..., 3 : 3 + depth, :, 4 : 4 + along]
    )
    u_yz = first_coef[1] * (grad_y[..., 5 : 5 + depth, :, :] - grad_y[..., 3 : 3 + depth, :, :])
    for k in range(2, 5):
        u_xy = u_xy + first_coef[k] * (
            grad_x[..., 4 : 4 + depth, :, 4 + k : 4 + k + along]
            - grad_x[..., 4 : 4 + depth, :, 4 - k : 4 - k + along]
        )
        u_xz = u_xz + first_coef[k] * (
            grad_x[..., 4 + k : 4 + k + depth, :, 4 : 4 + along]
            - grad_x[..., 4 - k : 4 - k + depth, :, 4 : 4 + along]
        )
        u_yz = u_yz + first_coef[k] * (
            grad_y[..., 4 + k : 4 + k + depth, :, :] - grad_y[..., 4 - k : 4 - k + depth, :, :]
        )
    return (u_zz, u_xx, u_yy, u_xy, u_xz, u_yz)


def anisotropy(tilt_angle, azimuth):
    sin_t = jnp.sin(tilt_angle)
    cos_t = jnp.cos(tilt_angle)
    sin_f = jnp.sin(azimuth)
    cos_f = jnp.cos(azimuth)
    a_xx = sin_t * sin_t * cos_f * cos_f
    a_yy = sin_t * sin_t * sin_f * sin_f
    a_zz = cos_t * cos_t
    a_xy = 2.0 * sin_t * sin_t * sin_f * cos_f
    a_xz = 2.0 * sin_t * cos_t * cos_f
    a_yz = 2.0 * sin_t * cos_t * sin_f
    return (a_xx, a_yy, a_zz, a_xy, a_xz, a_yz)


def advance_raw(padded, current, previous, fields, coefs):
    courant, eps_field, delta_field, shear, damp = fields
    a_xx, a_yy, a_zz, a_xy, a_xz, a_yz = coefs
    u_zz, u_xx, u_yy, u_xy, u_xz, u_yz = derivatives(padded)
    h_one = a_xx * u_xx + a_yy * u_yy + a_zz * u_zz + a_xy * u_xy + a_xz * u_xz + a_yz * u_yz
    h_two = u_xx + u_yy + u_zz - h_one
    wave_a = current[0]
    wave_b = current[1]
    old_a = previous[0]
    old_b = previous[1]
    new_a = (
        2.0 * wave_a
        - old_a
        + courant * ((1.0 + 2.0 * eps_field) * h_two[0] + h_one[1] + shear * (h_one[0] - h_one[1]))
        - damp * (wave_a - old_a)
    )
    new_b = (
        2.0 * wave_b
        - old_b
        + courant
        * ((1.0 + 2.0 * delta_field) * h_two[0] + h_one[1] + shear * (h_two[1] - h_two[0]))
        - damp * (wave_b - old_b)
    )
    return jnp.stack([new_a, new_b])


def step_amplitudes(samples, resample_filter, line_gain, lines):
    table = jnp.arange(line_gain.shape[0], dtype=jnp.int32)
    gains = jnp.sum(jnp.where(lines[:, None] == table[None, :], line_gain[None, :], 0.0), axis=1)
    return jnp.dot(samples, resample_filter.T, precision=lax.Precision.HIGHEST) * gains[:, None]


def plane_entries(receiver_inline, receiver_crossline, payload, inline_cells, cross_cells, halo):
    inl_count = lax.axis_size("inl")
    xl_count = lax.axis_size("xl")
    col_x = receiver_inline // inline_cells
    col_y = receiver_crossline // cross_cells
    off_x = receiver_inline % inline_cells
    off_y = receiver_crossline % cross_cells
    near_x = jnp.where(off_x < halo, col_x - 1, jnp.where(off_x >= inline_cells - halo, col_x + 1, -1))
    near_y = jnp.where(off_y < halo, col_y - 1, jnp.where(off_y >= cross_cells - halo, col_y + 1, -1))
    ok_x = (near_x >= 0) & (near_x < inl_count)
    ok_y = (near_y >= 0) & (near_y < xl_count)
    dest_x = jnp.concatenate([col_x, near_x, col_x, near_x])
    dest_y = jnp.concatenate([col_y, col_y, near_y, near_y])
    valid = jnp.concatenate([jnp.ones_like(ok_x), ok_x, ok_y, ok_x & ok_y])
    gx = jnp.concatenate([receiver_inline] * 4)
    gy = jnp.concatenate([receiver_crossline] * 4)
    local_x = gx - dest_x * inline_cells + halo
    local_y = gy - dest_y * cross_cells + halo
    dest = jnp.where(valid, dest_x * xl_count + dest_y, inl_count * xl_count)
    amps = jnp.concatenate([payload] * 4, axis=0)
    entries = jnp.concatenate(
        [amps, local_x.astype(jnp.float32)[:, None], local_y.astype(jnp.float32)[:, None]], axis=1
    )
    return dest, entries


def local(
    wave_p,
    wave_p_old,
    wave_q,
    wave_q_old,
    courant_square,
    thomsen_epsilon,
    thomsen_delta,
    tilt_angle,
    azimuth,
    shear_ratio,
    damping,
    trace_samples,
    resample_filter,
    line_gain,
    receiver_inline,
    receiver_crossline,
    shot_line,
):
    halo = 4
    depth, inline_cells, cross_cells = wave_p.shape
    steps = resample_filter.shape[0]
    xl_count = lax.axis_size("xl")
    gz_count = lax.axis_size("gz")
    columns = lax.axis_size("inl") * xl_count
    traces = trace_samples.shape[0]
    capacity = min(9 * (2 * traces // columns), traces)

    payload = step_amplitudes(trace_samples, resample_filter, line_gain, shot_line)
    dest, entries = plane_entries(
        receiver_inline, receiver_crossline, payload, inline_cells, cross_cells, halo
    )
    onehot = (dest[:, None] == jnp.arange(columns, dtype=jnp.int32)[None, :]).astype(jnp.int32)
    rank = jnp.sum(jnp.cumsum(onehot, axis=0) * onehot, axis=1) - 1
    slot = jnp.where(dest < columns, dest * (gz_count * capacity) + rank, columns * gz_count * capacity)
    width = entries.shape[1]
    send = (
        jnp.zeros((columns * gz_count * capacity, width), jnp.float32)
        .at[slot]
        .set(entries, mode="drop")
    )
    sides = (("inl", 2), ("xl", 3), ("gz", 1))
    current = jnp.stack([wave_p, wave_q])
    padded_now, send = with_halo(current, sides, halo, send)
    arrived = lax.all_to_all(send, ("inl", "xl", "gz"), split_axis=0, concat_axis=0, tiled=True)
    row_at = arrived[:, steps].astype(jnp.int32)
    col_at = arrived[:, steps + 1].astype(jnp.int32)
    row_hit = (
        row_at[:, None] == jnp.arange(inline_cells + 2 * halo, dtype=jnp.int32)[None, :]
    ).astype(jnp.float32)
    col_hit = (
        col_at[:, None] == jnp.arange(cross_cells + 2 * halo, dtype=jnp.int32)[None, :]
    ).astype(jnp.float32)
    weighted = arrived[:, :steps, None] * row_hit[:, None, :]
    planes = jnp.einsum("nkx,ny->kxy", weighted, col_hit, precision=lax.Precision.HIGHEST)

    fields = (courant_square, thomsen_epsilon, thomsen_delta, shear_ratio, damping)
    coefs = anisotropy(tilt_angle, azimuth)
    previous = jnp.stack([wave_p_old, wave_q_old])
    first = advance_raw(padded_now, current, previous, fields, coefs)
    padded = with_halo(first, sides, halo).at[:, halo].add(planes[0][None])
    first = first.at[:, 0].add(planes[0][halo:-halo, halo:-halo][None])
    second = advance_raw(padded, first, current, fields, coefs)
    second = second.at[:, 0].add(planes[1][halo:-halo, halo:-halo][None])
    return (second[0], second[1], first[0], first[1])


def solution(mesh):
    return jax.shard_map(
        local,
        mesh=mesh,
        in_specs=(
            P("gz", "inl", "xl"),
            P("gz", "inl", "xl"),
            P("gz", "inl", "xl"),
            P("gz", "inl", "xl"),
            P("gz", "inl", "xl"),
            P("gz", "inl", "xl"),
            P("gz", "inl", "xl"),
            P("gz", "inl", "xl"),
            P("gz", "inl", "xl"),
            P("gz", "inl", "xl"),
            P("gz", "inl", "xl"),
            P(("inl", "xl", "gz"), None),
            P(),
            P(),
            P(("inl", "xl", "gz")),
            P(("inl", "xl", "gz")),
            P(("inl", "xl", "gz")),
        ),
        out_specs=(
            P("gz", "inl", "xl"),
            P("gz", "inl", "xl"),
            P("gz", "inl", "xl"),
            P("gz", "inl", "xl"),
        ),
        check_vma=False,
    )
```

```python
import jax
import jax.numpy as jnp
from jax import lax
from jax.sharding import PartitionSpec as P

second_coef = (-205.0 / 72.0, 8.0 / 5.0, -1.0 / 5.0, 8.0 / 315.0, -1.0 / 560.0)
first_coef = (0.0, 4.0 / 5.0, -1.0 / 5.0, 4.0 / 105.0, -1.0 / 280.0)


def with_halo(block, sides, width):
    for axis, dim in sides:
        count = lax.axis_size(axis)
        if count == 2:
            first = lax.axis_index(axis) == 0
            top = lax.slice_in_dim(block, block.shape[dim] - width, None, axis=dim)
            bottom = lax.slice_in_dim(block, 0, width, axis=dim)
            got = lax.ppermute(jnp.where(first, top, bottom), axis, [(0, 1), (1, 0)])
            empty = jnp.zeros_like(got)
            low = jnp.where(first, empty, got)
            high = jnp.where(first, got, empty)
            block = jnp.concatenate([low, block, high], axis=dim)
            continue
        forward = [(i, i + 1) for i in range(count - 1)]
        backward = [(target, source) for source, target in forward]
        low = lax.ppermute(
            lax.slice_in_dim(block, block.shape[dim] - width, None, axis=dim), axis, forward
        )
        high = lax.ppermute(lax.slice_in_dim(block, 0, width, axis=dim), axis, backward)
        block = jnp.concatenate([low, block, high], axis=dim)
    return block


def derivatives(padded):
    depth = padded.shape[-3] - 8
    across = padded.shape[-2] - 8
    along = padded.shape[-1] - 8

    def piece(dz, dx, dy):
        return padded[
            ..., 4 + dz : 4 + dz + depth, 4 + dx : 4 + dx + across, 4 + dy : 4 + dy + along
        ]

    center = piece(0, 0, 0)
    u_zz = second_coef[0] * center
    u_xx = second_coef[0] * center
    u_yy = second_coef[0] * center
    for k in range(1, 5):
        u_zz = u_zz + second_coef[k] * (piece(k, 0, 0) + piece(-k, 0, 0))
        u_xx = u_xx + second_coef[k] * (piece(0, k, 0) + piece(0, -k, 0))
        u_yy = u_yy + second_coef[k] * (piece(0, 0, k) + piece(0, 0, -k))
    grad_x = first_coef[1] * (padded[..., :, 5 : 5 + across, :] - padded[..., :, 3 : 3 + across, :])
    grad_y = first_coef[1] * (
        padded[..., :, 4 : 4 + across, 5 : 5 + along]
        - padded[..., :, 4 : 4 + across, 3 : 3 + along]
    )
    for k in range(2, 5):
        grad_x = grad_x + first_coef[k] * (
            padded[..., :, 4 + k : 4 + k + across, :] - padded[..., :, 4 - k : 4 - k + across, :]
        )
        grad_y = grad_y + first_coef[k] * (
            padded[..., :, 4 : 4 + across, 4 + k : 4 + k + along]
            - padded[..., :, 4 : 4 + across, 4 - k : 4 - k + along]
        )
    u_xy = first_coef[1] * (
        grad_x[..., 4 : 4 + depth, :, 5 : 5 + along] - grad_x[..., 4 : 4 + depth, :, 3 : 3 + along]
    )
    u_xz = first_coef[1] * (
        grad_x[..., 5 : 5 + depth, :, 4 : 4 + along] - grad_x[..., 3 : 3 + depth, :, 4 : 4 + along]
    )
    u_yz = first_coef[1] * (grad_y[..., 5 : 5 + depth, :, :] - grad_y[..., 3 : 3 + depth, :, :])
    for k in range(2, 5):
        u_xy = u_xy + first_coef[k] * (
            grad_x[..., 4 : 4 + depth, :, 4 + k : 4 + k + along]
            - grad_x[..., 4 : 4 + depth, :, 4 - k : 4 - k + along]
        )
        u_xz = u_xz + first_coef[k] * (
            grad_x[..., 4 + k : 4 + k + depth, :, 4 : 4 + along]
            - grad_x[..., 4 - k : 4 - k + depth, :, 4 : 4 + along]
        )
        u_yz = u_yz + first_coef[k] * (
            grad_y[..., 4 + k : 4 + k + depth, :, :] - grad_y[..., 4 - k : 4 - k + depth, :, :]
        )
    return (u_zz, u_xx, u_yy, u_xy, u_xz, u_yz)


def anisotropy(tilt_angle, azimuth):
    sin_t = jnp.sin(tilt_angle)
    cos_t = jnp.cos(tilt_angle)
    sin_f = jnp.sin(azimuth)
    cos_f = jnp.cos(azimuth)
    a_xx = sin_t * sin_t * cos_f * cos_f
    a_yy = sin_t * sin_t * sin_f * sin_f
    a_zz = cos_t * cos_t
    a_xy = 2.0 * sin_t * sin_t * sin_f * cos_f
    a_xz = 2.0 * sin_t * cos_t * cos_f
    a_yz = 2.0 * sin_t * cos_t * sin_f
    return (a_xx, a_yy, a_zz, a_xy, a_xz, a_yz)


def advance(padded, current, previous, fields, coefs, plane, top):
    courant, eps_field, delta_field, shear, damp = fields
    a_xx, a_yy, a_zz, a_xy, a_xz, a_yz = coefs
    u_zz, u_xx, u_yy, u_xy, u_xz, u_yz = derivatives(padded)
    h_one = a_xx * u_xx + a_yy * u_yy + a_zz * u_zz + a_xy * u_xy + a_xz * u_xz + a_yz * u_yz
    h_two = u_xx + u_yy + u_zz - h_one
    wave_a = current[0]
    wave_b = current[1]
    old_a = previous[0]
    old_b = previous[1]
    new_a = (
        2.0 * wave_a
        - old_a
        + courant * ((1.0 + 2.0 * eps_field) * h_two[0] + h_one[1] + shear * (h_one[0] - h_one[1]))
        - damp * (wave_a - old_a)
    )
    new_b = (
        2.0 * wave_b
        - old_b
        + courant
        * ((1.0 + 2.0 * delta_field) * h_two[0] + h_one[1] + shear * (h_two[1] - h_two[0]))
        - damp * (wave_b - old_b)
    )
    new_a = new_a.at[top].add(plane)
    new_b = new_b.at[top].add(plane)
    return jnp.stack([new_a, new_b])


def step_amplitudes(samples, resample_filter, line_gain, lines):
    table = jnp.arange(line_gain.shape[0], dtype=jnp.int32)
    gains = jnp.sum(jnp.where(lines[:, None] == table[None, :], line_gain[None, :], 0.0), axis=1)
    return jnp.dot(samples, resample_filter.T, precision=lax.Precision.HIGHEST) * gains[:, None]


def local(
    wave_p,
    wave_p_old,
    wave_q,
    wave_q_old,
    courant_square,
    thomsen_epsilon,
    thomsen_delta,
    tilt_angle,
    azimuth,
    shear_ratio,
    damping,
    trace_samples,
    resample_filter,
    line_gain,
    receiver_inline,
    receiver_crossline,
    shot_line,
):
    depth, inline_cells, cross_cells = wave_p.shape
    cells = inline_cells * cross_cells
    steps = resample_filter.shape[0]
    xl_count = lax.axis_size("xl")
    gz_count = lax.axis_size("gz")
    columns = lax.axis_size("inl") * xl_count
    capacity = 2 * trace_samples.shape[0] // columns
    owner = receiver_inline // inline_cells * xl_count + receiver_crossline // cross_cells
    local_cell = receiver_inline % inline_cells * cross_cells + receiver_crossline % cross_cells
    payload = step_amplitudes(trace_samples, resample_filter, line_gain, shot_line)
    onehot = (owner[:, None] == jnp.arange(columns, dtype=jnp.int32)[None, :]).astype(jnp.int32)
    rank = jnp.sum(jnp.cumsum(onehot, axis=0) * onehot, axis=1) - 1
    slot = owner * (gz_count * capacity) + rank
    packed = jnp.concatenate([payload, local_cell.astype(jnp.float32)[:, None]], axis=1)
    width = packed.shape[1]
    send = jnp.zeros((columns * gz_count * capacity, width), jnp.float32).at[slot].set(packed)
    arrived = lax.all_to_all(send, ("inl", "xl", "gz"), split_axis=0, concat_axis=0, tiled=True)
    target = arrived[:, steps].astype(jnp.int32)
    row_hit = (
        target[:, None] // cross_cells == jnp.arange(inline_cells, dtype=jnp.int32)[None, :]
    ).astype(jnp.float32)
    col_hit = (
        target[:, None] % cross_cells == jnp.arange(cross_cells, dtype=jnp.int32)[None, :]
    ).astype(jnp.float32)
    weighted = arrived[:, :steps, None] * row_hit[:, None, :]
    planes = jnp.einsum("nkx,ny->kxy", weighted, col_hit, precision=lax.Precision.HIGHEST)
    fields = (courant_square, thomsen_epsilon, thomsen_delta, shear_ratio, damping)
    current = jnp.stack([wave_p, wave_q])
    previous = jnp.stack([wave_p_old, wave_q_old])
    coefs = anisotropy(tilt_angle, azimuth)
    for step in range(steps):
        padded = with_halo(current, (("inl", 2), ("xl", 3), ("gz", 1)), 4)
        newer = advance(padded, current, previous, fields, coefs, planes[step], 0)
        previous = current
        current = newer
    return (current[0], current[1], previous[0], previous[1])


def solution(mesh):
    return jax.shard_map(
        local,
        mesh=mesh,
        in_specs=(
            P("gz", "inl", "xl"),
            P("gz", "inl", "xl"),
            P("gz", "inl", "xl"),
            P("gz", "inl", "xl"),
            P("gz", "inl", "xl"),
            P("gz", "inl", "xl"),
            P("gz", "inl", "xl"),
            P("gz", "inl", "xl"),
            P("gz", "inl", "xl"),
            P("gz", "inl", "xl"),
            P("gz", "inl", "xl"),
            P(("inl", "xl", "gz"), None),
            P(),
            P(),
            P(("inl", "xl", "gz")),
            P(("inl", "xl", "gz")),
            P(("inl", "xl", "gz")),
        ),
        out_specs=(
            P("gz", "inl", "xl"),
            P("gz", "inl", "xl"),
            P("gz", "inl", "xl"),
            P("gz", "inl", "xl"),
        ),
        check_vma=False,
    )
```

```python
import jax
import jax.numpy as jnp
from jax import lax
from jax.sharding import PartitionSpec as P

second_coef = (-205.0 / 72.0, 8.0 / 5.0, -1.0 / 5.0, 8.0 / 315.0, -1.0 / 560.0)
first_coef = (0.0, 4.0 / 5.0, -1.0 / 5.0, 4.0 / 105.0, -1.0 / 280.0)


def with_halo(block, sides, width):
    for axis, dim in sides:
        count = lax.axis_size(axis)
        if count == 2:
            first = lax.axis_index(axis) == 0
            top = lax.slice_in_dim(block, block.shape[dim] - width, None, axis=dim)
            bottom = lax.slice_in_dim(block, 0, width, axis=dim)
            got = lax.ppermute(jnp.where(first, top, bottom), axis, [(0, 1), (1, 0)])
            empty = jnp.zeros_like(got)
            low = jnp.where(first, empty, got)
            high = jnp.where(first, got, empty)
            block = jnp.concatenate([low, block, high], axis=dim)
            continue
        forward = [(i, i + 1) for i in range(count - 1)]
        backward = [(target, source) for source, target in forward]
        low = lax.ppermute(
            lax.slice_in_dim(block, block.shape[dim] - width, None, axis=dim), axis, forward
        )
        high = lax.ppermute(lax.slice_in_dim(block, 0, width, axis=dim), axis, backward)
        block = jnp.concatenate([low, block, high], axis=dim)
    return block


def derivatives(padded):
    depth = padded.shape[-3] - 8
    across = padded.shape[-2] - 8
    along = padded.shape[-1] - 8

    def piece(dz, dx, dy):
        return padded[
            ..., 4 + dz : 4 + dz + depth, 4 + dx : 4 + dx + across, 4 + dy : 4 + dy + along
        ]

    center = piece(0, 0, 0)
    u_zz = second_coef[0] * center
    u_xx = second_coef[0] * center
    u_yy = second_coef[0] * center
    for k in range(1, 5):
        u_zz = u_zz + second_coef[k] * (piece(k, 0, 0) + piece(-k, 0, 0))
        u_xx = u_xx + second_coef[k] * (piece(0, k, 0) + piece(0, -k, 0))
        u_yy = u_yy + second_coef[k] * (piece(0, 0, k) + piece(0, 0, -k))
    grad_x = first_coef[1] * (padded[..., :, 5 : 5 + across, :] - padded[..., :, 3 : 3 + across, :])
    grad_y = first_coef[1] * (
        padded[..., :, 4 : 4 + across, 5 : 5 + along]
        - padded[..., :, 4 : 4 + across, 3 : 3 + along]
    )
    for k in range(2, 5):
        grad_x = grad_x + first_coef[k] * (
            padded[..., :, 4 + k : 4 + k + across, :] - padded[..., :, 4 - k : 4 - k + across, :]
        )
        grad_y = grad_y + first_coef[k] * (
            padded[..., :, 4 : 4 + across, 4 + k : 4 + k + along]
            - padded[..., :, 4 : 4 + across, 4 - k : 4 - k + along]
        )
    u_xy = first_coef[1] * (
        grad_x[..., 4 : 4 + depth, :, 5 : 5 + along] - grad_x[..., 4 : 4 + depth, :, 3 : 3 + along]
    )
    u_xz = first_coef[1] * (
        grad_x[..., 5 : 5 + depth, :, 4 : 4 + along] - grad_x[..., 3 : 3 + depth, :, 4 : 4 + along]
    )
    u_yz = first_coef[1] * (grad_y[..., 5 : 5 + depth, :, :] - grad_y[..., 3 : 3 + depth, :, :])
    for k in range(2, 5):
        u_xy = u_xy + first_coef[k] * (
            grad_x[..., 4 : 4 + depth, :, 4 + k : 4 + k + along]
            - grad_x[..., 4 : 4 + depth, :, 4 - k : 4 - k + along]
        )
        u_xz = u_xz + first_coef[k] * (
            grad_x[..., 4 + k : 4 + k + depth, :, 4 : 4 + along]
            - grad_x[..., 4 - k : 4 - k + depth, :, 4 : 4 + along]
        )
        u_yz = u_yz + first_coef[k] * (
            grad_y[..., 4 + k : 4 + k + depth, :, :] - grad_y[..., 4 - k : 4 - k + depth, :, :]
        )
    return (u_zz, u_xx, u_yy, u_xy, u_xz, u_yz)


def anisotropy(tilt_angle, azimuth):
    sin_t = jnp.sin(tilt_angle)
    cos_t = jnp.cos(tilt_angle)
    sin_f = jnp.sin(azimuth)
    cos_f = jnp.cos(azimuth)
    a_xx = sin_t * sin_t * cos_f * cos_f
    a_yy = sin_t * sin_t * sin_f * sin_f
    a_zz = cos_t * cos_t
    a_xy = 2.0 * sin_t * sin_t * sin_f * cos_f
    a_xz = 2.0 * sin_t * cos_t * cos_f
    a_yz = 2.0 * sin_t * cos_t * sin_f
    return (a_xx, a_yy, a_zz, a_xy, a_xz, a_yz)


def advance(padded, current, previous, fields, coefs, plane, top):
    courant, eps_field, delta_field, shear, damp = fields
    a_xx, a_yy, a_zz, a_xy, a_xz, a_yz = coefs
    u_zz, u_xx, u_yy, u_xy, u_xz, u_yz = derivatives(padded)
    h_one = a_xx * u_xx + a_yy * u_yy + a_zz * u_zz + a_xy * u_xy + a_xz * u_xz + a_yz * u_yz
    h_two = u_xx + u_yy + u_zz - h_one
    wave_a = current[0]
    wave_b = current[1]
    old_a = previous[0]
    old_b = previous[1]
    new_a = (
        2.0 * wave_a
        - old_a
        + courant * ((1.0 + 2.0 * eps_field) * h_two[0] + h_one[1] + shear * (h_one[0] - h_one[1]))
        - damp * (wave_a - old_a)
    )
    new_b = (
        2.0 * wave_b
        - old_b
        + courant
        * ((1.0 + 2.0 * delta_field) * h_two[0] + h_one[1] + shear * (h_two[1] - h_two[0]))
        - damp * (wave_b - old_b)
    )
    new_a = new_a.at[top].add(plane)
    new_b = new_b.at[top].add(plane)
    return jnp.stack([new_a, new_b])


def step_amplitudes(samples, resample_filter, line_gain, lines):
    table = jnp.arange(line_gain.shape[0], dtype=jnp.int32)
    gains = jnp.sum(jnp.where(lines[:, None] == table[None, :], line_gain[None, :], 0.0), axis=1)
    return jnp.dot(samples, resample_filter.T, precision=lax.Precision.HIGHEST) * gains[:, None]


def local(
    wave_p,
    wave_p_old,
    wave_q,
    wave_q_old,
    courant_square,
    thomsen_epsilon,
    thomsen_delta,
    tilt_angle,
    azimuth,
    shear_ratio,
    damping,
    trace_samples,
    resample_filter,
    line_gain,
    receiver_inline,
    receiver_crossline,
    shot_line,
):
    depth, inline_cells, cross_cells = wave_p.shape
    cells = inline_cells * cross_cells
    steps = resample_filter.shape[0]
    xl_count = lax.axis_size("xl")
    gz_count = lax.axis_size("gz")
    columns = lax.axis_size("inl") * xl_count
    capacity = 2 * trace_samples.shape[0] // columns
    devices = columns * gz_count
    owner = receiver_inline // inline_cells * xl_count + receiver_crossline // cross_cells
    local_cell = receiver_inline % inline_cells * cross_cells + receiver_crossline % cross_cells
    payload = step_amplitudes(trace_samples, resample_filter, line_gain, shot_line)
    traces = owner.shape[0]
    highest = lax.Precision.HIGHEST
    in_column = (owner[:, None] == jnp.arange(columns, dtype=jnp.int32)[None, :]).astype(jnp.float32)
    order = jnp.arange(traces, dtype=jnp.int32)
    earlier = (order[:, None] > order[None, :]).astype(jnp.float32)
    rank = jnp.sum(jnp.dot(earlier, in_column, precision=highest) * in_column, axis=1)
    lane = jnp.arange(3 * capacity, dtype=jnp.int32)[None, :]
    value = jnp.where(
        lane < capacity,
        payload[:, 0:1],
        jnp.where(lane < 2 * capacity, payload[:, 1:2], local_cell.astype(jnp.float32)[:, None]),
    )
    spread = jnp.where(rank.astype(jnp.int32)[:, None] == lane % capacity, value, 0.0)
    to_device = (
        (owner * gz_count)[:, None] == jnp.arange(devices, dtype=jnp.int32)[None, :]
    ).astype(jnp.float32)
    send = lax.dot_general(to_device, spread, (((0,), (0,)), ((), ())), precision=highest)
    arrived = lax.all_to_all(send, ("inl", "xl", "gz"), split_axis=0, concat_axis=0, tiled=True)
    amp = arrived[:, : steps * capacity].reshape(devices, steps, capacity)
    cell = (arrived[:, steps * capacity :] + 0.5).astype(jnp.int32)
    row_hit = (
        cell[None, :, :] // cross_cells
        == jnp.arange(inline_cells, dtype=jnp.int32)[:, None, None]
    ).astype(jnp.float32)
    col_hit = (
        cell[None, :, :] % cross_cells == jnp.arange(cross_cells, dtype=jnp.int32)[:, None, None]
    ).astype(jnp.float32)
    weighted = (jnp.transpose(amp, (1, 0, 2))[:, None] * row_hit[None]).reshape(
        steps * inline_cells, devices, capacity
    )
    planes = lax.dot_general(
        weighted, col_hit, (((1, 2), (1, 2)), ((), ())), precision=highest
    ).reshape(steps, inline_cells, cross_cells)
    fields = (courant_square, thomsen_epsilon, thomsen_delta, shear_ratio, damping)
    current = jnp.stack([wave_p, wave_q])
    previous = jnp.stack([wave_p_old, wave_q_old])
    coefs = anisotropy(tilt_angle, azimuth)
    for step in range(steps):
        padded = with_halo(current, (("inl", 2), ("xl", 3), ("gz", 1)), 4)
        newer = advance(padded, current, previous, fields, coefs, planes[step], 0)
        previous = current
        current = newer
    return (current[0], current[1], previous[0], previous[1])


def solution(mesh):
    return jax.shard_map(
        local,
        mesh=mesh,
        in_specs=(
            P("gz", "inl", "xl"),
            P("gz", "inl", "xl"),
            P("gz", "inl", "xl"),
            P("gz", "inl", "xl"),
            P("gz", "inl", "xl"),
            P("gz", "inl", "xl"),
            P("gz", "inl", "xl"),
            P("gz", "inl", "xl"),
            P("gz", "inl", "xl"),
            P("gz", "inl", "xl"),
            P("gz", "inl", "xl"),
            P(("inl", "xl", "gz"), None),
            P(),
            P(),
            P(("inl", "xl", "gz")),
            P(("inl", "xl", "gz")),
            P(("inl", "xl", "gz")),
        ),
        out_specs=(
            P("gz", "inl", "xl"),
            P("gz", "inl", "xl"),
            P("gz", "inl", "xl"),
            P("gz", "inl", "xl"),
        ),
        check_vma=False,
    )
```

```python
import jax
import jax.numpy as jnp
from jax import lax
from jax.sharding import PartitionSpec as P

second_coef = (-205.0 / 72.0, 8.0 / 5.0, -1.0 / 5.0, 8.0 / 315.0, -1.0 / 560.0)
first_coef = (0.0, 4.0 / 5.0, -1.0 / 5.0, 4.0 / 105.0, -1.0 / 280.0)


def shift_pair(top, bottom, axis):
    count = lax.axis_size(axis)
    if count == 2:
        first = lax.axis_index(axis) == 0
        got = lax.ppermute(jnp.where(first, top, bottom), axis, [(0, 1), (1, 0)])
        empty = jnp.zeros_like(got)
        return jnp.where(first, empty, got), jnp.where(first, got, empty)
    forward = [(i, i + 1) for i in range(count - 1)]
    backward = [(target, source) for source, target in forward]
    return lax.ppermute(top, axis, forward), lax.ppermute(bottom, axis, backward)


def with_halo(block, width):
    cut = lambda a, dim, lo, hi: lax.slice_in_dim(a, lo, hi, axis=dim)
    depth, across, along = block.shape[1:]
    low_x, high_x = shift_pair(cut(block, 2, across - width, None), cut(block, 2, 0, width), "inl")
    low_y, high_y = shift_pair(cut(block, 3, along - width, None), cut(block, 3, 0, width), "xl")
    strips = jnp.concatenate([low_x, high_x], axis=2)
    low_c, high_c = shift_pair(cut(strips, 3, along - width, None), cut(strips, 3, 0, width), "xl")
    wide_x = jnp.concatenate([low_x, block, high_x], axis=2)
    pad_x = ((0, 0), (0, 0), (width, width), (0, 0))
    bare = jnp.concatenate([jnp.pad(low_y, pad_x), wide_x, jnp.pad(high_y, pad_x)], axis=3)
    low_z, high_z = shift_pair(cut(bare, 1, depth - width, None), cut(bare, 1, 0, width), "gz")
    side_low = jnp.concatenate([low_c[:, :, :width], low_y, low_c[:, :, width:]], axis=2)
    side_high = jnp.concatenate([high_c[:, :, :width], high_y, high_c[:, :, width:]], axis=2)
    full = jnp.concatenate([side_low, wide_x, side_high], axis=3)
    return jnp.concatenate([low_z, full, high_z], axis=1)


def derivatives(padded):
    depth = padded.shape[-3] - 8
    across = padded.shape[-2] - 8
    along = padded.shape[-1] - 8

    def piece(dz, dx, dy):
        return padded[
            ..., 4 + dz : 4 + dz + depth, 4 + dx : 4 + dx + across, 4 + dy : 4 + dy + along
        ]

    center = piece(0, 0, 0)
    u_zz = second_coef[0] * center
    u_xx = second_coef[0] * center
    u_yy = second_coef[0] * center
    for k in range(1, 5):
        u_zz = u_zz + second_coef[k] * (piece(k, 0, 0) + piece(-k, 0, 0))
        u_xx = u_xx + second_coef[k] * (piece(0, k, 0) + piece(0, -k, 0))
        u_yy = u_yy + second_coef[k] * (piece(0, 0, k) + piece(0, 0, -k))
    grad_x = first_coef[1] * (padded[..., :, 5 : 5 + across, :] - padded[..., :, 3 : 3 + across, :])
    grad_y = first_coef[1] * (
        padded[..., :, 4 : 4 + across, 5 : 5 + along]
        - padded[..., :, 4 : 4 + across, 3 : 3 + along]
    )
    for k in range(2, 5):
        grad_x = grad_x + first_coef[k] * (
            padded[..., :, 4 + k : 4 + k + across, :] - padded[..., :, 4 - k : 4 - k + across, :]
        )
        grad_y = grad_y + first_coef[k] * (
            padded[..., :, 4 : 4 + across, 4 + k : 4 + k + along]
            - padded[..., :, 4 : 4 + across, 4 - k : 4 - k + along]
        )
    u_xy = first_coef[1] * (
        grad_x[..., 4 : 4 + depth, :, 5 : 5 + along] - grad_x[..., 4 : 4 + depth, :, 3 : 3 + along]
    )
    u_xz = first_coef[1] * (
        grad_x[..., 5 : 5 + depth, :, 4 : 4 + along] - grad_x[..., 3 : 3 + depth, :, 4 : 4 + along]
    )
    u_yz = first_coef[1] * (grad_y[..., 5 : 5 + depth, :, :] - grad_y[..., 3 : 3 + depth, :, :])
    for k in range(2, 5):
        u_xy = u_xy + first_coef[k] * (
            grad_x[..., 4 : 4 + depth, :, 4 + k : 4 + k + along]
            - grad_x[..., 4 : 4 + depth, :, 4 - k : 4 - k + along]
        )
        u_xz = u_xz + first_coef[k] * (
            grad_x[..., 4 + k : 4 + k + depth, :, 4 : 4 + along]
            - grad_x[..., 4 - k : 4 - k + depth, :, 4 : 4 + along]
        )
        u_yz = u_yz + first_coef[k] * (
            grad_y[..., 4 + k : 4 + k + depth, :, :] - grad_y[..., 4 - k : 4 - k + depth, :, :]
        )
    return (u_zz, u_xx, u_yy, u_xy, u_xz, u_yz)


def anisotropy(tilt_angle, azimuth):
    sin_t = jnp.sin(tilt_angle)
    cos_t = jnp.cos(tilt_angle)
    sin_f = jnp.sin(azimuth)
    cos_f = jnp.cos(azimuth)
    a_xx = sin_t * sin_t * cos_f * cos_f
    a_yy = sin_t * sin_t * sin_f * sin_f
    a_zz = cos_t * cos_t
    a_xy = 2.0 * sin_t * sin_t * sin_f * cos_f
    a_xz = 2.0 * sin_t * cos_t * cos_f
    a_yz = 2.0 * sin_t * cos_t * sin_f
    return (a_xx, a_yy, a_zz, a_xy, a_xz, a_yz)


def advance(padded, current, previous, fields, coefs, plane, top):
    courant, eps_field, delta_field, shear, damp = fields
    a_xx, a_yy, a_zz, a_xy, a_xz, a_yz = coefs
    u_zz, u_xx, u_yy, u_xy, u_xz, u_yz = derivatives(padded)
    h_one = a_xx * u_xx + a_yy * u_yy + a_zz * u_zz + a_xy * u_xy + a_xz * u_xz + a_yz * u_yz
    h_two = u_xx + u_yy + u_zz - h_one
    wave_a = current[0]
    wave_b = current[1]
    old_a = previous[0]
    old_b = previous[1]
    new_a = (
        2.0 * wave_a
        - old_a
        + courant * ((1.0 + 2.0 * eps_field) * h_two[0] + h_one[1] + shear * (h_one[0] - h_one[1]))
        - damp * (wave_a - old_a)
    )
    new_b = (
        2.0 * wave_b
        - old_b
        + courant
        * ((1.0 + 2.0 * delta_field) * h_two[0] + h_one[1] + shear * (h_two[1] - h_two[0]))
        - damp * (wave_b - old_b)
    )
    new_a = new_a.at[top].add(plane)
    new_b = new_b.at[top].add(plane)
    return jnp.stack([new_a, new_b])


def step_amplitudes(samples, resample_filter, line_gain, lines):
    table = jnp.arange(line_gain.shape[0], dtype=jnp.int32)
    gains = jnp.sum(jnp.where(lines[:, None] == table[None, :], line_gain[None, :], 0.0), axis=1)
    return jnp.dot(samples, resample_filter.T, precision=lax.Precision.HIGHEST) * gains[:, None]


def local(
    wave_p,
    wave_p_old,
    wave_q,
    wave_q_old,
    courant_square,
    thomsen_epsilon,
    thomsen_delta,
    tilt_angle,
    azimuth,
    shear_ratio,
    damping,
    trace_samples,
    resample_filter,
    line_gain,
    receiver_inline,
    receiver_crossline,
    shot_line,
):
    depth, inline_cells, cross_cells = wave_p.shape
    cells = inline_cells * cross_cells
    steps = resample_filter.shape[0]
    xl_count = lax.axis_size("xl")
    gz_count = lax.axis_size("gz")
    columns = lax.axis_size("inl") * xl_count
    capacity = 2 * trace_samples.shape[0] // columns
    devices = columns * gz_count
    owner = receiver_inline // inline_cells * xl_count + receiver_crossline // cross_cells
    local_cell = receiver_inline % inline_cells * cross_cells + receiver_crossline % cross_cells
    payload = step_amplitudes(trace_samples, resample_filter, line_gain, shot_line)
    traces = owner.shape[0]
    highest = lax.Precision.HIGHEST
    in_column = (owner[:, None] == jnp.arange(columns, dtype=jnp.int32)[None, :]).astype(jnp.float32)
    order = jnp.arange(traces, dtype=jnp.int32)
    earlier = (order[:, None] > order[None, :]).astype(jnp.float32)
    rank = jnp.sum(jnp.dot(earlier, in_column, precision=highest) * in_column, axis=1)
    lane = jnp.arange(3 * capacity, dtype=jnp.int32)[None, :]
    value = jnp.where(
        lane < capacity,
        payload[:, 0:1],
        jnp.where(lane < 2 * capacity, payload[:, 1:2], local_cell.astype(jnp.float32)[:, None]),
    )
    spread = jnp.where(rank.astype(jnp.int32)[:, None] == lane % capacity, value, 0.0)
    to_device = (
        (owner * gz_count)[:, None] == jnp.arange(devices, dtype=jnp.int32)[None, :]
    ).astype(jnp.float32)
    send = lax.dot_general(to_device, spread, (((0,), (0,)), ((), ())), precision=highest)
    arrived = lax.all_to_all(send, ("inl", "xl", "gz"), split_axis=0, concat_axis=0, tiled=True)
    amp = arrived[:, : steps * capacity].reshape(devices, steps, capacity)
    cell = (arrived[:, steps * capacity :] + 0.5).astype(jnp.int32)
    row_hit = (
        cell[None, :, :] // cross_cells
        == jnp.arange(inline_cells, dtype=jnp.int32)[:, None, None]
    ).astype(jnp.float32)
    col_hit = (
        cell[None, :, :] % cross_cells == jnp.arange(cross_cells, dtype=jnp.int32)[:, None, None]
    ).astype(jnp.float32)
    weighted = (jnp.transpose(amp, (1, 0, 2))[:, None] * row_hit[None]).reshape(
        steps * inline_cells, devices, capacity
    )
    planes = lax.dot_general(
        weighted, col_hit, (((1, 2), (1, 2)), ((), ())), precision=highest
    ).reshape(steps, inline_cells, cross_cells)
    fields = (courant_square, thomsen_epsilon, thomsen_delta, shear_ratio, damping)
    current = jnp.stack([wave_p, wave_q])
    previous = jnp.stack([wave_p_old, wave_q_old])
    coefs = anisotropy(tilt_angle, azimuth)
    for step in range(steps):
        padded = with_halo(current, 4)
        newer = advance(padded, current, previous, fields, coefs, planes[step], 0)
        previous = current
        current = newer
    return (current[0], current[1], previous[0], previous[1])


def solution(mesh):
    return jax.shard_map(
        local,
        mesh=mesh,
        in_specs=(
            P("gz", "inl", "xl"),
            P("gz", "inl", "xl"),
            P("gz", "inl", "xl"),
            P("gz", "inl", "xl"),
            P("gz", "inl", "xl"),
            P("gz", "inl", "xl"),
            P("gz", "inl", "xl"),
            P("gz", "inl", "xl"),
            P("gz", "inl", "xl"),
            P("gz", "inl", "xl"),
            P("gz", "inl", "xl"),
            P(("inl", "xl", "gz"), None),
            P(),
            P(),
            P(("inl", "xl", "gz")),
            P(("inl", "xl", "gz")),
            P(("inl", "xl", "gz")),
        ),
        out_specs=(
            P("gz", "inl", "xl"),
            P("gz", "inl", "xl"),
            P("gz", "inl", "xl"),
            P("gz", "inl", "xl"),
        ),
        check_vma=False,
    )
```

```python
import jax
import jax.numpy as jnp
from jax import lax
from jax.sharding import PartitionSpec as P

second_coef = (-205.0 / 72.0, 8.0 / 5.0, -1.0 / 5.0, 8.0 / 315.0, -1.0 / 560.0)
first_coef = (0.0, 4.0 / 5.0, -1.0 / 5.0, 4.0 / 105.0, -1.0 / 280.0)


def shift_pair(top, bottom, axis):
    count = lax.axis_size(axis)
    if count == 2:
        first = lax.axis_index(axis) == 0
        got = lax.ppermute(jnp.where(first, top, bottom), axis, [(0, 1), (1, 0)])
        empty = jnp.zeros_like(got)
        return jnp.where(first, empty, got), jnp.where(first, got, empty)
    forward = [(i, i + 1) for i in range(count - 1)]
    backward = [(target, source) for source, target in forward]
    return lax.ppermute(top, axis, forward), lax.ppermute(bottom, axis, backward)


def first_round(block, width):
    cut = lambda a, dim, lo, hi: lax.slice_in_dim(a, lo, hi, axis=dim)
    across, along = block.shape[2:]
    low_x, high_x = shift_pair(cut(block, 2, across - width, None), cut(block, 2, 0, width), "inl")
    low_y, high_y = shift_pair(cut(block, 3, along - width, None), cut(block, 3, 0, width), "xl")
    return low_x, high_x, low_y, high_y


def second_round(block, width, faces):
    cut = lambda a, dim, lo, hi: lax.slice_in_dim(a, lo, hi, axis=dim)
    depth, along = block.shape[1], block.shape[3]
    low_x, high_x, low_y, high_y = faces
    strips = jnp.concatenate([low_x, high_x], axis=2)
    low_c, high_c = shift_pair(cut(strips, 3, along - width, None), cut(strips, 3, 0, width), "xl")
    wide_x = jnp.concatenate([low_x, block, high_x], axis=2)
    pad_x = ((0, 0), (0, 0), (width, width), (0, 0))
    bare = jnp.concatenate([jnp.pad(low_y, pad_x), wide_x, jnp.pad(high_y, pad_x)], axis=3)
    low_z, high_z = shift_pair(cut(bare, 1, depth - width, None), cut(bare, 1, 0, width), "gz")
    side_low = jnp.concatenate([low_c[:, :, :width], low_y, low_c[:, :, width:]], axis=2)
    side_high = jnp.concatenate([high_c[:, :, :width], high_y, high_c[:, :, width:]], axis=2)
    full = jnp.concatenate([side_low, wide_x, side_high], axis=3)
    return jnp.concatenate([low_z, full, high_z], axis=1)


def with_halo(block, width):
    return second_round(block, width, first_round(block, width))


def derivatives(padded):
    depth = padded.shape[-3] - 8
    across = padded.shape[-2] - 8
    along = padded.shape[-1] - 8

    def piece(dz, dx, dy):
        return padded[
            ..., 4 + dz : 4 + dz + depth, 4 + dx : 4 + dx + across, 4 + dy : 4 + dy + along
        ]

    center = piece(0, 0, 0)
    u_zz = second_coef[0] * center
    u_xx = second_coef[0] * center
    u_yy = second_coef[0] * center
    for k in range(1, 5):
        u_zz = u_zz + second_coef[k] * (piece(k, 0, 0) + piece(-k, 0, 0))
        u_xx = u_xx + second_coef[k] * (piece(0, k, 0) + piece(0, -k, 0))
        u_yy = u_yy + second_coef[k] * (piece(0, 0, k) + piece(0, 0, -k))
    grad_x = first_coef[1] * (padded[..., :, 5 : 5 + across, :] - padded[..., :, 3 : 3 + across, :])
    grad_y = first_coef[1] * (
        padded[..., :, 4 : 4 + across, 5 : 5 + along]
        - padded[..., :, 4 : 4 + across, 3 : 3 + along]
    )
    for k in range(2, 5):
        grad_x = grad_x + first_coef[k] * (
            padded[..., :, 4 + k : 4 + k + across, :] - padded[..., :, 4 - k : 4 - k + across, :]
        )
        grad_y = grad_y + first_coef[k] * (
            padded[..., :, 4 : 4 + across, 4 + k : 4 + k + along]
            - padded[..., :, 4 : 4 + across, 4 - k : 4 - k + along]
        )
    u_xy = first_coef[1] * (
        grad_x[..., 4 : 4 + depth, :, 5 : 5 + along] - grad_x[..., 4 : 4 + depth, :, 3 : 3 + along]
    )
    u_xz = first_coef[1] * (
        grad_x[..., 5 : 5 + depth, :, 4 : 4 + along] - grad_x[..., 3 : 3 + depth, :, 4 : 4 + along]
    )
    u_yz = first_coef[1] * (grad_y[..., 5 : 5 + depth, :, :] - grad_y[..., 3 : 3 + depth, :, :])
    for k in range(2, 5):
        u_xy = u_xy + first_coef[k] * (
            grad_x[..., 4 : 4 + depth, :, 4 + k : 4 + k + along]
            - grad_x[..., 4 : 4 + depth, :, 4 - k : 4 - k + along]
        )
        u_xz = u_xz + first_coef[k] * (
            grad_x[..., 4 + k : 4 + k + depth, :, 4 : 4 + along]
            - grad_x[..., 4 - k : 4 - k + depth, :, 4 : 4 + along]
        )
        u_yz = u_yz + first_coef[k] * (
            grad_y[..., 4 + k : 4 + k + depth, :, :] - grad_y[..., 4 - k : 4 - k + depth, :, :]
        )
    return (u_zz, u_xx, u_yy, u_xy, u_xz, u_yz)


def anisotropy(tilt_angle, azimuth):
    sin_t = jnp.sin(tilt_angle)
    cos_t = jnp.cos(tilt_angle)
    sin_f = jnp.sin(azimuth)
    cos_f = jnp.cos(azimuth)
    a_xx = sin_t * sin_t * cos_f * cos_f
    a_yy = sin_t * sin_t * sin_f * sin_f
    a_zz = cos_t * cos_t
    a_xy = 2.0 * sin_t * sin_t * sin_f * cos_f
    a_xz = 2.0 * sin_t * cos_t * cos_f
    a_yz = 2.0 * sin_t * cos_t * sin_f
    return (a_xx, a_yy, a_zz, a_xy, a_xz, a_yz)


def advance(padded, current, previous, fields, coefs, plane, top):
    courant, eps_field, delta_field, shear, damp = fields
    a_xx, a_yy, a_zz, a_xy, a_xz, a_yz = coefs
    u_zz, u_xx, u_yy, u_xy, u_xz, u_yz = derivatives(padded)
    h_one = a_xx * u_xx + a_yy * u_yy + a_zz * u_zz + a_xy * u_xy + a_xz * u_xz + a_yz * u_yz
    h_two = u_xx + u_yy + u_zz - h_one
    wave_a = current[0]
    wave_b = current[1]
    old_a = previous[0]
    old_b = previous[1]
    new_a = (
        2.0 * wave_a
        - old_a
        + courant * ((1.0 + 2.0 * eps_field) * h_two[0] + h_one[1] + shear * (h_one[0] - h_one[1]))
        - damp * (wave_a - old_a)
    )
    new_b = (
        2.0 * wave_b
        - old_b
        + courant
        * ((1.0 + 2.0 * delta_field) * h_two[0] + h_one[1] + shear * (h_two[1] - h_two[0]))
        - damp * (wave_b - old_b)
    )
    new_a = new_a.at[top].add(plane)
    new_b = new_b.at[top].add(plane)
    return jnp.stack([new_a, new_b])


def step_amplitudes(samples, resample_filter, line_gain, lines):
    table = jnp.arange(line_gain.shape[0], dtype=jnp.int32)
    gains = jnp.sum(jnp.where(lines[:, None] == table[None, :], line_gain[None, :], 0.0), axis=1)
    return jnp.dot(samples, resample_filter.T, precision=lax.Precision.HIGHEST) * gains[:, None]


def local(
    wave_p,
    wave_p_old,
    wave_q,
    wave_q_old,
    courant_square,
    thomsen_epsilon,
    thomsen_delta,
    tilt_angle,
    azimuth,
    shear_ratio,
    damping,
    trace_samples,
    resample_filter,
    line_gain,
    receiver_inline,
    receiver_crossline,
    shot_line,
):
    depth, inline_cells, cross_cells = wave_p.shape
    cells = inline_cells * cross_cells
    steps = resample_filter.shape[0]
    xl_count = lax.axis_size("xl")
    gz_count = lax.axis_size("gz")
    columns = lax.axis_size("inl") * xl_count
    capacity = 2 * trace_samples.shape[0] // columns
    devices = columns * gz_count
    owner = receiver_inline // inline_cells * xl_count + receiver_crossline // cross_cells
    local_cell = receiver_inline % inline_cells * cross_cells + receiver_crossline % cross_cells
    payload = step_amplitudes(trace_samples, resample_filter, line_gain, shot_line)
    traces = owner.shape[0]
    highest = lax.Precision.HIGHEST
    in_column = (owner[:, None] == jnp.arange(columns, dtype=jnp.int32)[None, :]).astype(jnp.float32)
    order = jnp.arange(traces, dtype=jnp.int32)
    earlier = (order[:, None] > order[None, :]).astype(jnp.float32)
    rank = jnp.sum(jnp.dot(earlier, in_column, precision=highest) * in_column, axis=1)
    lane = jnp.arange(3 * capacity, dtype=jnp.int32)[None, :]
    value = jnp.where(
        lane < capacity,
        payload[:, 0:1],
        jnp.where(lane < 2 * capacity, payload[:, 1:2], local_cell.astype(jnp.float32)[:, None]),
    )
    spread = jnp.where(rank.astype(jnp.int32)[:, None] == lane % capacity, value, 0.0)
    to_device = (
        (owner * gz_count)[:, None] == jnp.arange(devices, dtype=jnp.int32)[None, :]
    ).astype(jnp.float32)
    send = lax.dot_general(to_device, spread, (((0,), (0,)), ((), ())), precision=highest)
    current = jnp.stack([wave_p, wave_q])
    faces = first_round(current, 4)
    send, faces = lax.optimization_barrier((send, faces))
    arrived = lax.all_to_all(send, ("inl", "xl", "gz"), split_axis=0, concat_axis=0, tiled=True)
    amp = arrived[:, : steps * capacity].reshape(devices, steps, capacity)
    cell = (arrived[:, steps * capacity :] + 0.5).astype(jnp.int32)
    row_hit = (
        cell[None, :, :] // cross_cells
        == jnp.arange(inline_cells, dtype=jnp.int32)[:, None, None]
    ).astype(jnp.float32)
    col_hit = (
        cell[None, :, :] % cross_cells == jnp.arange(cross_cells, dtype=jnp.int32)[:, None, None]
    ).astype(jnp.float32)
    weighted = (jnp.transpose(amp, (1, 0, 2))[:, None] * row_hit[None]).reshape(
        steps * inline_cells, devices, capacity
    )
    planes = lax.dot_general(
        weighted, col_hit, (((1, 2), (1, 2)), ((), ())), precision=highest
    ).reshape(steps, inline_cells, cross_cells)
    fields = (courant_square, thomsen_epsilon, thomsen_delta, shear_ratio, damping)
    current = jnp.stack([wave_p, wave_q])
    previous = jnp.stack([wave_p_old, wave_q_old])
    coefs = anisotropy(tilt_angle, azimuth)
    for step in range(steps):
        padded = second_round(current, 4, faces) if step == 0 else with_halo(current, 4)
        newer = advance(padded, current, previous, fields, coefs, planes[step], 0)
        previous = current
        current = newer
    return (current[0], current[1], previous[0], previous[1])


def solution(mesh):
    return jax.shard_map(
        local,
        mesh=mesh,
        in_specs=(
            P("gz", "inl", "xl"),
            P("gz", "inl", "xl"),
            P("gz", "inl", "xl"),
            P("gz", "inl", "xl"),
            P("gz", "inl", "xl"),
            P("gz", "inl", "xl"),
            P("gz", "inl", "xl"),
            P("gz", "inl", "xl"),
            P("gz", "inl", "xl"),
            P("gz", "inl", "xl"),
            P("gz", "inl", "xl"),
            P(("inl", "xl", "gz"), None),
            P(),
            P(),
            P(("inl", "xl", "gz")),
            P(("inl", "xl", "gz")),
            P(("inl", "xl", "gz")),
        ),
        out_specs=(
            P("gz", "inl", "xl"),
            P("gz", "inl", "xl"),
            P("gz", "inl", "xl"),
            P("gz", "inl", "xl"),
        ),
        check_vma=False,
    )
```

```python
import jax
import jax.numpy as jnp
from jax import lax
from jax.sharding import PartitionSpec as P

second_coef = (-205.0 / 72.0, 8.0 / 5.0, -1.0 / 5.0, 8.0 / 315.0, -1.0 / 560.0)
first_coef = (0.0, 4.0 / 5.0, -1.0 / 5.0, 4.0 / 105.0, -1.0 / 280.0)


def shift_pair(top, bottom, axis):
    count = lax.axis_size(axis)
    if count == 2:
        first = lax.axis_index(axis) == 0
        got = lax.ppermute(jnp.where(first, top, bottom), axis, [(0, 1), (1, 0)])
        empty = jnp.zeros_like(got)
        return jnp.where(first, empty, got), jnp.where(first, got, empty)
    if count % 2 == 0:
        even = lax.axis_index(axis) % 2 == 0
        inner = [(i, i ^ 1) for i in range(count)]
        outer = [(i, i + 1 if i % 2 else i - 1) for i in range(1, count - 1)]
        got_inner = lax.ppermute(jnp.where(even, top, bottom), axis, inner)
        got_outer = lax.ppermute(jnp.where(even, bottom, top), axis, outer)
        return jnp.where(even, got_outer, got_inner), jnp.where(even, got_inner, got_outer)
    forward = [(i, i + 1) for i in range(count - 1)]
    backward = [(target, source) for source, target in forward]
    return lax.ppermute(top, axis, forward), lax.ppermute(bottom, axis, backward)


def first_round(block, width):
    cut = lambda a, dim, lo, hi: lax.slice_in_dim(a, lo, hi, axis=dim)
    across, along = block.shape[2:]
    low_x, high_x = shift_pair(cut(block, 2, across - width, None), cut(block, 2, 0, width), "inl")
    low_y, high_y = shift_pair(cut(block, 3, along - width, None), cut(block, 3, 0, width), "xl")
    return low_x, high_x, low_y, high_y


def second_round(block, width, faces):
    cut = lambda a, dim, lo, hi: lax.slice_in_dim(a, lo, hi, axis=dim)
    depth, along = block.shape[1], block.shape[3]
    low_x, high_x, low_y, high_y = faces
    strips = jnp.concatenate([low_x, high_x], axis=2)
    low_c, high_c = shift_pair(cut(strips, 3, along - width, None), cut(strips, 3, 0, width), "xl")
    wide_x = jnp.concatenate([low_x, block, high_x], axis=2)
    pad_x = ((0, 0), (0, 0), (width, width), (0, 0))
    bare = jnp.concatenate([jnp.pad(low_y, pad_x), wide_x, jnp.pad(high_y, pad_x)], axis=3)
    low_z, high_z = shift_pair(cut(bare, 1, depth - width, None), cut(bare, 1, 0, width), "gz")
    side_low = jnp.concatenate([low_c[:, :, :width], low_y, low_c[:, :, width:]], axis=2)
    side_high = jnp.concatenate([high_c[:, :, :width], high_y, high_c[:, :, width:]], axis=2)
    full = jnp.concatenate([side_low, wide_x, side_high], axis=3)
    return jnp.concatenate([low_z, full, high_z], axis=1)


def with_halo(block, width):
    return second_round(block, width, first_round(block, width))


def derivatives(padded):
    depth = padded.shape[-3] - 8
    across = padded.shape[-2] - 8
    along = padded.shape[-1] - 8

    def piece(dz, dx, dy):
        return padded[
            ..., 4 + dz : 4 + dz + depth, 4 + dx : 4 + dx + across, 4 + dy : 4 + dy + along
        ]

    center = piece(0, 0, 0)
    u_zz = second_coef[0] * center
    u_xx = second_coef[0] * center
    u_yy = second_coef[0] * center
    for k in range(1, 5):
        u_zz = u_zz + second_coef[k] * (piece(k, 0, 0) + piece(-k, 0, 0))
        u_xx = u_xx + second_coef[k] * (piece(0, k, 0) + piece(0, -k, 0))
        u_yy = u_yy + second_coef[k] * (piece(0, 0, k) + piece(0, 0, -k))
    grad_x = first_coef[1] * (padded[..., :, 5 : 5 + across, :] - padded[..., :, 3 : 3 + across, :])
    grad_y = first_coef[1] * (
        padded[..., :, 4 : 4 + across, 5 : 5 + along]
        - padded[..., :, 4 : 4 + across, 3 : 3 + along]
    )
    for k in range(2, 5):
        grad_x = grad_x + first_coef[k] * (
            padded[..., :, 4 + k : 4 + k + across, :] - padded[..., :, 4 - k : 4 - k + across, :]
        )
        grad_y = grad_y + first_coef[k] * (
            padded[..., :, 4 : 4 + across, 4 + k : 4 + k + along]
            - padded[..., :, 4 : 4 + across, 4 - k : 4 - k + along]
        )
    u_xy = first_coef[1] * (
        grad_x[..., 4 : 4 + depth, :, 5 : 5 + along] - grad_x[..., 4 : 4 + depth, :, 3 : 3 + along]
    )
    u_xz = first_coef[1] * (
        grad_x[..., 5 : 5 + depth, :, 4 : 4 + along] - grad_x[..., 3 : 3 + depth, :, 4 : 4 + along]
    )
    u_yz = first_coef[1] * (grad_y[..., 5 : 5 + depth, :, :] - grad_y[..., 3 : 3 + depth, :, :])
    for k in range(2, 5):
        u_xy = u_xy + first_coef[k] * (
            grad_x[..., 4 : 4 + depth, :, 4 + k : 4 + k + along]
            - grad_x[..., 4 : 4 + depth, :, 4 - k : 4 - k + along]
        )
        u_xz = u_xz + first_coef[k] * (
            grad_x[..., 4 + k : 4 + k + depth, :, 4 : 4 + along]
            - grad_x[..., 4 - k : 4 - k + depth, :, 4 : 4 + along]
        )
        u_yz = u_yz + first_coef[k] * (
            grad_y[..., 4 + k : 4 + k + depth, :, :] - grad_y[..., 4 - k : 4 - k + depth, :, :]
        )
    return (u_zz, u_xx, u_yy, u_xy, u_xz, u_yz)


def anisotropy(tilt_angle, azimuth):
    sin_t = jnp.sin(tilt_angle)
    cos_t = jnp.cos(tilt_angle)
    sin_f = jnp.sin(azimuth)
    cos_f = jnp.cos(azimuth)
    a_xx = sin_t * sin_t * cos_f * cos_f
    a_yy = sin_t * sin_t * sin_f * sin_f
    a_zz = cos_t * cos_t
    a_xy = 2.0 * sin_t * sin_t * sin_f * cos_f
    a_xz = 2.0 * sin_t * cos_t * cos_f
    a_yz = 2.0 * sin_t * cos_t * sin_f
    return (a_xx, a_yy, a_zz, a_xy, a_xz, a_yz)


def advance(padded, current, previous, fields, coefs, plane, top):
    courant, eps_field, delta_field, shear, damp = fields
    a_xx, a_yy, a_zz, a_xy, a_xz, a_yz = coefs
    u_zz, u_xx, u_yy, u_xy, u_xz, u_yz = derivatives(padded)
    h_one = a_xx * u_xx + a_yy * u_yy + a_zz * u_zz + a_xy * u_xy + a_xz * u_xz + a_yz * u_yz
    h_two = u_xx + u_yy + u_zz - h_one
    wave_a = current[0]
    wave_b = current[1]
    old_a = previous[0]
    old_b = previous[1]
    new_a = (
        2.0 * wave_a
        - old_a
        + courant * ((1.0 + 2.0 * eps_field) * h_two[0] + h_one[1] + shear * (h_one[0] - h_one[1]))
        - damp * (wave_a - old_a)
    )
    new_b = (
        2.0 * wave_b
        - old_b
        + courant
        * ((1.0 + 2.0 * delta_field) * h_two[0] + h_one[1] + shear * (h_two[1] - h_two[0]))
        - damp * (wave_b - old_b)
    )
    new_a = new_a.at[top].add(plane)
    new_b = new_b.at[top].add(plane)
    return jnp.stack([new_a, new_b])


def step_amplitudes(samples, resample_filter, line_gain, lines):
    table = jnp.arange(line_gain.shape[0], dtype=jnp.int32)
    gains = jnp.sum(jnp.where(lines[:, None] == table[None, :], line_gain[None, :], 0.0), axis=1)
    return jnp.dot(samples, resample_filter.T, precision=lax.Precision.HIGHEST) * gains[:, None]


def local(
    wave_p,
    wave_p_old,
    wave_q,
    wave_q_old,
    courant_square,
    thomsen_epsilon,
    thomsen_delta,
    tilt_angle,
    azimuth,
    shear_ratio,
    damping,
    trace_samples,
    resample_filter,
    line_gain,
    receiver_inline,
    receiver_crossline,
    shot_line,
):
    depth, inline_cells, cross_cells = wave_p.shape
    cells = inline_cells * cross_cells
    steps = resample_filter.shape[0]
    xl_count = lax.axis_size("xl")
    gz_count = lax.axis_size("gz")
    columns = lax.axis_size("inl") * xl_count
    capacity = 2 * trace_samples.shape[0] // columns
    devices = columns * gz_count
    owner = receiver_inline // inline_cells * xl_count + receiver_crossline // cross_cells
    local_cell = receiver_inline % inline_cells * cross_cells + receiver_crossline % cross_cells
    payload = step_amplitudes(trace_samples, resample_filter, line_gain, shot_line)
    traces = owner.shape[0]
    highest = lax.Precision.HIGHEST
    in_column = (owner[:, None] == jnp.arange(columns, dtype=jnp.int32)[None, :]).astype(jnp.float32)
    order = jnp.arange(traces, dtype=jnp.int32)
    earlier = (order[:, None] > order[None, :]).astype(jnp.float32)
    rank = jnp.sum(jnp.dot(earlier, in_column, precision=highest) * in_column, axis=1)
    lane = jnp.arange(3 * capacity, dtype=jnp.int32)[None, :]
    value = jnp.where(
        lane < capacity,
        payload[:, 0:1],
        jnp.where(lane < 2 * capacity, payload[:, 1:2], local_cell.astype(jnp.float32)[:, None]),
    )
    spread = jnp.where(rank.astype(jnp.int32)[:, None] == lane % capacity, value, 0.0)
    to_device = (
        (owner * gz_count)[:, None] == jnp.arange(devices, dtype=jnp.int32)[None, :]
    ).astype(jnp.float32)
    send = lax.dot_general(to_device, spread, (((0,), (0,)), ((), ())), precision=highest)
    current = jnp.stack([wave_p, wave_q])
    faces = first_round(current, 4)
    send, faces = lax.optimization_barrier((send, faces))
    arrived = lax.all_to_all(send, ("inl", "xl", "gz"), split_axis=0, concat_axis=0, tiled=True)
    amp = arrived[:, : steps * capacity].reshape(devices, steps, capacity)
    cell = (arrived[:, steps * capacity :] + 0.5).astype(jnp.int32)
    row_hit = (
        cell[None, :, :] // cross_cells
        == jnp.arange(inline_cells, dtype=jnp.int32)[:, None, None]
    ).astype(jnp.float32)
    col_hit = (
        cell[None, :, :] % cross_cells == jnp.arange(cross_cells, dtype=jnp.int32)[:, None, None]
    ).astype(jnp.float32)
    weighted = (jnp.transpose(amp, (1, 0, 2))[:, None] * row_hit[None]).reshape(
        steps * inline_cells, devices, capacity
    )
    planes = lax.dot_general(
        weighted, col_hit, (((1, 2), (1, 2)), ((), ())), precision=highest
    ).reshape(steps, inline_cells, cross_cells)
    fields = (courant_square, thomsen_epsilon, thomsen_delta, shear_ratio, damping)
    current = jnp.stack([wave_p, wave_q])
    previous = jnp.stack([wave_p_old, wave_q_old])
    coefs = anisotropy(tilt_angle, azimuth)
    for step in range(steps):
        padded = second_round(current, 4, faces) if step == 0 else with_halo(current, 4)
        newer = advance(padded, current, previous, fields, coefs, planes[step], 0)
        previous = current
        current = newer
    return (current[0], current[1], previous[0], previous[1])


def solution(mesh):
    return jax.shard_map(
        local,
        mesh=mesh,
        in_specs=(
            P("gz", "inl", "xl"),
            P("gz", "inl", "xl"),
            P("gz", "inl", "xl"),
            P("gz", "inl", "xl"),
            P("gz", "inl", "xl"),
            P("gz", "inl", "xl"),
            P("gz", "inl", "xl"),
            P("gz", "inl", "xl"),
            P("gz", "inl", "xl"),
            P("gz", "inl", "xl"),
            P("gz", "inl", "xl"),
            P(("inl", "xl", "gz"), None),
            P(),
            P(),
            P(("inl", "xl", "gz")),
            P(("inl", "xl", "gz")),
            P(("inl", "xl", "gz")),
        ),
        out_specs=(
            P("gz", "inl", "xl"),
            P("gz", "inl", "xl"),
            P("gz", "inl", "xl"),
            P("gz", "inl", "xl"),
        ),
        check_vma=False,
    )
```

```python
import jax
import jax.numpy as jnp
from jax import lax
from jax.sharding import PartitionSpec as P

second_coef = (-205.0 / 72.0, 8.0 / 5.0, -1.0 / 5.0, 8.0 / 315.0, -1.0 / 560.0)
first_coef = (0.0, 4.0 / 5.0, -1.0 / 5.0, 4.0 / 105.0, -1.0 / 280.0)


def shift_pair(top, bottom, axis):
    count = lax.axis_size(axis)
    if count == 2:
        first = lax.axis_index(axis) == 0
        got = lax.ppermute(jnp.where(first, top, bottom), axis, [(0, 1), (1, 0)])
        empty = jnp.zeros_like(got)
        return jnp.where(first, empty, got), jnp.where(first, got, empty)
    if count % 2 == 0:
        even = lax.axis_index(axis) % 2 == 0
        inner = [(i, i ^ 1) for i in range(count)]
        outer = [(i, i + 1 if i % 2 else i - 1) for i in range(1, count - 1)]
        got_inner = lax.ppermute(jnp.where(even, top, bottom), axis, inner)
        got_outer = lax.ppermute(jnp.where(even, bottom, top), axis, outer)
        return jnp.where(even, got_outer, got_inner), jnp.where(even, got_inner, got_outer)
    forward = [(i, i + 1) for i in range(count - 1)]
    backward = [(target, source) for source, target in forward]
    return lax.ppermute(top, axis, forward), lax.ppermute(bottom, axis, backward)


def first_round(block, width):
    cut = lambda a, dim, lo, hi: lax.slice_in_dim(a, lo, hi, axis=dim)
    across, along = block.shape[2:]
    low_x, high_x = shift_pair(cut(block, 2, across - width, None), cut(block, 2, 0, width), "inl")
    low_y, high_y = shift_pair(cut(block, 3, along - width, None), cut(block, 3, 0, width), "xl")
    return low_x, high_x, low_y, high_y


def second_round(block, width, faces):
    cut = lambda a, dim, lo, hi: lax.slice_in_dim(a, lo, hi, axis=dim)
    depth, along = block.shape[1], block.shape[3]
    low_x, high_x, low_y, high_y = faces
    strips = jnp.concatenate([low_x, high_x], axis=2)
    low_c, high_c = shift_pair(cut(strips, 3, along - width, None), cut(strips, 3, 0, width), "xl")
    wide_x = jnp.concatenate([low_x, block, high_x], axis=2)
    pad_x = ((0, 0), (0, 0), (width, width), (0, 0))
    bare = jnp.concatenate([jnp.pad(low_y, pad_x), wide_x, jnp.pad(high_y, pad_x)], axis=3)
    low_z, high_z = shift_pair(cut(bare, 1, depth - width, None), cut(bare, 1, 0, width), "gz")
    side_low = jnp.concatenate([low_c[:, :, :width], low_y, low_c[:, :, width:]], axis=2)
    side_high = jnp.concatenate([high_c[:, :, :width], high_y, high_c[:, :, width:]], axis=2)
    full = jnp.concatenate([side_low, wide_x, side_high], axis=3)
    return jnp.concatenate([low_z, full, high_z], axis=1)


def with_halo(block, width):
    return second_round(block, width, first_round(block, width))


def derivatives(padded):
    depth = padded.shape[-3] - 8
    across = padded.shape[-2] - 8
    along = padded.shape[-1] - 8

    def piece(dz, dx, dy):
        return padded[
            ..., 4 + dz : 4 + dz + depth, 4 + dx : 4 + dx + across, 4 + dy : 4 + dy + along
        ]

    center = piece(0, 0, 0)
    u_zz = second_coef[0] * center
    u_xx = second_coef[0] * center
    u_yy = second_coef[0] * center
    for k in range(1, 5):
        u_zz = u_zz + second_coef[k] * (piece(k, 0, 0) + piece(-k, 0, 0))
        u_xx = u_xx + second_coef[k] * (piece(0, k, 0) + piece(0, -k, 0))
        u_yy = u_yy + second_coef[k] * (piece(0, 0, k) + piece(0, 0, -k))
    grad_x = first_coef[1] * (padded[..., :, 5 : 5 + across, :] - padded[..., :, 3 : 3 + across, :])
    grad_y = first_coef[1] * (
        padded[..., :, 4 : 4 + across, 5 : 5 + along]
        - padded[..., :, 4 : 4 + across, 3 : 3 + along]
    )
    for k in range(2, 5):
        grad_x = grad_x + first_coef[k] * (
            padded[..., :, 4 + k : 4 + k + across, :] - padded[..., :, 4 - k : 4 - k + across, :]
        )
        grad_y = grad_y + first_coef[k] * (
            padded[..., :, 4 : 4 + across, 4 + k : 4 + k + along]
            - padded[..., :, 4 : 4 + across, 4 - k : 4 - k + along]
        )
    u_xy = first_coef[1] * (
        grad_x[..., 4 : 4 + depth, :, 5 : 5 + along] - grad_x[..., 4 : 4 + depth, :, 3 : 3 + along]
    )
    u_xz = first_coef[1] * (
        grad_x[..., 5 : 5 + depth, :, 4 : 4 + along] - grad_x[..., 3 : 3 + depth, :, 4 : 4 + along]
    )
    u_yz = first_coef[1] * (grad_y[..., 5 : 5 + depth, :, :] - grad_y[..., 3 : 3 + depth, :, :])
    for k in range(2, 5):
        u_xy = u_xy + first_coef[k] * (
            grad_x[..., 4 : 4 + depth, :, 4 + k : 4 + k + along]
            - grad_x[..., 4 : 4 + depth, :, 4 - k : 4 - k + along]
        )
        u_xz = u_xz + first_coef[k] * (
            grad_x[..., 4 + k : 4 + k + depth, :, 4 : 4 + along]
            - grad_x[..., 4 - k : 4 - k + depth, :, 4 : 4 + along]
        )
        u_yz = u_yz + first_coef[k] * (
            grad_y[..., 4 + k : 4 + k + depth, :, :] - grad_y[..., 4 - k : 4 - k + depth, :, :]
        )
    return (u_zz, u_xx, u_yy, u_xy, u_xz, u_yz)


def anisotropy(tilt_angle, azimuth):
    sin_t = jnp.sin(tilt_angle)
    cos_t = jnp.cos(tilt_angle)
    sin_f = jnp.sin(azimuth)
    cos_f = jnp.cos(azimuth)
    a_xx = sin_t * sin_t * cos_f * cos_f
    a_yy = sin_t * sin_t * sin_f * sin_f
    a_zz = cos_t * cos_t
    a_xy = 2.0 * sin_t * sin_t * sin_f * cos_f
    a_xz = 2.0 * sin_t * cos_t * cos_f
    a_yz = 2.0 * sin_t * cos_t * sin_f
    return (a_xx, a_yy, a_zz, a_xy, a_xz, a_yz)


def advance(padded, current, previous, fields, coefs, plane, top):
    courant, eps_field, delta_field, shear, damp = fields
    a_xx, a_yy, a_zz, a_xy, a_xz, a_yz = coefs
    u_zz, u_xx, u_yy, u_xy, u_xz, u_yz = derivatives(padded)
    h_one = a_xx * u_xx + a_yy * u_yy + a_zz * u_zz + a_xy * u_xy + a_xz * u_xz + a_yz * u_yz
    h_two = u_xx + u_yy + u_zz - h_one
    wave_a = current[0]
    wave_b = current[1]
    old_a = previous[0]
    old_b = previous[1]
    new_a = (
        2.0 * wave_a
        - old_a
        + courant * ((1.0 + 2.0 * eps_field) * h_two[0] + h_one[1] + shear * (h_one[0] - h_one[1]))
        - damp * (wave_a - old_a)
    )
    new_b = (
        2.0 * wave_b
        - old_b
        + courant
        * ((1.0 + 2.0 * delta_field) * h_two[0] + h_one[1] + shear * (h_two[1] - h_two[0]))
        - damp * (wave_b - old_b)
    )
    new_a = new_a.at[top].add(plane)
    new_b = new_b.at[top].add(plane)
    return jnp.stack([new_a, new_b])


def step_amplitudes(samples, resample_filter, line_gain, lines):
    table = jnp.arange(line_gain.shape[0], dtype=jnp.int32)
    gains = jnp.sum(jnp.where(lines[:, None] == table[None, :], line_gain[None, :], 0.0), axis=1)
    return jnp.dot(samples, resample_filter.T, precision=lax.Precision.HIGHEST) * gains[:, None]


def local(
    wave_p,
    wave_p_old,
    wave_q,
    wave_q_old,
    courant_square,
    thomsen_epsilon,
    thomsen_delta,
    tilt_angle,
    azimuth,
    shear_ratio,
    damping,
    trace_samples,
    resample_filter,
    line_gain,
    receiver_inline,
    receiver_crossline,
    shot_line,
):
    depth, inline_cells, cross_cells = wave_p.shape
    cells = inline_cells * cross_cells
    steps = resample_filter.shape[0]
    xl_count = lax.axis_size("xl")
    gz_count = lax.axis_size("gz")
    columns = lax.axis_size("inl") * xl_count
    capacity = 2 * trace_samples.shape[0] // columns
    devices = columns * gz_count
    owner = receiver_inline // inline_cells * xl_count + receiver_crossline // cross_cells
    local_cell = receiver_inline % inline_cells * cross_cells + receiver_crossline % cross_cells
    payload = step_amplitudes(trace_samples, resample_filter, line_gain, shot_line)
    traces = owner.shape[0]
    highest = lax.Precision.HIGHEST
    in_column = (owner[:, None] == jnp.arange(columns, dtype=jnp.int32)[None, :]).astype(jnp.float32)
    order = jnp.arange(traces, dtype=jnp.int32)
    earlier = (order[:, None] > order[None, :]).astype(jnp.float32)
    rank = jnp.sum(jnp.dot(earlier, in_column, precision=highest) * in_column, axis=1)
    lanes = 128 if 3 * capacity > 128 else 3 * capacity
    rows = -(-3 * capacity // lanes)
    lane = jnp.arange(rows * lanes, dtype=jnp.int32)[None, :]
    value = jnp.where(
        lane < capacity,
        payload[:, 0:1],
        jnp.where(lane < 2 * capacity, payload[:, 1:2], local_cell.astype(jnp.float32)[:, None]),
    )
    hit = (rank.astype(jnp.int32)[:, None] == lane % capacity) & (lane < 3 * capacity)
    spread = jnp.where(hit, value, 0.0)
    to_device = (
        (owner * gz_count)[:, None] == jnp.arange(devices, dtype=jnp.int32)[None, :]
    ).astype(jnp.float32)
    send = lax.dot_general(to_device, spread, (((0,), (0,)), ((), ())), precision=highest)
    current = jnp.stack([wave_p, wave_q])
    faces = first_round(current, 4)
    send, faces = lax.optimization_barrier((send, faces))
    send = send.reshape(devices, rows, lanes)
    arrived = lax.all_to_all(send, ("inl", "xl", "gz"), split_axis=0, concat_axis=0, tiled=True)
    arrived = arrived.reshape(devices, rows * lanes)
    amp = arrived[:, : steps * capacity].reshape(devices, steps, capacity)
    cell = (arrived[:, steps * capacity : 3 * capacity] + 0.5).astype(jnp.int32)
    row_hit = (
        cell[None, :, :] // cross_cells
        == jnp.arange(inline_cells, dtype=jnp.int32)[:, None, None]
    ).astype(jnp.float32)
    col_hit = (
        cell[None, :, :] % cross_cells == jnp.arange(cross_cells, dtype=jnp.int32)[:, None, None]
    ).astype(jnp.float32)
    weighted = (jnp.transpose(amp, (1, 0, 2))[:, None] * row_hit[None]).reshape(
        steps * inline_cells, devices, capacity
    )
    planes = lax.dot_general(
        weighted, col_hit, (((1, 2), (1, 2)), ((), ())), precision=highest
    ).reshape(steps, inline_cells, cross_cells)
    fields = (courant_square, thomsen_epsilon, thomsen_delta, shear_ratio, damping)
    current = jnp.stack([wave_p, wave_q])
    previous = jnp.stack([wave_p_old, wave_q_old])
    coefs = anisotropy(tilt_angle, azimuth)
    for step in range(steps):
        padded = second_round(current, 4, faces) if step == 0 else with_halo(current, 4)
        newer = advance(padded, current, previous, fields, coefs, planes[step], 0)
        previous = current
        current = newer
    return (current[0], current[1], previous[0], previous[1])


def solution(mesh):
    return jax.shard_map(
        local,
        mesh=mesh,
        in_specs=(
            P("gz", "inl", "xl"),
            P("gz", "inl", "xl"),
            P("gz", "inl", "xl"),
            P("gz", "inl", "xl"),
            P("gz", "inl", "xl"),
            P("gz", "inl", "xl"),
            P("gz", "inl", "xl"),
            P("gz", "inl", "xl"),
            P("gz", "inl", "xl"),
            P("gz", "inl", "xl"),
            P("gz", "inl", "xl"),
            P(("inl", "xl", "gz"), None),
            P(),
            P(),
            P(("inl", "xl", "gz")),
            P(("inl", "xl", "gz")),
            P(("inl", "xl", "gz")),
        ),
        out_specs=(
            P("gz", "inl", "xl"),
            P("gz", "inl", "xl"),
            P("gz", "inl", "xl"),
            P("gz", "inl", "xl"),
        ),
        check_vma=False,
    )
```

```python
import jax
import jax.numpy as jnp
from jax import lax
from jax.sharding import PartitionSpec as P

second_coef = (-205.0 / 72.0, 8.0 / 5.0, -1.0 / 5.0, 8.0 / 315.0, -1.0 / 560.0)
first_coef = (0.0, 4.0 / 5.0, -1.0 / 5.0, 4.0 / 105.0, -1.0 / 280.0)


def shift_pair(block, dim, width, axis):
    count = lax.axis_size(axis)
    size = block.shape[dim]
    index = lax.axis_index(axis)
    if count % 2 == 0:
        even = index % 2 == 0
        inner = [(i, i ^ 1) for i in range(count)]
        outer = [(i, i + 1 if i % 2 else i - 1) for i in range(1, count - 1)]
        got_inner = lax.ppermute(
            lax.dynamic_slice_in_dim(block, jnp.where(even, size - width, 0), width, axis=dim),
            axis,
            inner,
        )
        if count == 2:
            empty = jnp.zeros_like(got_inner)
            return jnp.where(even, empty, got_inner), jnp.where(even, got_inner, empty)
        got_outer = lax.ppermute(
            lax.dynamic_slice_in_dim(block, jnp.where(even, 0, size - width), width, axis=dim),
            axis,
            outer,
        )
        return jnp.where(even, got_outer, got_inner), jnp.where(even, got_inner, got_outer)
    forward = [(i, i + 1) for i in range(count - 1)]
    backward = [(target, source) for source, target in forward]
    top = lax.slice_in_dim(block, size - width, None, axis=dim)
    bottom = lax.slice_in_dim(block, 0, width, axis=dim)
    return lax.ppermute(top, axis, forward), lax.ppermute(bottom, axis, backward)


def first_round(block, width):
    low_x, high_x = shift_pair(block, 2, width, "inl")
    low_y, high_y = shift_pair(block, 3, width, "xl")
    return low_x, high_x, low_y, high_y


def second_round(block, width, faces):
    low_x, high_x, low_y, high_y = faces
    strips = jnp.concatenate([low_x, high_x], axis=2)
    low_c, high_c = shift_pair(strips, 3, width, "xl")
    wide_x = jnp.concatenate([low_x, block, high_x], axis=2)
    pad_x = ((0, 0), (0, 0), (width, width), (0, 0))
    bare = jnp.concatenate([jnp.pad(low_y, pad_x), wide_x, jnp.pad(high_y, pad_x)], axis=3)
    low_z, high_z = shift_pair(bare, 1, width, "gz")
    side_low = jnp.concatenate([low_c[:, :, :width], low_y, low_c[:, :, width:]], axis=2)
    side_high = jnp.concatenate([high_c[:, :, :width], high_y, high_c[:, :, width:]], axis=2)
    full = jnp.concatenate([side_low, wide_x, side_high], axis=3)
    return jnp.concatenate([low_z, full, high_z], axis=1)


def with_halo(block, width):
    return second_round(block, width, first_round(block, width))


def derivatives(padded):
    depth = padded.shape[-3] - 8
    across = padded.shape[-2] - 8
    along = padded.shape[-1] - 8

    def piece(dz, dx, dy):
        return padded[
            ..., 4 + dz : 4 + dz + depth, 4 + dx : 4 + dx + across, 4 + dy : 4 + dy + along
        ]

    center = piece(0, 0, 0)
    u_zz = second_coef[0] * center
    u_xx = second_coef[0] * center
    u_yy = second_coef[0] * center
    for k in range(1, 5):
        u_zz = u_zz + second_coef[k] * (piece(k, 0, 0) + piece(-k, 0, 0))
        u_xx = u_xx + second_coef[k] * (piece(0, k, 0) + piece(0, -k, 0))
        u_yy = u_yy + second_coef[k] * (piece(0, 0, k) + piece(0, 0, -k))
    grad_x = first_coef[1] * (padded[..., :, 5 : 5 + across, :] - padded[..., :, 3 : 3 + across, :])
    grad_y = first_coef[1] * (
        padded[..., :, 4 : 4 + across, 5 : 5 + along]
        - padded[..., :, 4 : 4 + across, 3 : 3 + along]
    )
    for k in range(2, 5):
        grad_x = grad_x + first_coef[k] * (
            padded[..., :, 4 + k : 4 + k + across, :] - padded[..., :, 4 - k : 4 - k + across, :]
        )
        grad_y = grad_y + first_coef[k] * (
            padded[..., :, 4 : 4 + across, 4 + k : 4 + k + along]
            - padded[..., :, 4 : 4 + across, 4 - k : 4 - k + along]
        )
    u_xy = first_coef[1] * (
        grad_x[..., 4 : 4 + depth, :, 5 : 5 + along] - grad_x[..., 4 : 4 + depth, :, 3 : 3 + along]
    )
    u_xz = first_coef[1] * (
        grad_x[..., 5 : 5 + depth, :, 4 : 4 + along] - grad_x[..., 3 : 3 + depth, :, 4 : 4 + along]
    )
    u_yz = first_coef[1] * (grad_y[..., 5 : 5 + depth, :, :] - grad_y[..., 3 : 3 + depth, :, :])
    for k in range(2, 5):
        u_xy = u_xy + first_coef[k] * (
            grad_x[..., 4 : 4 + depth, :, 4 + k : 4 + k + along]
            - grad_x[..., 4 : 4 + depth, :, 4 - k : 4 - k + along]
        )
        u_xz = u_xz + first_coef[k] * (
            grad_x[..., 4 + k : 4 + k + depth, :, 4 : 4 + along]
            - grad_x[..., 4 - k : 4 - k + depth, :, 4 : 4 + along]
        )
        u_yz = u_yz + first_coef[k] * (
            grad_y[..., 4 + k : 4 + k + depth, :, :] - grad_y[..., 4 - k : 4 - k + depth, :, :]
        )
    return (u_zz, u_xx, u_yy, u_xy, u_xz, u_yz)


def anisotropy(tilt_angle, azimuth):
    sin_t = jnp.sin(tilt_angle)
    cos_t = jnp.cos(tilt_angle)
    sin_f = jnp.sin(azimuth)
    cos_f = jnp.cos(azimuth)
    a_xx = sin_t * sin_t * cos_f * cos_f
    a_yy = sin_t * sin_t * sin_f * sin_f
    a_zz = cos_t * cos_t
    a_xy = 2.0 * sin_t * sin_t * sin_f * cos_f
    a_xz = 2.0 * sin_t * cos_t * cos_f
    a_yz = 2.0 * sin_t * cos_t * sin_f
    return (a_xx, a_yy, a_zz, a_xy, a_xz, a_yz)


def advance(padded, current, previous, fields, coefs, plane, top):
    courant, eps_field, delta_field, shear, damp = fields
    a_xx, a_yy, a_zz, a_xy, a_xz, a_yz = coefs
    u_zz, u_xx, u_yy, u_xy, u_xz, u_yz = derivatives(padded)
    h_one = a_xx * u_xx + a_yy * u_yy + a_zz * u_zz + a_xy * u_xy + a_xz * u_xz + a_yz * u_yz
    h_two = u_xx + u_yy + u_zz - h_one
    wave_a = current[0]
    wave_b = current[1]
    old_a = previous[0]
    old_b = previous[1]
    new_a = (
        2.0 * wave_a
        - old_a
        + courant * ((1.0 + 2.0 * eps_field) * h_two[0] + h_one[1] + shear * (h_one[0] - h_one[1]))
        - damp * (wave_a - old_a)
    )
    new_b = (
        2.0 * wave_b
        - old_b
        + courant
        * ((1.0 + 2.0 * delta_field) * h_two[0] + h_one[1] + shear * (h_two[1] - h_two[0]))
        - damp * (wave_b - old_b)
    )
    new_a = new_a.at[top].add(plane)
    new_b = new_b.at[top].add(plane)
    return jnp.stack([new_a, new_b])


def step_amplitudes(samples, resample_filter, line_gain, lines):
    table = jnp.arange(line_gain.shape[0], dtype=jnp.int32)
    gains = jnp.sum(jnp.where(lines[:, None] == table[None, :], line_gain[None, :], 0.0), axis=1)
    return jnp.dot(samples, resample_filter.T, precision=lax.Precision.HIGHEST) * gains[:, None]


def local(
    wave_p,
    wave_p_old,
    wave_q,
    wave_q_old,
    courant_square,
    thomsen_epsilon,
    thomsen_delta,
    tilt_angle,
    azimuth,
    shear_ratio,
    damping,
    trace_samples,
    resample_filter,
    line_gain,
    receiver_inline,
    receiver_crossline,
    shot_line,
):
    depth, inline_cells, cross_cells = wave_p.shape
    cells = inline_cells * cross_cells
    steps = resample_filter.shape[0]
    xl_count = lax.axis_size("xl")
    gz_count = lax.axis_size("gz")
    columns = lax.axis_size("inl") * xl_count
    capacity = 2 * trace_samples.shape[0] // columns
    devices = columns * gz_count
    owner = receiver_inline // inline_cells * xl_count + receiver_crossline // cross_cells
    local_cell = receiver_inline % inline_cells * cross_cells + receiver_crossline % cross_cells
    payload = step_amplitudes(trace_samples, resample_filter, line_gain, shot_line)
    traces = owner.shape[0]
    highest = lax.Precision.HIGHEST
    in_column = (owner[:, None] == jnp.arange(columns, dtype=jnp.int32)[None, :]).astype(jnp.float32)
    order = jnp.arange(traces, dtype=jnp.int32)
    earlier = (order[:, None] > order[None, :]).astype(jnp.float32)
    rank = jnp.sum(jnp.dot(earlier, in_column, precision=highest) * in_column, axis=1)
    lane = jnp.arange(3 * capacity, dtype=jnp.int32)[None, :]
    value = jnp.where(
        lane < capacity,
        payload[:, 0:1],
        jnp.where(lane < 2 * capacity, payload[:, 1:2], local_cell.astype(jnp.float32)[:, None]),
    )
    spread = jnp.where(rank.astype(jnp.int32)[:, None] == lane % capacity, value, 0.0)
    to_device = (
        (owner * gz_count)[:, None] == jnp.arange(devices, dtype=jnp.int32)[None, :]
    ).astype(jnp.float32)
    send = lax.dot_general(to_device, spread, (((0,), (0,)), ((), ())), precision=highest)
    current = jnp.stack([wave_p, wave_q])
    faces = first_round(current, 4)
    send, faces = lax.optimization_barrier((send, faces))
    arrived = lax.all_to_all(send, ("inl", "xl", "gz"), split_axis=0, concat_axis=0, tiled=True)
    amp = arrived[:, : steps * capacity].reshape(devices, steps, capacity)
    cell = (arrived[:, steps * capacity :] + 0.5).astype(jnp.int32)
    row_hit = (
        cell[None, :, :] // cross_cells
        == jnp.arange(inline_cells, dtype=jnp.int32)[:, None, None]
    ).astype(jnp.float32)
    col_hit = (
        cell[None, :, :] % cross_cells == jnp.arange(cross_cells, dtype=jnp.int32)[:, None, None]
    ).astype(jnp.float32)
    weighted = (jnp.transpose(amp, (1, 0, 2))[:, None] * row_hit[None]).reshape(
        steps * inline_cells, devices, capacity
    )
    planes = lax.dot_general(
        weighted, col_hit, (((1, 2), (1, 2)), ((), ())), precision=highest
    ).reshape(steps, inline_cells, cross_cells)
    fields = (courant_square, thomsen_epsilon, thomsen_delta, shear_ratio, damping)
    current = jnp.stack([wave_p, wave_q])
    previous = jnp.stack([wave_p_old, wave_q_old])
    coefs = anisotropy(tilt_angle, azimuth)
    for step in range(steps):
        padded = second_round(current, 4, faces) if step == 0 else with_halo(current, 4)
        newer = advance(padded, current, previous, fields, coefs, planes[step], 0)
        previous = current
        current = newer
    return (current[0], current[1], previous[0], previous[1])


def solution(mesh):
    return jax.shard_map(
        local,
        mesh=mesh,
        in_specs=(
            P("gz", "inl", "xl"),
            P("gz", "inl", "xl"),
            P("gz", "inl", "xl"),
            P("gz", "inl", "xl"),
            P("gz", "inl", "xl"),
            P("gz", "inl", "xl"),
            P("gz", "inl", "xl"),
            P("gz", "inl", "xl"),
            P("gz", "inl", "xl"),
            P("gz", "inl", "xl"),
            P("gz", "inl", "xl"),
            P(("inl", "xl", "gz"), None),
            P(),
            P(),
            P(("inl", "xl", "gz")),
            P(("inl", "xl", "gz")),
            P(("inl", "xl", "gz")),
        ),
        out_specs=(
            P("gz", "inl", "xl"),
            P("gz", "inl", "xl"),
            P("gz", "inl", "xl"),
            P("gz", "inl", "xl"),
        ),
        check_vma=False,
    )
```

```python
import jax
import jax.numpy as jnp
from jax import lax
from jax.sharding import PartitionSpec as P

second_coef = (-205.0 / 72.0, 8.0 / 5.0, -1.0 / 5.0, 8.0 / 315.0, -1.0 / 560.0)
first_coef = (0.0, 4.0 / 5.0, -1.0 / 5.0, 4.0 / 105.0, -1.0 / 280.0)


def shift_pair(block, dim, width, axis):
    count = lax.axis_size(axis)
    size = block.shape[dim]
    index = lax.axis_index(axis)
    if count % 2 == 0:
        even = index % 2 == 0
        inner = [(i, i ^ 1) for i in range(count)]
        outer = [(i, i + 1 if i % 2 else i - 1) for i in range(1, count - 1)]
        got_inner = lax.ppermute(
            lax.dynamic_slice_in_dim(block, jnp.where(even, size - width, 0), width, axis=dim),
            axis,
            inner,
        )
        if count == 2:
            empty = jnp.zeros_like(got_inner)
            return jnp.where(even, empty, got_inner), jnp.where(even, got_inner, empty)
        got_outer = lax.ppermute(
            lax.dynamic_slice_in_dim(block, jnp.where(even, 0, size - width), width, axis=dim),
            axis,
            outer,
        )
        return jnp.where(even, got_outer, got_inner), jnp.where(even, got_inner, got_outer)
    forward = [(i, i + 1) for i in range(count - 1)]
    backward = [(target, source) for source, target in forward]
    top = lax.slice_in_dim(block, size - width, None, axis=dim)
    bottom = lax.slice_in_dim(block, 0, width, axis=dim)
    return lax.ppermute(top, axis, forward), lax.ppermute(bottom, axis, backward)


def first_round(block, width):
    low_z, high_z = shift_pair(block, 1, width, "gz")
    low_y, high_y = shift_pair(block, 3, width, "xl")
    return low_z, high_z, low_y, high_y


def second_round(block, width, faces):
    low_z, high_z, low_y, high_y = faces
    strips = jnp.concatenate([low_z, high_z], axis=1)
    low_c, high_c = shift_pair(strips, 3, width, "xl")
    wide_z = jnp.concatenate([low_z, block, high_z], axis=1)
    pad_z = ((0, 0), (width, width), (0, 0), (0, 0))
    bare = jnp.concatenate([jnp.pad(low_y, pad_z), wide_z, jnp.pad(high_y, pad_z)], axis=3)
    low_x, high_x = shift_pair(bare, 2, width, "inl")
    side_low = jnp.concatenate([low_c[:, :width], low_y, low_c[:, width:]], axis=1)
    side_high = jnp.concatenate([high_c[:, :width], high_y, high_c[:, width:]], axis=1)
    full = jnp.concatenate([side_low, wide_z, side_high], axis=3)
    return jnp.concatenate([low_x, full, high_x], axis=2)


def with_halo(block, width):
    return second_round(block, width, first_round(block, width))


def derivatives(padded):
    depth = padded.shape[-3] - 8
    across = padded.shape[-2] - 8
    along = padded.shape[-1] - 8

    def piece(dz, dx, dy):
        return padded[
            ..., 4 + dz : 4 + dz + depth, 4 + dx : 4 + dx + across, 4 + dy : 4 + dy + along
        ]

    center = piece(0, 0, 0)
    u_zz = second_coef[0] * center
    u_xx = second_coef[0] * center
    u_yy = second_coef[0] * center
    for k in range(1, 5):
        u_zz = u_zz + second_coef[k] * (piece(k, 0, 0) + piece(-k, 0, 0))
        u_xx = u_xx + second_coef[k] * (piece(0, k, 0) + piece(0, -k, 0))
        u_yy = u_yy + second_coef[k] * (piece(0, 0, k) + piece(0, 0, -k))
    grad_x = first_coef[1] * (padded[..., :, 5 : 5 + across, :] - padded[..., :, 3 : 3 + across, :])
    grad_y = first_coef[1] * (
        padded[..., :, 4 : 4 + across, 5 : 5 + along]
        - padded[..., :, 4 : 4 + across, 3 : 3 + along]
    )
    for k in range(2, 5):
        grad_x = grad_x + first_coef[k] * (
            padded[..., :, 4 + k : 4 + k + across, :] - padded[..., :, 4 - k : 4 - k + across, :]
        )
        grad_y = grad_y + first_coef[k] * (
            padded[..., :, 4 : 4 + across, 4 + k : 4 + k + along]
            - padded[..., :, 4 : 4 + across, 4 - k : 4 - k + along]
        )
    u_xy = first_coef[1] * (
        grad_x[..., 4 : 4 + depth, :, 5 : 5 + along] - grad_x[..., 4 : 4 + depth, :, 3 : 3 + along]
    )
    u_xz = first_coef[1] * (
        grad_x[..., 5 : 5 + depth, :, 4 : 4 + along] - grad_x[..., 3 : 3 + depth, :, 4 : 4 + along]
    )
    u_yz = first_coef[1] * (grad_y[..., 5 : 5 + depth, :, :] - grad_y[..., 3 : 3 + depth, :, :])
    for k in range(2, 5):
        u_xy = u_xy + first_coef[k] * (
            grad_x[..., 4 : 4 + depth, :, 4 + k : 4 + k + along]
            - grad_x[..., 4 : 4 + depth, :, 4 - k : 4 - k + along]
        )
        u_xz = u_xz + first_coef[k] * (
            grad_x[..., 4 + k : 4 + k + depth, :, 4 : 4 + along]
            - grad_x[..., 4 - k : 4 - k + depth, :, 4 : 4 + along]
        )
        u_yz = u_yz + first_coef[k] * (
            grad_y[..., 4 + k : 4 + k + depth, :, :] - grad_y[..., 4 - k : 4 - k + depth, :, :]
        )
    return (u_zz, u_xx, u_yy, u_xy, u_xz, u_yz)


def anisotropy(tilt_angle, azimuth):
    sin_t = jnp.sin(tilt_angle)
    cos_t = jnp.cos(tilt_angle)
    sin_f = jnp.sin(azimuth)
    cos_f = jnp.cos(azimuth)
    a_xx = sin_t * sin_t * cos_f * cos_f
    a_yy = sin_t * sin_t * sin_f * sin_f
    a_zz = cos_t * cos_t
    a_xy = 2.0 * sin_t * sin_t * sin_f * cos_f
    a_xz = 2.0 * sin_t * cos_t * cos_f
    a_yz = 2.0 * sin_t * cos_t * sin_f
    return (a_xx, a_yy, a_zz, a_xy, a_xz, a_yz)


def advance(padded, current, previous, fields, coefs, plane, top):
    courant, eps_field, delta_field, shear, damp = fields
    a_xx, a_yy, a_zz, a_xy, a_xz, a_yz = coefs
    u_zz, u_xx, u_yy, u_xy, u_xz, u_yz = derivatives(padded)
    h_one = a_xx * u_xx + a_yy * u_yy + a_zz * u_zz + a_xy * u_xy + a_xz * u_xz + a_yz * u_yz
    h_two = u_xx + u_yy + u_zz - h_one
    wave_a = current[0]
    wave_b = current[1]
    old_a = previous[0]
    old_b = previous[1]
    new_a = (
        2.0 * wave_a
        - old_a
        + courant * ((1.0 + 2.0 * eps_field) * h_two[0] + h_one[1] + shear * (h_one[0] - h_one[1]))
        - damp * (wave_a - old_a)
    )
    new_b = (
        2.0 * wave_b
        - old_b
        + courant
        * ((1.0 + 2.0 * delta_field) * h_two[0] + h_one[1] + shear * (h_two[1] - h_two[0]))
        - damp * (wave_b - old_b)
    )
    new_a = new_a.at[top].add(plane)
    new_b = new_b.at[top].add(plane)
    return jnp.stack([new_a, new_b])


def step_amplitudes(samples, resample_filter, line_gain, lines):
    table = jnp.arange(line_gain.shape[0], dtype=jnp.int32)
    gains = jnp.sum(jnp.where(lines[:, None] == table[None, :], line_gain[None, :], 0.0), axis=1)
    return jnp.dot(samples, resample_filter.T, precision=lax.Precision.HIGHEST) * gains[:, None]


def local(
    wave_p,
    wave_p_old,
    wave_q,
    wave_q_old,
    courant_square,
    thomsen_epsilon,
    thomsen_delta,
    tilt_angle,
    azimuth,
    shear_ratio,
    damping,
    trace_samples,
    resample_filter,
    line_gain,
    receiver_inline,
    receiver_crossline,
    shot_line,
):
    depth, inline_cells, cross_cells = wave_p.shape
    cells = inline_cells * cross_cells
    steps = resample_filter.shape[0]
    xl_count = lax.axis_size("xl")
    gz_count = lax.axis_size("gz")
    columns = lax.axis_size("inl") * xl_count
    capacity = 2 * trace_samples.shape[0] // columns
    devices = columns * gz_count
    owner = receiver_inline // inline_cells * xl_count + receiver_crossline // cross_cells
    local_cell = receiver_inline % inline_cells * cross_cells + receiver_crossline % cross_cells
    payload = step_amplitudes(trace_samples, resample_filter, line_gain, shot_line)
    traces = owner.shape[0]
    highest = lax.Precision.HIGHEST
    in_column = (owner[:, None] == jnp.arange(columns, dtype=jnp.int32)[None, :]).astype(jnp.float32)
    order = jnp.arange(traces, dtype=jnp.int32)
    earlier = (order[:, None] > order[None, :]).astype(jnp.float32)
    rank = jnp.sum(jnp.dot(earlier, in_column, precision=highest) * in_column, axis=1)
    lane = jnp.arange(3 * capacity, dtype=jnp.int32)[None, :]
    value = jnp.where(
        lane < capacity,
        payload[:, 0:1],
        jnp.where(lane < 2 * capacity, payload[:, 1:2], local_cell.astype(jnp.float32)[:, None]),
    )
    spread = jnp.where(rank.astype(jnp.int32)[:, None] == lane % capacity, value, 0.0)
    to_device = (
        (owner * gz_count)[:, None] == jnp.arange(devices, dtype=jnp.int32)[None, :]
    ).astype(jnp.float32)
    send = lax.dot_general(to_device, spread, (((0,), (0,)), ((), ())), precision=highest)
    current = jnp.stack([wave_p, wave_q])
    faces = first_round(current, 4)
    send, faces = lax.optimization_barrier((send, faces))
    arrived = lax.all_to_all(send, ("inl", "xl", "gz"), split_axis=0, concat_axis=0, tiled=True)
    amp = arrived[:, : steps * capacity].reshape(devices, steps, capacity)
    cell = (arrived[:, steps * capacity :] + 0.5).astype(jnp.int32)
    row_hit = (
        cell[None, :, :] // cross_cells
        == jnp.arange(inline_cells, dtype=jnp.int32)[:, None, None]
    ).astype(jnp.float32)
    col_hit = (
        cell[None, :, :] % cross_cells == jnp.arange(cross_cells, dtype=jnp.int32)[:, None, None]
    ).astype(jnp.float32)
    weighted = (jnp.transpose(amp, (1, 0, 2))[:, None] * row_hit[None]).reshape(
        steps * inline_cells, devices, capacity
    )
    planes = lax.dot_general(
        weighted, col_hit, (((1, 2), (1, 2)), ((), ())), precision=highest
    ).reshape(steps, inline_cells, cross_cells)
    fields = (courant_square, thomsen_epsilon, thomsen_delta, shear_ratio, damping)
    current = jnp.stack([wave_p, wave_q])
    previous = jnp.stack([wave_p_old, wave_q_old])
    coefs = anisotropy(tilt_angle, azimuth)
    for step in range(steps):
        padded = second_round(current, 4, faces) if step == 0 else with_halo(current, 4)
        newer = advance(padded, current, previous, fields, coefs, planes[step], 0)
        previous = current
        current = newer
    return (current[0], current[1], previous[0], previous[1])


def solution(mesh):
    return jax.shard_map(
        local,
        mesh=mesh,
        in_specs=(
            P("gz", "inl", "xl"),
            P("gz", "inl", "xl"),
            P("gz", "inl", "xl"),
            P("gz", "inl", "xl"),
            P("gz", "inl", "xl"),
            P("gz", "inl", "xl"),
            P("gz", "inl", "xl"),
            P("gz", "inl", "xl"),
            P("gz", "inl", "xl"),
            P("gz", "inl", "xl"),
            P("gz", "inl", "xl"),
            P(("inl", "xl", "gz"), None),
            P(),
            P(),
            P(("inl", "xl", "gz")),
            P(("inl", "xl", "gz")),
            P(("inl", "xl", "gz")),
        ),
        out_specs=(
            P("gz", "inl", "xl"),
            P("gz", "inl", "xl"),
            P("gz", "inl", "xl"),
            P("gz", "inl", "xl"),
        ),
        check_vma=False,
    )
```

```python
import jax
import jax.numpy as jnp
from jax import lax
from jax.sharding import PartitionSpec as P

second_coef = (-205.0 / 72.0, 8.0 / 5.0, -1.0 / 5.0, 8.0 / 315.0, -1.0 / 560.0)
first_coef = (0.0, 4.0 / 5.0, -1.0 / 5.0, 4.0 / 105.0, -1.0 / 280.0)


def shift_pair(block, dim, width, axis):
    count = lax.axis_size(axis)
    size = block.shape[dim]
    index = lax.axis_index(axis)
    if count % 2 == 0:
        even = index % 2 == 0
        inner = [(i, i ^ 1) for i in range(count)]
        outer = [(i, i + 1 if i % 2 else i - 1) for i in range(1, count - 1)]
        got_inner = lax.ppermute(
            lax.dynamic_slice_in_dim(block, jnp.where(even, size - width, 0), width, axis=dim),
            axis,
            inner,
        )
        if count == 2:
            empty = jnp.zeros_like(got_inner)
            return jnp.where(even, empty, got_inner), jnp.where(even, got_inner, empty)
        got_outer = lax.ppermute(
            lax.dynamic_slice_in_dim(block, jnp.where(even, 0, size - width), width, axis=dim),
            axis,
            outer,
        )
        return jnp.where(even, got_outer, got_inner), jnp.where(even, got_inner, got_outer)
    forward = [(i, i + 1) for i in range(count - 1)]
    backward = [(target, source) for source, target in forward]
    top = lax.slice_in_dim(block, size - width, None, axis=dim)
    bottom = lax.slice_in_dim(block, 0, width, axis=dim)
    return lax.ppermute(top, axis, forward), lax.ppermute(bottom, axis, backward)


def first_round(block, width):
    low_z, high_z = shift_pair(block, 1, width, "gz")
    low_y, high_y = shift_pair(block, 3, width, "xl")
    return low_z, high_z, low_y, high_y


def second_round(block, width, faces):
    low_z, high_z, low_y, high_y = faces
    strips = jnp.concatenate([low_z, high_z], axis=1)
    low_c, high_c = shift_pair(strips, 3, width, "xl")
    wide_z = jnp.concatenate([low_z, block, high_z], axis=1)
    pad_z = ((0, 0), (width, width), (0, 0), (0, 0))
    bare = jnp.concatenate([jnp.pad(low_y, pad_z), wide_z, jnp.pad(high_y, pad_z)], axis=3)
    low_x, high_x = shift_pair(bare, 2, width, "inl")
    side_low = jnp.concatenate([low_c[:, :width], low_y, low_c[:, width:]], axis=1)
    side_high = jnp.concatenate([high_c[:, :width], high_y, high_c[:, width:]], axis=1)
    full = jnp.concatenate([side_low, wide_z, side_high], axis=3)
    return jnp.concatenate([low_x, full, high_x], axis=2)


def with_halo(block, width):
    return second_round(block, width, first_round(block, width))


def derivatives(padded):
    depth = padded.shape[-3] - 8
    across = padded.shape[-2] - 8
    along = padded.shape[-1] - 8

    def piece(dz, dx, dy):
        return padded[
            ..., 4 + dz : 4 + dz + depth, 4 + dx : 4 + dx + across, 4 + dy : 4 + dy + along
        ]

    center = piece(0, 0, 0)
    u_zz = second_coef[0] * center
    u_xx = second_coef[0] * center
    u_yy = second_coef[0] * center
    for k in range(1, 5):
        u_zz = u_zz + second_coef[k] * (piece(k, 0, 0) + piece(-k, 0, 0))
        u_xx = u_xx + second_coef[k] * (piece(0, k, 0) + piece(0, -k, 0))
        u_yy = u_yy + second_coef[k] * (piece(0, 0, k) + piece(0, 0, -k))
    grad_x = first_coef[1] * (padded[..., :, 5 : 5 + across, :] - padded[..., :, 3 : 3 + across, :])
    grad_y = first_coef[1] * (
        padded[..., :, 4 : 4 + across, 5 : 5 + along]
        - padded[..., :, 4 : 4 + across, 3 : 3 + along]
    )
    for k in range(2, 5):
        grad_x = grad_x + first_coef[k] * (
            padded[..., :, 4 + k : 4 + k + across, :] - padded[..., :, 4 - k : 4 - k + across, :]
        )
        grad_y = grad_y + first_coef[k] * (
            padded[..., :, 4 : 4 + across, 4 + k : 4 + k + along]
            - padded[..., :, 4 : 4 + across, 4 - k : 4 - k + along]
        )
    u_xy = first_coef[1] * (
        grad_x[..., 4 : 4 + depth, :, 5 : 5 + along] - grad_x[..., 4 : 4 + depth, :, 3 : 3 + along]
    )
    u_xz = first_coef[1] * (
        grad_x[..., 5 : 5 + depth, :, 4 : 4 + along] - grad_x[..., 3 : 3 + depth, :, 4 : 4 + along]
    )
    u_yz = first_coef[1] * (grad_y[..., 5 : 5 + depth, :, :] - grad_y[..., 3 : 3 + depth, :, :])
    for k in range(2, 5):
        u_xy = u_xy + first_coef[k] * (
            grad_x[..., 4 : 4 + depth, :, 4 + k : 4 + k + along]
            - grad_x[..., 4 : 4 + depth, :, 4 - k : 4 - k + along]
        )
        u_xz = u_xz + first_coef[k] * (
            grad_x[..., 4 + k : 4 + k + depth, :, 4 : 4 + along]
            - grad_x[..., 4 - k : 4 - k + depth, :, 4 : 4 + along]
        )
        u_yz = u_yz + first_coef[k] * (
            grad_y[..., 4 + k : 4 + k + depth, :, :] - grad_y[..., 4 - k : 4 - k + depth, :, :]
        )
    return (u_zz, u_xx, u_yy, u_xy, u_xz, u_yz)


def anisotropy(tilt_angle, azimuth):
    sin_t = jnp.sin(tilt_angle)
    cos_t = jnp.cos(tilt_angle)
    sin_f = jnp.sin(azimuth)
    cos_f = jnp.cos(azimuth)
    a_xx = sin_t * sin_t * cos_f * cos_f
    a_yy = sin_t * sin_t * sin_f * sin_f
    a_zz = cos_t * cos_t
    a_xy = 2.0 * sin_t * sin_t * sin_f * cos_f
    a_xz = 2.0 * sin_t * cos_t * cos_f
    a_yz = 2.0 * sin_t * cos_t * sin_f
    return (a_xx, a_yy, a_zz, a_xy, a_xz, a_yz)


def advance(padded, current, previous, fields, coefs, plane, top):
    courant, eps_field, delta_field, shear, damp = fields
    a_xx, a_yy, a_zz, a_xy, a_xz, a_yz = coefs
    u_zz, u_xx, u_yy, u_xy, u_xz, u_yz = derivatives(padded)
    h_one = a_xx * u_xx + a_yy * u_yy + a_zz * u_zz + a_xy * u_xy + a_xz * u_xz + a_yz * u_yz
    h_two = u_xx + u_yy + u_zz - h_one
    wave_a = current[0]
    wave_b = current[1]
    old_a = previous[0]
    old_b = previous[1]
    new_a = (
        2.0 * wave_a
        - old_a
        + courant * ((1.0 + 2.0 * eps_field) * h_two[0] + h_one[1] + shear * (h_one[0] - h_one[1]))
        - damp * (wave_a - old_a)
    )
    new_b = (
        2.0 * wave_b
        - old_b
        + courant
        * ((1.0 + 2.0 * delta_field) * h_two[0] + h_one[1] + shear * (h_two[1] - h_two[0]))
        - damp * (wave_b - old_b)
    )
    new_a = new_a.at[top].add(plane)
    new_b = new_b.at[top].add(plane)
    return jnp.stack([new_a, new_b])


def step_amplitudes(samples, resample_filter, line_gain, lines):
    table = jnp.arange(line_gain.shape[0], dtype=jnp.int32)
    gains = jnp.sum(jnp.where(lines[:, None] == table[None, :], line_gain[None, :], 0.0), axis=1)
    return jnp.dot(samples, resample_filter.T, precision=lax.Precision.HIGHEST) * gains[:, None]


def local(
    wave_p,
    wave_p_old,
    wave_q,
    wave_q_old,
    courant_square,
    thomsen_epsilon,
    thomsen_delta,
    tilt_angle,
    azimuth,
    shear_ratio,
    damping,
    trace_samples,
    resample_filter,
    line_gain,
    receiver_inline,
    receiver_crossline,
    shot_line,
):
    depth, inline_cells, cross_cells = wave_p.shape
    cells = inline_cells * cross_cells
    steps = resample_filter.shape[0]
    xl_count = lax.axis_size("xl")
    gz_count = lax.axis_size("gz")
    columns = lax.axis_size("inl") * xl_count
    capacity = 2 * trace_samples.shape[0] // columns
    devices = columns * gz_count
    owner = receiver_inline // inline_cells * xl_count + receiver_crossline // cross_cells
    local_cell = receiver_inline % inline_cells * cross_cells + receiver_crossline % cross_cells
    payload = step_amplitudes(trace_samples, resample_filter, line_gain, shot_line)
    traces = owner.shape[0]
    highest = lax.Precision.HIGHEST
    in_column = (owner[:, None] == jnp.arange(columns, dtype=jnp.int32)[None, :]).astype(jnp.float32)
    order = jnp.arange(traces, dtype=jnp.int32)
    earlier = (order[:, None] > order[None, :]).astype(jnp.float32)
    rank = jnp.sum(jnp.dot(earlier, in_column, precision=highest) * in_column, axis=1)
    lane = jnp.arange(3 * capacity, dtype=jnp.int32)[None, :]
    value = jnp.where(
        lane < capacity,
        payload[:, 0:1],
        jnp.where(lane < 2 * capacity, payload[:, 1:2], local_cell.astype(jnp.float32)[:, None]),
    )
    spread = jnp.where(rank.astype(jnp.int32)[:, None] == lane % capacity, value, 0.0)
    to_device = (
        (owner * gz_count)[:, None] == jnp.arange(devices, dtype=jnp.int32)[None, :]
    ).astype(jnp.float32)
    send = lax.dot_general(to_device, spread, (((0,), (0,)), ((), ())), precision=highest)
    current, send = lax.optimization_barrier((jnp.stack([wave_p, wave_q]), send))
    faces = first_round(current, 4)
    send, faces = lax.optimization_barrier((send, faces))
    arrived = lax.all_to_all(send, ("inl", "xl", "gz"), split_axis=0, concat_axis=0, tiled=True)
    amp = arrived[:, : steps * capacity].reshape(devices, steps, capacity)
    cell = (arrived[:, steps * capacity :] + 0.5).astype(jnp.int32)
    row_hit = (
        cell[None, :, :] // cross_cells
        == jnp.arange(inline_cells, dtype=jnp.int32)[:, None, None]
    ).astype(jnp.float32)
    col_hit = (
        cell[None, :, :] % cross_cells == jnp.arange(cross_cells, dtype=jnp.int32)[:, None, None]
    ).astype(jnp.float32)
    weighted = (jnp.transpose(amp, (1, 0, 2))[:, None] * row_hit[None]).reshape(
        steps * inline_cells, devices, capacity
    )
    planes = lax.dot_general(
        weighted, col_hit, (((1, 2), (1, 2)), ((), ())), precision=highest
    ).reshape(steps, inline_cells, cross_cells)
    fields = (courant_square, thomsen_epsilon, thomsen_delta, shear_ratio, damping)
    current = jnp.stack([wave_p, wave_q])
    previous = jnp.stack([wave_p_old, wave_q_old])
    coefs = anisotropy(tilt_angle, azimuth)
    for step in range(steps):
        padded = second_round(current, 4, faces) if step == 0 else with_halo(current, 4)
        newer = advance(padded, current, previous, fields, coefs, planes[step], 0)
        previous = current
        current = newer
    return (current[0], current[1], previous[0], previous[1])


def solution(mesh):
    return jax.shard_map(
        local,
        mesh=mesh,
        in_specs=(
            P("gz", "inl", "xl"),
            P("gz", "inl", "xl"),
            P("gz", "inl", "xl"),
            P("gz", "inl", "xl"),
            P("gz", "inl", "xl"),
            P("gz", "inl", "xl"),
            P("gz", "inl", "xl"),
            P("gz", "inl", "xl"),
            P("gz", "inl", "xl"),
            P("gz", "inl", "xl"),
            P("gz", "inl", "xl"),
            P(("inl", "xl", "gz"), None),
            P(),
            P(),
            P(("inl", "xl", "gz")),
            P(("inl", "xl", "gz")),
            P(("inl", "xl", "gz")),
        ),
        out_specs=(
            P("gz", "inl", "xl"),
            P("gz", "inl", "xl"),
            P("gz", "inl", "xl"),
            P("gz", "inl", "xl"),
        ),
        check_vma=False,
    )
```

```python
import jax
import jax.numpy as jnp
from jax import lax
from jax.sharding import PartitionSpec as P

second_coef = (-205.0 / 72.0, 8.0 / 5.0, -1.0 / 5.0, 8.0 / 315.0, -1.0 / 560.0)
first_coef = (0.0, 4.0 / 5.0, -1.0 / 5.0, 4.0 / 105.0, -1.0 / 280.0)


def shift_pair(block, dim, width, axis):
    count = lax.axis_size(axis)
    size = block.shape[dim]
    index = lax.axis_index(axis)
    if count % 2 == 0:
        even = index % 2 == 0
        inner = [(i, i ^ 1) for i in range(count)]
        outer = [(i, i + 1 if i % 2 else i - 1) for i in range(1, count - 1)]
        got_inner = lax.ppermute(
            lax.dynamic_slice_in_dim(block, jnp.where(even, size - width, 0), width, axis=dim),
            axis,
            inner,
        )
        if count == 2:
            empty = jnp.zeros_like(got_inner)
            return jnp.where(even, empty, got_inner), jnp.where(even, got_inner, empty)
        got_outer = lax.ppermute(
            lax.dynamic_slice_in_dim(block, jnp.where(even, 0, size - width), width, axis=dim),
            axis,
            outer,
        )
        return jnp.where(even, got_outer, got_inner), jnp.where(even, got_inner, got_outer)
    forward = [(i, i + 1) for i in range(count - 1)]
    backward = [(target, source) for source, target in forward]
    top = lax.slice_in_dim(block, size - width, None, axis=dim)
    bottom = lax.slice_in_dim(block, 0, width, axis=dim)
    return lax.ppermute(top, axis, forward), lax.ppermute(bottom, axis, backward)


def first_round(block, width):
    low_z, high_z = shift_pair(block, 1, width, "gz")
    low_y, high_y = shift_pair(block, 3, width, "xl")
    return low_z, high_z, low_y, high_y


def second_round(block, width, faces):
    low_z, high_z, low_y, high_y = faces
    strips = jnp.concatenate([low_z, high_z], axis=1)
    low_c, high_c = shift_pair(strips, 3, width, "xl")
    wide_z = jnp.concatenate([low_z, block, high_z], axis=1)
    pad_z = ((0, 0), (width, width), (0, 0), (0, 0))
    bare = jnp.concatenate([jnp.pad(low_y, pad_z), wide_z, jnp.pad(high_y, pad_z)], axis=3)
    low_x, high_x = shift_pair(bare, 2, width, "inl")
    side_low = jnp.concatenate([low_c[:, :width], low_y, low_c[:, width:]], axis=1)
    side_high = jnp.concatenate([high_c[:, :width], high_y, high_c[:, width:]], axis=1)
    full = jnp.concatenate([side_low, wide_z, side_high], axis=3)
    return jnp.concatenate([low_x, full, high_x], axis=2)


def with_halo(block, width):
    return second_round(block, width, first_round(block, width))


def derivatives(padded):
    depth = padded.shape[-3] - 8
    across = padded.shape[-2] - 8
    along = padded.shape[-1] - 8

    def piece(dz, dx, dy):
        return padded[
            ..., 4 + dz : 4 + dz + depth, 4 + dx : 4 + dx + across, 4 + dy : 4 + dy + along
        ]

    center = piece(0, 0, 0)
    u_zz = second_coef[0] * center
    u_xx = second_coef[0] * center
    u_yy = second_coef[0] * center
    for k in range(1, 5):
        u_zz = u_zz + second_coef[k] * (piece(k, 0, 0) + piece(-k, 0, 0))
        u_xx = u_xx + second_coef[k] * (piece(0, k, 0) + piece(0, -k, 0))
        u_yy = u_yy + second_coef[k] * (piece(0, 0, k) + piece(0, 0, -k))
    grad_x = first_coef[1] * (padded[..., :, 5 : 5 + across, :] - padded[..., :, 3 : 3 + across, :])
    grad_y = first_coef[1] * (
        padded[..., :, 4 : 4 + across, 5 : 5 + along]
        - padded[..., :, 4 : 4 + across, 3 : 3 + along]
    )
    for k in range(2, 5):
        grad_x = grad_x + first_coef[k] * (
            padded[..., :, 4 + k : 4 + k + across, :] - padded[..., :, 4 - k : 4 - k + across, :]
        )
        grad_y = grad_y + first_coef[k] * (
            padded[..., :, 4 : 4 + across, 4 + k : 4 + k + along]
            - padded[..., :, 4 : 4 + across, 4 - k : 4 - k + along]
        )
    u_xy = first_coef[1] * (
        grad_x[..., 4 : 4 + depth, :, 5 : 5 + along] - grad_x[..., 4 : 4 + depth, :, 3 : 3 + along]
    )
    u_xz = first_coef[1] * (
        grad_x[..., 5 : 5 + depth, :, 4 : 4 + along] - grad_x[..., 3 : 3 + depth, :, 4 : 4 + along]
    )
    u_yz = first_coef[1] * (grad_y[..., 5 : 5 + depth, :, :] - grad_y[..., 3 : 3 + depth, :, :])
    for k in range(2, 5):
        u_xy = u_xy + first_coef[k] * (
            grad_x[..., 4 : 4 + depth, :, 4 + k : 4 + k + along]
            - grad_x[..., 4 : 4 + depth, :, 4 - k : 4 - k + along]
        )
        u_xz = u_xz + first_coef[k] * (
            grad_x[..., 4 + k : 4 + k + depth, :, 4 : 4 + along]
            - grad_x[..., 4 - k : 4 - k + depth, :, 4 : 4 + along]
        )
        u_yz = u_yz + first_coef[k] * (
            grad_y[..., 4 + k : 4 + k + depth, :, :] - grad_y[..., 4 - k : 4 - k + depth, :, :]
        )
    return (u_zz, u_xx, u_yy, u_xy, u_xz, u_yz)


def anisotropy(tilt_angle, azimuth):
    sin_t = jnp.sin(tilt_angle)
    cos_t = jnp.cos(tilt_angle)
    sin_f = jnp.sin(azimuth)
    cos_f = jnp.cos(azimuth)
    a_xx = sin_t * sin_t * cos_f * cos_f
    a_yy = sin_t * sin_t * sin_f * sin_f
    a_zz = cos_t * cos_t
    a_xy = 2.0 * sin_t * sin_t * sin_f * cos_f
    a_xz = 2.0 * sin_t * cos_t * cos_f
    a_yz = 2.0 * sin_t * cos_t * sin_f
    return (a_xx, a_yy, a_zz, a_xy, a_xz, a_yz)


def advance(padded, current, previous, fields, coefs, plane, top):
    courant, eps_field, delta_field, shear, damp = fields
    a_xx, a_yy, a_zz, a_xy, a_xz, a_yz = coefs
    u_zz, u_xx, u_yy, u_xy, u_xz, u_yz = derivatives(padded)
    h_one = a_xx * u_xx + a_yy * u_yy + a_zz * u_zz + a_xy * u_xy + a_xz * u_xz + a_yz * u_yz
    h_two = u_xx + u_yy + u_zz - h_one
    wave_a = current[0]
    wave_b = current[1]
    old_a = previous[0]
    old_b = previous[1]
    new_a = (
        2.0 * wave_a
        - old_a
        + courant * ((1.0 + 2.0 * eps_field) * h_two[0] + h_one[1] + shear * (h_one[0] - h_one[1]))
        - damp * (wave_a - old_a)
    )
    new_b = (
        2.0 * wave_b
        - old_b
        + courant
        * ((1.0 + 2.0 * delta_field) * h_two[0] + h_one[1] + shear * (h_two[1] - h_two[0]))
        - damp * (wave_b - old_b)
    )
    new_a = new_a.at[top].add(plane)
    new_b = new_b.at[top].add(plane)
    return jnp.stack([new_a, new_b])


def step_amplitudes(samples, resample_filter, line_gain, lines):
    table = jnp.arange(line_gain.shape[0], dtype=jnp.int32)
    gains = jnp.sum(jnp.where(lines[:, None] == table[None, :], line_gain[None, :], 0.0), axis=1)
    return jnp.dot(samples, resample_filter.T, precision=lax.Precision.HIGHEST) * gains[:, None]


def local(
    wave_p,
    wave_p_old,
    wave_q,
    wave_q_old,
    courant_square,
    thomsen_epsilon,
    thomsen_delta,
    tilt_angle,
    azimuth,
    shear_ratio,
    damping,
    trace_samples,
    resample_filter,
    line_gain,
    receiver_inline,
    receiver_crossline,
    shot_line,
):
    depth, inline_cells, cross_cells = wave_p.shape
    cells = inline_cells * cross_cells
    steps = resample_filter.shape[0]
    xl_count = lax.axis_size("xl")
    gz_count = lax.axis_size("gz")
    columns = lax.axis_size("inl") * xl_count
    capacity = 2 * trace_samples.shape[0] // columns
    devices = columns * gz_count
    owner = receiver_inline // inline_cells * xl_count + receiver_crossline // cross_cells
    local_cell = receiver_inline % inline_cells * cross_cells + receiver_crossline % cross_cells
    payload = step_amplitudes(trace_samples, resample_filter, line_gain, shot_line)
    traces = owner.shape[0]
    highest = lax.Precision.HIGHEST
    in_column = (owner[:, None] == jnp.arange(columns, dtype=jnp.int32)[None, :]).astype(jnp.float32)
    order = jnp.arange(traces, dtype=jnp.int32)
    earlier = (order[:, None] > order[None, :]).astype(jnp.float32)
    rank = jnp.sum(jnp.dot(earlier, in_column, precision=highest) * in_column, axis=1)
    lane = jnp.arange(3 * capacity, dtype=jnp.int32)[None, :]
    value = jnp.where(
        lane < capacity,
        payload[:, 0:1],
        jnp.where(lane < 2 * capacity, payload[:, 1:2], local_cell.astype(jnp.float32)[:, None]),
    )
    spread = jnp.where(rank.astype(jnp.int32)[:, None] == lane % capacity, value, 0.0)
    to_device = (
        (owner * gz_count)[:, None] == jnp.arange(devices, dtype=jnp.int32)[None, :]
    ).astype(jnp.float32)
    send = lax.dot_general(to_device, spread, (((0,), (0,)), ((), ())), precision=highest)
    current = jnp.stack([wave_p, wave_q])
    faces = first_round(current, 4)
    send, faces = lax.optimization_barrier((send, faces))
    arrived = lax.all_to_all(send, ("inl", "xl", "gz"), split_axis=0, concat_axis=0, tiled=True)
    def surface_planes(arrived):
        amp = arrived[:, : steps * capacity].reshape(devices, steps, capacity)
        cell = (arrived[:, steps * capacity :] + 0.5).astype(jnp.int32)
        row_hit = (
            cell[None, :, :] // cross_cells
            == jnp.arange(inline_cells, dtype=jnp.int32)[:, None, None]
        ).astype(jnp.float32)
        col_hit = (
            cell[None, :, :] % cross_cells == jnp.arange(cross_cells, dtype=jnp.int32)[:, None, None]
        ).astype(jnp.float32)
        weighted = (jnp.transpose(amp, (1, 0, 2))[:, None] * row_hit[None]).reshape(
            steps * inline_cells, devices, capacity
        )
        planes = lax.dot_general(
            weighted, col_hit, (((1, 2), (1, 2)), ((), ())), precision=highest
        ).reshape(steps, inline_cells, cross_cells)
        return planes

    planes = lax.cond(
        lax.axis_index("gz") == 0,
        surface_planes,
        lambda arrived: jnp.zeros((steps, inline_cells, cross_cells), jnp.float32),
        arrived,
    )
    fields = (courant_square, thomsen_epsilon, thomsen_delta, shear_ratio, damping)
    current = jnp.stack([wave_p, wave_q])
    previous = jnp.stack([wave_p_old, wave_q_old])
    coefs = anisotropy(tilt_angle, azimuth)
    for step in range(steps):
        padded = second_round(current, 4, faces) if step == 0 else with_halo(current, 4)
        newer = advance(padded, current, previous, fields, coefs, planes[step], 0)
        previous = current
        current = newer
    return (current[0], current[1], previous[0], previous[1])


def solution(mesh):
    return jax.shard_map(
        local,
        mesh=mesh,
        in_specs=(
            P("gz", "inl", "xl"),
            P("gz", "inl", "xl"),
            P("gz", "inl", "xl"),
            P("gz", "inl", "xl"),
            P("gz", "inl", "xl"),
            P("gz", "inl", "xl"),
            P("gz", "inl", "xl"),
            P("gz", "inl", "xl"),
            P("gz", "inl", "xl"),
            P("gz", "inl", "xl"),
            P("gz", "inl", "xl"),
            P(("inl", "xl", "gz"), None),
            P(),
            P(),
            P(("inl", "xl", "gz")),
            P(("inl", "xl", "gz")),
            P(("inl", "xl", "gz")),
        ),
        out_specs=(
            P("gz", "inl", "xl"),
            P("gz", "inl", "xl"),
            P("gz", "inl", "xl"),
            P("gz", "inl", "xl"),
        ),
        check_vma=False,
    )
```

```python
import jax
import jax.numpy as jnp
from jax import lax
from jax.sharding import PartitionSpec as P

second_coef = (-205.0 / 72.0, 8.0 / 5.0, -1.0 / 5.0, 8.0 / 315.0, -1.0 / 560.0)
first_coef = (0.0, 4.0 / 5.0, -1.0 / 5.0, 4.0 / 105.0, -1.0 / 280.0)


def shift_pair(block, dim, width, axis):
    count = lax.axis_size(axis)
    size = block.shape[dim]
    index = lax.axis_index(axis)
    if count % 2 == 0:
        even = index % 2 == 0
        inner = [(i, i ^ 1) for i in range(count)]
        outer = [(i, i + 1 if i % 2 else i - 1) for i in range(1, count - 1)]
        got_inner = lax.ppermute(
            lax.dynamic_slice_in_dim(block, jnp.where(even, size - width, 0), width, axis=dim),
            axis,
            inner,
        )
        if count == 2:
            empty = jnp.zeros_like(got_inner)
            return jnp.where(even, empty, got_inner), jnp.where(even, got_inner, empty)
        got_outer = lax.ppermute(
            lax.dynamic_slice_in_dim(block, jnp.where(even, 0, size - width), width, axis=dim),
            axis,
            outer,
        )
        return jnp.where(even, got_outer, got_inner), jnp.where(even, got_inner, got_outer)
    forward = [(i, i + 1) for i in range(count - 1)]
    backward = [(target, source) for source, target in forward]
    top = lax.slice_in_dim(block, size - width, None, axis=dim)
    bottom = lax.slice_in_dim(block, 0, width, axis=dim)
    return lax.ppermute(top, axis, forward), lax.ppermute(bottom, axis, backward)


def first_round(block, width):
    low_z, high_z = shift_pair(block, 1, width, "gz")
    low_y, high_y = shift_pair(block, 3, width, "xl")
    return low_z, high_z, low_y, high_y


def second_round(block, width, faces):
    low_z, high_z, low_y, high_y = faces
    strips = jnp.concatenate([low_z, high_z], axis=1)
    low_c, high_c = shift_pair(strips, 3, width, "xl")
    wide_z = jnp.concatenate([low_z, block, high_z], axis=1)
    pad_z = ((0, 0), (width, width), (0, 0), (0, 0))
    bare = jnp.concatenate([jnp.pad(low_y, pad_z), wide_z, jnp.pad(high_y, pad_z)], axis=3)
    low_x, high_x = shift_pair(bare, 2, width, "inl")
    side_low = jnp.concatenate([low_c[:, :width], low_y, low_c[:, width:]], axis=1)
    side_high = jnp.concatenate([high_c[:, :width], high_y, high_c[:, width:]], axis=1)
    full = jnp.concatenate([side_low, wide_z, side_high], axis=3)
    return jnp.concatenate([low_x, full, high_x], axis=2)


def with_halo(block, width):
    return second_round(block, width, first_round(block, width))


def derivatives(padded):
    depth = padded.shape[-3] - 8
    across = padded.shape[-2] - 8
    along = padded.shape[-1] - 8

    def piece(dz, dx, dy):
        return padded[
            ..., 4 + dz : 4 + dz + depth, 4 + dx : 4 + dx + across, 4 + dy : 4 + dy + along
        ]

    center = piece(0, 0, 0)
    u_zz = second_coef[0] * center
    u_xx = second_coef[0] * center
    u_yy = second_coef[0] * center
    for k in range(1, 5):
        u_zz = u_zz + second_coef[k] * (piece(k, 0, 0) + piece(-k, 0, 0))
        u_xx = u_xx + second_coef[k] * (piece(0, k, 0) + piece(0, -k, 0))
        u_yy = u_yy + second_coef[k] * (piece(0, 0, k) + piece(0, 0, -k))
    grad_x = first_coef[1] * (padded[..., :, 5 : 5 + across, :] - padded[..., :, 3 : 3 + across, :])
    grad_y = first_coef[1] * (
        padded[..., :, 4 : 4 + across, 5 : 5 + along]
        - padded[..., :, 4 : 4 + across, 3 : 3 + along]
    )
    for k in range(2, 5):
        grad_x = grad_x + first_coef[k] * (
            padded[..., :, 4 + k : 4 + k + across, :] - padded[..., :, 4 - k : 4 - k + across, :]
        )
        grad_y = grad_y + first_coef[k] * (
            padded[..., :, 4 : 4 + across, 4 + k : 4 + k + along]
            - padded[..., :, 4 : 4 + across, 4 - k : 4 - k + along]
        )
    u_xy = first_coef[1] * (
        grad_x[..., 4 : 4 + depth, :, 5 : 5 + along] - grad_x[..., 4 : 4 + depth, :, 3 : 3 + along]
    )
    u_xz = first_coef[1] * (
        grad_x[..., 5 : 5 + depth, :, 4 : 4 + along] - grad_x[..., 3 : 3 + depth, :, 4 : 4 + along]
    )
    u_yz = first_coef[1] * (grad_y[..., 5 : 5 + depth, :, :] - grad_y[..., 3 : 3 + depth, :, :])
    for k in range(2, 5):
        u_xy = u_xy + first_coef[k] * (
            grad_x[..., 4 : 4 + depth, :, 4 + k : 4 + k + along]
            - grad_x[..., 4 : 4 + depth, :, 4 - k : 4 - k + along]
        )
        u_xz = u_xz + first_coef[k] * (
            grad_x[..., 4 + k : 4 + k + depth, :, 4 : 4 + along]
            - grad_x[..., 4 - k : 4 - k + depth, :, 4 : 4 + along]
        )
        u_yz = u_yz + first_coef[k] * (
            grad_y[..., 4 + k : 4 + k + depth, :, :] - grad_y[..., 4 - k : 4 - k + depth, :, :]
        )
    return (u_zz, u_xx, u_yy, u_xy, u_xz, u_yz)


def anisotropy(tilt_angle, azimuth):
    sin_t = jnp.sin(tilt_angle)
    cos_t = jnp.cos(tilt_angle)
    sin_f = jnp.sin(azimuth)
    cos_f = jnp.cos(azimuth)
    a_xx = sin_t * sin_t * cos_f * cos_f
    a_yy = sin_t * sin_t * sin_f * sin_f
    a_zz = cos_t * cos_t
    a_xy = 2.0 * sin_t * sin_t * sin_f * cos_f
    a_xz = 2.0 * sin_t * cos_t * cos_f
    a_yz = 2.0 * sin_t * cos_t * sin_f
    return (a_xx, a_yy, a_zz, a_xy, a_xz, a_yz)


def advance(padded, current, previous, fields, coefs, plane, top):
    courant, eps_field, delta_field, shear, damp = fields
    a_xx, a_yy, a_zz, a_xy, a_xz, a_yz = coefs
    u_zz, u_xx, u_yy, u_xy, u_xz, u_yz = derivatives(padded)
    h_one = a_xx * u_xx + a_yy * u_yy + a_zz * u_zz + a_xy * u_xy + a_xz * u_xz + a_yz * u_yz
    h_two = u_xx + u_yy + u_zz - h_one
    wave_a = current[0]
    wave_b = current[1]
    old_a = previous[0]
    old_b = previous[1]
    new_a = (
        2.0 * wave_a
        - old_a
        + courant * ((1.0 + 2.0 * eps_field) * h_two[0] + h_one[1] + shear * (h_one[0] - h_one[1]))
        - damp * (wave_a - old_a)
    )
    new_b = (
        2.0 * wave_b
        - old_b
        + courant
        * ((1.0 + 2.0 * delta_field) * h_two[0] + h_one[1] + shear * (h_two[1] - h_two[0]))
        - damp * (wave_b - old_b)
    )
    new_a = new_a.at[top].add(plane)
    new_b = new_b.at[top].add(plane)
    return jnp.stack([new_a, new_b])


def step_amplitudes(samples, resample_filter, line_gain, lines):
    table = jnp.arange(line_gain.shape[0], dtype=jnp.int32)
    gains = jnp.sum(jnp.where(lines[:, None] == table[None, :], line_gain[None, :], 0.0), axis=1)
    return jnp.dot(samples, resample_filter.T, precision=lax.Precision.HIGHEST) * gains[:, None]


def local(
    wave_p,
    wave_p_old,
    wave_q,
    wave_q_old,
    courant_square,
    thomsen_epsilon,
    thomsen_delta,
    tilt_angle,
    azimuth,
    shear_ratio,
    damping,
    trace_samples,
    resample_filter,
    line_gain,
    receiver_inline,
    receiver_crossline,
    shot_line,
):
    depth, inline_cells, cross_cells = wave_p.shape
    cells = inline_cells * cross_cells
    steps = resample_filter.shape[0]
    xl_count = lax.axis_size("xl")
    gz_count = lax.axis_size("gz")
    columns = lax.axis_size("inl") * xl_count
    capacity = 2 * trace_samples.shape[0] // columns
    devices = columns * gz_count
    owner = receiver_inline // inline_cells * xl_count + receiver_crossline // cross_cells
    local_cell = receiver_inline % inline_cells * cross_cells + receiver_crossline % cross_cells
    payload = step_amplitudes(trace_samples, resample_filter, line_gain, shot_line)
    traces = owner.shape[0]
    highest = lax.Precision.HIGHEST
    in_column = (owner[:, None] == jnp.arange(columns, dtype=jnp.int32)[None, :]).astype(jnp.float32)
    order = jnp.arange(traces, dtype=jnp.int32)
    earlier = (order[:, None] > order[None, :]).astype(jnp.bfloat16)
    before = jnp.dot(earlier, in_column.astype(jnp.bfloat16), preferred_element_type=jnp.float32)
    rank = jnp.sum(before * in_column, axis=1)
    lane = jnp.arange(3 * capacity, dtype=jnp.int32)[None, :]
    value = jnp.where(
        lane < capacity,
        payload[:, 0:1],
        jnp.where(lane < 2 * capacity, payload[:, 1:2], local_cell.astype(jnp.float32)[:, None]),
    )
    spread = jnp.where(rank.astype(jnp.int32)[:, None] == lane % capacity, value, 0.0)
    to_device = (
        (owner * gz_count)[:, None] == jnp.arange(devices, dtype=jnp.int32)[None, :]
    ).astype(jnp.float32)
    send = lax.dot_general(to_device, spread, (((0,), (0,)), ((), ())), precision=highest)
    current = jnp.stack([wave_p, wave_q])
    faces = first_round(current, 4)
    send, faces = lax.optimization_barrier((send, faces))
    arrived = lax.all_to_all(send, ("inl", "xl", "gz"), split_axis=0, concat_axis=0, tiled=True)
    amp = arrived[:, : steps * capacity].reshape(devices, steps, capacity)
    cell = (arrived[:, steps * capacity :] + 0.5).astype(jnp.int32)
    row_hit = (
        cell[None, :, :] // cross_cells
        == jnp.arange(inline_cells, dtype=jnp.int32)[:, None, None]
    ).astype(jnp.float32)
    col_hit = (
        cell[None, :, :] % cross_cells == jnp.arange(cross_cells, dtype=jnp.int32)[:, None, None]
    ).astype(jnp.float32)
    weighted = (jnp.transpose(amp, (1, 0, 2))[:, None] * row_hit[None]).reshape(
        steps * inline_cells, devices, capacity
    )
    planes = lax.dot_general(
        weighted, col_hit, (((1, 2), (1, 2)), ((), ())), precision=highest
    ).reshape(steps, inline_cells, cross_cells)
    fields = (courant_square, thomsen_epsilon, thomsen_delta, shear_ratio, damping)
    current = jnp.stack([wave_p, wave_q])
    previous = jnp.stack([wave_p_old, wave_q_old])
    coefs = anisotropy(tilt_angle, azimuth)
    for step in range(steps):
        padded = second_round(current, 4, faces) if step == 0 else with_halo(current, 4)
        newer = advance(padded, current, previous, fields, coefs, planes[step], 0)
        previous = current
        current = newer
    return (current[0], current[1], previous[0], previous[1])


def solution(mesh):
    return jax.shard_map(
        local,
        mesh=mesh,
        in_specs=(
            P("gz", "inl", "xl"),
            P("gz", "inl", "xl"),
            P("gz", "inl", "xl"),
            P("gz", "inl", "xl"),
            P("gz", "inl", "xl"),
            P("gz", "inl", "xl"),
            P("gz", "inl", "xl"),
            P("gz", "inl", "xl"),
            P("gz", "inl", "xl"),
            P("gz", "inl", "xl"),
            P("gz", "inl", "xl"),
            P(("inl", "xl", "gz"), None),
            P(),
            P(),
            P(("inl", "xl", "gz")),
            P(("inl", "xl", "gz")),
            P(("inl", "xl", "gz")),
        ),
        out_specs=(
            P("gz", "inl", "xl"),
            P("gz", "inl", "xl"),
            P("gz", "inl", "xl"),
            P("gz", "inl", "xl"),
        ),
        check_vma=False,
    )
```

```python
import jax
import numpy as np
import jax.numpy as jnp
from jax import lax
from jax.sharding import PartitionSpec as P

second_coef = (-205.0 / 72.0, 8.0 / 5.0, -1.0 / 5.0, 8.0 / 315.0, -1.0 / 560.0)
first_coef = (0.0, 4.0 / 5.0, -1.0 / 5.0, 4.0 / 105.0, -1.0 / 280.0)


def shift_pair(block, dim, width, axis):
    count = lax.axis_size(axis)
    size = block.shape[dim]
    index = lax.axis_index(axis)
    if count % 2 == 0:
        even = index % 2 == 0
        inner = [(i, i ^ 1) for i in range(count)]
        outer = [(i, i + 1 if i % 2 else i - 1) for i in range(1, count - 1)]
        got_inner = lax.ppermute(
            lax.dynamic_slice_in_dim(block, jnp.where(even, size - width, 0), width, axis=dim),
            axis,
            inner,
        )
        if count == 2:
            empty = jnp.zeros_like(got_inner)
            return jnp.where(even, empty, got_inner), jnp.where(even, got_inner, empty)
        got_outer = lax.ppermute(
            lax.dynamic_slice_in_dim(block, jnp.where(even, 0, size - width), width, axis=dim),
            axis,
            outer,
        )
        return jnp.where(even, got_outer, got_inner), jnp.where(even, got_inner, got_outer)
    forward = [(i, i + 1) for i in range(count - 1)]
    backward = [(target, source) for source, target in forward]
    top = lax.slice_in_dim(block, size - width, None, axis=dim)
    bottom = lax.slice_in_dim(block, 0, width, axis=dim)
    return lax.ppermute(top, axis, forward), lax.ppermute(bottom, axis, backward)


def first_round(block, width):
    low_z, high_z = shift_pair(block, 1, width, "gz")
    low_y, high_y = shift_pair(block, 3, width, "xl")
    return low_z, high_z, low_y, high_y


def second_round(block, width, faces):
    low_z, high_z, low_y, high_y = faces
    strips = jnp.concatenate([low_z, high_z], axis=1)
    low_c, high_c = shift_pair(strips, 3, width, "xl")
    wide_z = jnp.concatenate([low_z, block, high_z], axis=1)
    pad_z = ((0, 0), (width, width), (0, 0), (0, 0))
    bare = jnp.concatenate([jnp.pad(low_y, pad_z), wide_z, jnp.pad(high_y, pad_z)], axis=3)
    low_x, high_x = shift_pair(bare, 2, width, "inl")
    side_low = jnp.concatenate([low_c[:, :width], low_y, low_c[:, width:]], axis=1)
    side_high = jnp.concatenate([high_c[:, :width], high_y, high_c[:, width:]], axis=1)
    full = jnp.concatenate([side_low, wide_z, side_high], axis=3)
    return jnp.concatenate([low_x, full, high_x], axis=2)


def with_halo(block, width):
    return second_round(block, width, first_round(block, width))


def derivatives(padded):
    depth = padded.shape[-3] - 8
    across = padded.shape[-2] - 8
    along = padded.shape[-1] - 8

    def piece(dz, dx, dy):
        return padded[
            ..., 4 + dz : 4 + dz + depth, 4 + dx : 4 + dx + across, 4 + dy : 4 + dy + along
        ]

    center = piece(0, 0, 0)
    u_zz = second_coef[0] * center
    u_xx = second_coef[0] * center
    u_yy = second_coef[0] * center
    for k in range(1, 5):
        u_zz = u_zz + second_coef[k] * (piece(k, 0, 0) + piece(-k, 0, 0))
        u_xx = u_xx + second_coef[k] * (piece(0, k, 0) + piece(0, -k, 0))
        u_yy = u_yy + second_coef[k] * (piece(0, 0, k) + piece(0, 0, -k))
    grad_x = first_coef[1] * (padded[..., :, 5 : 5 + across, :] - padded[..., :, 3 : 3 + across, :])
    grad_y = first_coef[1] * (
        padded[..., :, 4 : 4 + across, 5 : 5 + along]
        - padded[..., :, 4 : 4 + across, 3 : 3 + along]
    )
    for k in range(2, 5):
        grad_x = grad_x + first_coef[k] * (
            padded[..., :, 4 + k : 4 + k + across, :] - padded[..., :, 4 - k : 4 - k + across, :]
        )
        grad_y = grad_y + first_coef[k] * (
            padded[..., :, 4 : 4 + across, 4 + k : 4 + k + along]
            - padded[..., :, 4 : 4 + across, 4 - k : 4 - k + along]
        )
    u_xy = first_coef[1] * (
        grad_x[..., 4 : 4 + depth, :, 5 : 5 + along] - grad_x[..., 4 : 4 + depth, :, 3 : 3 + along]
    )
    u_xz = first_coef[1] * (
        grad_x[..., 5 : 5 + depth, :, 4 : 4 + along] - grad_x[..., 3 : 3 + depth, :, 4 : 4 + along]
    )
    u_yz = first_coef[1] * (grad_y[..., 5 : 5 + depth, :, :] - grad_y[..., 3 : 3 + depth, :, :])
    for k in range(2, 5):
        u_xy = u_xy + first_coef[k] * (
            grad_x[..., 4 : 4 + depth, :, 4 + k : 4 + k + along]
            - grad_x[..., 4 : 4 + depth, :, 4 - k : 4 - k + along]
        )
        u_xz = u_xz + first_coef[k] * (
            grad_x[..., 4 + k : 4 + k + depth, :, 4 : 4 + along]
            - grad_x[..., 4 - k : 4 - k + depth, :, 4 : 4 + along]
        )
        u_yz = u_yz + first_coef[k] * (
            grad_y[..., 4 + k : 4 + k + depth, :, :] - grad_y[..., 4 - k : 4 - k + depth, :, :]
        )
    return (u_zz, u_xx, u_yy, u_xy, u_xz, u_yz)


def anisotropy(tilt_angle, azimuth):
    sin_t = jnp.sin(tilt_angle)
    cos_t = jnp.cos(tilt_angle)
    sin_f = jnp.sin(azimuth)
    cos_f = jnp.cos(azimuth)
    a_xx = sin_t * sin_t * cos_f * cos_f
    a_yy = sin_t * sin_t * sin_f * sin_f
    a_zz = cos_t * cos_t
    a_xy = 2.0 * sin_t * sin_t * sin_f * cos_f
    a_xz = 2.0 * sin_t * cos_t * cos_f
    a_yz = 2.0 * sin_t * cos_t * sin_f
    return (a_xx, a_yy, a_zz, a_xy, a_xz, a_yz)


def advance(padded, current, previous, fields, coefs, plane, top):
    courant, eps_field, delta_field, shear, damp = fields
    a_xx, a_yy, a_zz, a_xy, a_xz, a_yz = coefs
    u_zz, u_xx, u_yy, u_xy, u_xz, u_yz = derivatives(padded)
    h_one = a_xx * u_xx + a_yy * u_yy + a_zz * u_zz + a_xy * u_xy + a_xz * u_xz + a_yz * u_yz
    h_two = u_xx + u_yy + u_zz - h_one
    wave_a = current[0]
    wave_b = current[1]
    old_a = previous[0]
    old_b = previous[1]
    new_a = (
        2.0 * wave_a
        - old_a
        + courant * ((1.0 + 2.0 * eps_field) * h_two[0] + h_one[1] + shear * (h_one[0] - h_one[1]))
        - damp * (wave_a - old_a)
    )
    new_b = (
        2.0 * wave_b
        - old_b
        + courant
        * ((1.0 + 2.0 * delta_field) * h_two[0] + h_one[1] + shear * (h_two[1] - h_two[0]))
        - damp * (wave_b - old_b)
    )
    new_a = new_a.at[top].add(plane)
    new_b = new_b.at[top].add(plane)
    return jnp.stack([new_a, new_b])


def step_amplitudes(samples, resample_filter, line_gain, lines):
    table = jnp.arange(line_gain.shape[0], dtype=jnp.int32)
    gains = jnp.sum(jnp.where(lines[:, None] == table[None, :], line_gain[None, :], 0.0), axis=1)
    return jnp.dot(samples, resample_filter.T, precision=lax.Precision.HIGHEST) * gains[:, None]


def local(
    wave_p,
    wave_p_old,
    wave_q,
    wave_q_old,
    courant_square,
    thomsen_epsilon,
    thomsen_delta,
    tilt_angle,
    azimuth,
    shear_ratio,
    damping,
    trace_samples,
    resample_filter,
    line_gain,
    receiver_inline,
    receiver_crossline,
    shot_line,
):
    depth, inline_cells, cross_cells = wave_p.shape
    cells = inline_cells * cross_cells
    steps = resample_filter.shape[0]
    xl_count = lax.axis_size("xl")
    gz_count = lax.axis_size("gz")
    columns = lax.axis_size("inl") * xl_count
    capacity = 2 * trace_samples.shape[0] // columns
    devices = columns * gz_count
    owner = receiver_inline // inline_cells * xl_count + receiver_crossline // cross_cells
    local_cell = receiver_inline % inline_cells * cross_cells + receiver_crossline % cross_cells
    payload = step_amplitudes(trace_samples, resample_filter, line_gain, shot_line)
    traces = owner.shape[0]
    highest = lax.Precision.HIGHEST
    in_column = (owner[:, None] == jnp.arange(columns, dtype=jnp.int32)[None, :]).astype(jnp.float32)
    earlier = jnp.asarray(np.tri(traces, traces, -1), dtype=jnp.bfloat16)
    before = jnp.dot(earlier, in_column.astype(jnp.bfloat16), preferred_element_type=jnp.float32)
    rank = jnp.sum(before * in_column, axis=1)
    lane = jnp.arange(3 * capacity, dtype=jnp.int32)[None, :]
    value = jnp.where(
        lane < capacity,
        payload[:, 0:1],
        jnp.where(lane < 2 * capacity, payload[:, 1:2], local_cell.astype(jnp.float32)[:, None]),
    )
    spread = jnp.where(rank.astype(jnp.int32)[:, None] == lane % capacity, value, 0.0)
    to_device = (
        (owner * gz_count)[:, None] == jnp.arange(devices, dtype=jnp.int32)[None, :]
    ).astype(jnp.float32)
    send = lax.dot_general(to_device, spread, (((0,), (0,)), ((), ())), precision=highest)
    current = jnp.stack([wave_p, wave_q])
    faces = first_round(current, 4)
    send, faces = lax.optimization_barrier((send, faces))
    arrived = lax.all_to_all(send, ("inl", "xl", "gz"), split_axis=0, concat_axis=0, tiled=True)
    amp = arrived[:, : steps * capacity].reshape(devices, steps, capacity)
    cell = (arrived[:, steps * capacity :] + 0.5).astype(jnp.int32)
    row_hit = (
        cell[None, :, :] // cross_cells
        == jnp.arange(inline_cells, dtype=jnp.int32)[:, None, None]
    ).astype(jnp.float32)
    col_hit = (
        cell[None, :, :] % cross_cells == jnp.arange(cross_cells, dtype=jnp.int32)[:, None, None]
    ).astype(jnp.float32)
    weighted = (jnp.transpose(amp, (1, 0, 2))[:, None] * row_hit[None]).reshape(
        steps * inline_cells, devices, capacity
    )
    planes = lax.dot_general(
        weighted, col_hit, (((1, 2), (1, 2)), ((), ())), precision=highest
    ).reshape(steps, inline_cells, cross_cells)
    fields = (courant_square, thomsen_epsilon, thomsen_delta, shear_ratio, damping)
    current = jnp.stack([wave_p, wave_q])
    previous = jnp.stack([wave_p_old, wave_q_old])
    coefs = anisotropy(tilt_angle, azimuth)
    for step in range(steps):
        padded = second_round(current, 4, faces) if step == 0 else with_halo(current, 4)
        newer = advance(padded, current, previous, fields, coefs, planes[step], 0)
        previous = current
        current = newer
    return (current[0], current[1], previous[0], previous[1])


def solution(mesh):
    return jax.shard_map(
        local,
        mesh=mesh,
        in_specs=(
            P("gz", "inl", "xl"),
            P("gz", "inl", "xl"),
            P("gz", "inl", "xl"),
            P("gz", "inl", "xl"),
            P("gz", "inl", "xl"),
            P("gz", "inl", "xl"),
            P("gz", "inl", "xl"),
            P("gz", "inl", "xl"),
            P("gz", "inl", "xl"),
            P("gz", "inl", "xl"),
            P("gz", "inl", "xl"),
            P(("inl", "xl", "gz"), None),
            P(),
            P(),
            P(("inl", "xl", "gz")),
            P(("inl", "xl", "gz")),
            P(("inl", "xl", "gz")),
        ),
        out_specs=(
            P("gz", "inl", "xl"),
            P("gz", "inl", "xl"),
            P("gz", "inl", "xl"),
            P("gz", "inl", "xl"),
        ),
        check_vma=False,
    )
```
